32 devices in a mesh: dp: 8 (over y, x, core), fsdp: 4 (over z).
Axes of the slice: x: 2, y: 2, z: 4, core: 2. Of those that a mesh axis runs over, the one named last changes fastest.
Arguments:
- query_cache: bfloat16 [384, 1024], P('dp', 'fsdp'), may hold values from -8 to 8
- region_cache: bfloat16 [384, 1024], P('dp', 'fsdp'), may hold values from -8 to 8
- positive: int32 [384], P('dp'), may hold values from 0 to 383, each once
- hidden_states: bfloat16 [4096, 4096], P(('dp', 'fsdp')), may hold values from -12 to 12
- segment_ids: int32 [8, 512], P('dp', 'fsdp'), may hold values from 0 to 47, never falling along the last dimension, each value on 1 to 21 neighbouring positions
- norm_gain: bfloat16 [4096], replicated, may hold values from 0.099609375 to 1.8984375
- proj_weight: bfloat16 [4096, 1024], P('fsdp'), may hold values from -1 to 1
Outputs:
- mean_loss: float32 [], replicated
- query_grad: float32 [384, 1024], P('dp', 'fsdp')
- region_grad: float32 [384, 1024], P('dp', 'fsdp')
- hidden_grad: bfloat16 [4096, 4096], P(('dp', 'fsdp'))
- gain_grad: float32 [4096], replicated
- proj_grad: float32 [4096, 1024], P('dp', 'fsdp')
The draws below stay inside these ranges and needn't reach their ends.
Inputs may be any that keep to these rules, and one draw needn't show every extreme that they name: Each region is the positive of exactly one instruction. `segment_ids`: within a pair group the ids never fall, every instruction has at least one token, and one has exactly 21.
All inputs are finite; a program needn't handle non-finite values.
Results may differ from the reference program's by a relative error of at most 0.0088.
Values may be sent and summed in bfloat16 or wider, within the bound.
No kernel may reach another device: no remote copies, remote signals or barrier semaphores. Data moves between devices by JAX's collectives and lax.ppermute only.
A program may use at most 64 MiB of HBM per device.

```python
import math
import jax
import jax.numpy as jnp
import numpy as np
from jax import lax

D = 4096
E = 1024
ROWS = 48
PAIRS = 384
GROUP = 512
MOST = 21
N_DP = 8


def common_signs(key):
    model_bits = jax.random.bernoulli(jax.random.fold_in(key, 31), 0.5, (D,))
    embed_bits = jax.random.bernoulli(jax.random.fold_in(key, 37), 0.5, (E,))
    model_signs = jnp.where(model_bits, 1.0, -1.0).astype(jnp.float32)
    embed_signs = jnp.where(embed_bits, 1.0, -1.0).astype(jnp.float32)
    return (model_signs, embed_signs)


def draw_query_cache(key, part):
    values = 1.73 * jnp.clip(jax.random.normal(jax.random.fold_in(key, 11), (PAIRS, E), jnp.float32), -4.6, 4.6)
    return values.astype(jnp.bfloat16)


def draw_region_cache(key, part):
    values = 1.73 * jnp.clip(jax.random.normal(jax.random.fold_in(key, 21), (PAIRS, E), jnp.float32), -4.6, 4.6)
    return values.astype(jnp.bfloat16)


def draw_hidden_states(key, part):
    model_signs, embed_signs = common_signs(key)
    token_total = N_DP * GROUP
    background = jnp.clip(jax.random.normal(jax.random.fold_in(key, 43), (token_total, D), jnp.float32), -5.0, 5.0)
    values = background + model_signs[None, :]
    return values.astype(jnp.bfloat16)


def draw_proj_weight(key, part):
    model_signs, embed_signs = common_signs(key)
    fan_scale = float(D) ** (-0.5)
    background = jnp.clip(jax.random.normal(jax.random.fold_in(key, 53), (D, E), jnp.float32), -4.5, 4.5)
    values = fan_scale * (background + model_signs[:, None] * embed_signs[None, :])
    return values.astype(jnp.bfloat16)


def profile(number_of, total, most, slope):
    portions = [(1 << 20) // math.isqrt(rank ** slope) + 1 for rank in range(2, number_of + 1)]
    surplus, given = total - most - (number_of - 1), [1] * (number_of - 1)
    while surplus > 0:
        free = [i for i in range(number_of - 1) if given[i] < most]
        mass, remaining = sum([portions[i] for i in free]), surplus
        for i in free:
            more = min(most - given[i], max(1, remaining * portions[i] // mass), surplus)
            given[i] = given[i] + more
            surplus = surplus - more
    return np.array([most] + given)


def uneven_parts(rng, count, total, reach, skew):
    if count == 2:
        one = jax.random.randint(rng, (), max(1, total - reach), min(reach, total - 1) + 1)
        return jnp.stack([one, total - one])
    lengths = jnp.asarray(profile(count, total, reach, skew), jnp.int32)
    twos = (count - 1) // 2
    source_of, receiver = lengths[1:1 + 2 * twos:2], lengths[2:2 + 2 * twos:2]
    slack = jnp.minimum(source_of - 1, reach - receiver)
    shifted = jax.random.randint(jax.random.fold_in(rng, 1), (twos,), 0, 1 << 20) % (slack + 1)
    lengths = lengths.at[1:1 + 2 * twos:2].set(source_of - shifted).at[2:2 + 2 * twos:2].set(receiver + shifted)
    return lengths[jax.random.permutation(jax.random.fold_in(rng, 2), count)]


def setup_inputs(seed: int = 0) -> dict:
    splits = jax.random.split(jax.random.key(seed), 8)
    query_cache = draw_query_cache(jax.random.fold_in(splits[7], 71), 0)
    region_cache = draw_region_cache(jax.random.fold_in(splits[7], 71), 0)
    positive = jax.random.permutation(splits[2], PAIRS).astype(jnp.int32)
    hidden_states = draw_hidden_states(jax.random.fold_in(splits[7], 71), 0)
    segment_ids = jax.vmap(lambda own: jnp.searchsorted(jnp.cumsum(uneven_parts(own, ROWS, GROUP, MOST, 1)), jnp.arange(GROUP), side="right"))(jax.random.split(splits[4], N_DP)).reshape((N_DP, GROUP)).astype(jnp.int32)
    norm_gain = jnp.clip(1.0 + 0.18 * jax.random.normal(splits[5], (D,), jnp.float32), 0.099609375, 1.8984375).astype(jnp.bfloat16)
    proj_weight = draw_proj_weight(jax.random.fold_in(splits[7], 71), 0)
    return {"query_cache": query_cache, "region_cache": region_cache, "positive": positive, "hidden_states": hidden_states, "segment_ids": segment_ids, "norm_gain": norm_gain, "proj_weight": proj_weight}


EPS = 1e-05

def reference(query_cache, region_cache, positive, hidden_states, segment_ids, norm_gain, proj_weight):
    logit_scale = float(E) ** (-0.5)
    columns = jnp.arange(PAIRS, dtype=jnp.int32)
    query_blocks = query_cache.reshape(N_DP, ROWS, E)
    target_blocks = positive.reshape(N_DP, ROWS)

    def loss_block(carry, inputs):
        region_sum, loss_sum = carry
        query_block, target_block = inputs
        scores = jnp.dot(query_block, region_cache.T, preferred_element_type=jnp.float32) * logit_scale
        row_max = lax.optimization_barrier(jnp.max(scores, axis=1, keepdims=True))
        log_total = row_max[:, 0] + jnp.log(lax.optimization_barrier(jnp.sum(jnp.exp(scores - row_max), axis=1)))
        matched = columns[None, :] == target_block[:, None]
        target_score = lax.optimization_barrier(jnp.sum(jnp.where(matched, scores, jnp.zeros_like(scores)), axis=1))
        grad_probs = (jnp.exp(scores - log_total[:, None]) - matched.astype(jnp.float32)).astype(jnp.bfloat16)
        query_grad = logit_scale * jnp.dot(grad_probs, region_cache, preferred_element_type=jnp.float32)
        region_sum = region_sum + jnp.dot(grad_probs.T, query_block, preferred_element_type=jnp.float32)
        loss_sum = loss_sum + jnp.sum(log_total - target_score)
        return ((region_sum, loss_sum), query_grad)
    start_loss = (jnp.zeros((PAIRS, E), jnp.float32), jnp.zeros((), jnp.float32))
    (region_sum, loss_sum), query_parts = lax.scan(loss_block, start_loss, (query_blocks, target_blocks))
    query_grad = query_parts.reshape(PAIRS, E)
    region_grad = logit_scale * region_sum
    mean_loss = loss_sum / PAIRS
    gain = norm_gain.astype(jnp.float32)
    labels = jnp.arange(ROWS, dtype=jnp.int32)

    def layer_block(carry, inputs):
        weight_sum, gain_sum = carry
        block_states, block_ids, block_grad = inputs
        states = block_states.astype(jnp.float32)
        inv_rms = lax.rsqrt(lax.optimization_barrier(jnp.mean(states * states, axis=1, keepdims=True)) + EPS)
        normed = (states * inv_rms * gain).astype(jnp.bfloat16)
        member = block_ids[None, :] == labels[:, None]
        pooled = jnp.dot(member.astype(jnp.bfloat16), normed, preferred_element_type=jnp.float32)
        counts = lax.optimization_barrier(jnp.sum(member.astype(jnp.float32), axis=1))
        mean_pooled = (pooled / counts[:, None]).astype(jnp.bfloat16)
        grad_low = block_grad.astype(jnp.bfloat16)
        mean_grad = jnp.dot(grad_low, proj_weight.T, preferred_element_type=jnp.float32)
        pool_grad = mean_grad / counts[:, None]
        normed_grad = pool_grad[block_ids]
        gain_sum = gain_sum + lax.optimization_barrier(jnp.sum(normed_grad * states * inv_rms, axis=0))
        scaled = gain * normed_grad
        inner = lax.optimization_barrier(jnp.mean(scaled * states, axis=1, keepdims=True))
        state_grad = (inv_rms * scaled - states * inv_rms ** 3 * inner).astype(jnp.bfloat16)
        weight_sum = weight_sum + jnp.dot(mean_pooled.T, grad_low, preferred_element_type=jnp.float32)
        return ((weight_sum, gain_sum), state_grad)
    start_layer = (jnp.zeros((D, E), jnp.float32), jnp.zeros((D,), jnp.float32))
    layer_inputs = (hidden_states.reshape(N_DP, GROUP, D), segment_ids, query_parts)
    (weight_sum, gain_sum), state_parts = lax.scan(layer_block, start_layer, layer_inputs)
    hidden_grad = state_parts.reshape(N_DP * GROUP, D)
    return (mean_loss, query_grad, region_grad, hidden_grad, gain_sum, weight_sum)
```

```python
import jax
import jax.numpy as jnp
from jax import lax
from jax.sharding import PartitionSpec as P

E = 1024


EPS = 1e-05


def local_sharded(query_cache, region_cache, positive, hidden_states, segment_ids, norm_gain, proj_weight):
    row_count = query_cache.shape[0]
    data_count = lax.axis_size("dp")
    pair_count = row_count * data_count
    logit_scale = float(E) ** (-0.5)
    contract_last = (((1,), (1,)), ((), ()))
    contract_first = (((0,), (0,)), ((), ()))
    region_all, query_all = (
        lax.all_gather(region_cache, "dp", axis=0, tiled=True),
        lax.all_gather(query_cache, "dp", axis=0, tiled=True),
    )
    partial_value = lax.dot_general(
        query_cache, region_all, contract_last, preferred_element_type=jnp.float32
    )
    scores = lax.psum(partial_value, "fsdp") * logit_scale
    row_max = jnp.max(scores, axis=1, keepdims=True)
    log_total = row_max[:, 0] + jnp.log(jnp.sum(jnp.exp(scores - row_max), axis=1))
    columns = lax.broadcasted_iota(jnp.int32, (1, pair_count), 1)
    matched = columns == positive[:, None]
    target_score = jnp.sum(jnp.where(matched, scores, jnp.zeros_like(scores)), axis=1)
    loss_local = jnp.sum(log_total - target_score)
    grad_probs = (jnp.exp(scores - log_total[:, None]) - matched.astype(jnp.float32)).astype(
        jnp.bfloat16
    )
    query_grad = logit_scale * jnp.dot(grad_probs, region_all, preferred_element_type=jnp.float32)
    totals_all, targets_all = (
        lax.all_gather(log_total, "dp", axis=0, tiled=True),
        lax.all_gather(positive.astype(jnp.float32), "dp", axis=0, tiled=True),
    )
    partial_t = lax.dot_general(
        region_cache, query_all, contract_last, preferred_element_type=jnp.float32
    )
    scores_t = lax.psum(partial_t, "fsdp") * logit_scale
    own_rows = (
        lax.axis_index("dp") * row_count + lax.broadcasted_iota(jnp.int32, (row_count, 1), 0)
    ).astype(jnp.float32)
    matched_t = targets_all[None, :] == own_rows
    probs_t = (jnp.exp(scores_t - totals_all[None, :]) - matched_t.astype(jnp.float32)).astype(
        jnp.bfloat16
    )
    region_grad = logit_scale * jnp.dot(probs_t, query_all, preferred_element_type=jnp.float32)
    gain = norm_gain.astype(jnp.float32)
    states = hidden_states.astype(jnp.float32)
    inv_rms = lax.rsqrt(jnp.mean(states * states, axis=1, keepdims=True) + EPS)
    normed = (states * inv_rms * gain).astype(jnp.bfloat16)
    labels = lax.broadcasted_iota(jnp.int32, (row_count, 1), 0)
    member = segment_ids[0][None, :] == labels
    pooled_part = jnp.dot(member.astype(jnp.bfloat16), normed, preferred_element_type=jnp.float32)
    counts_part = jnp.sum(member.astype(jnp.float32), axis=1)
    pooled, counts = lax.psum((pooled_part, counts_part), "fsdp")
    mean_pooled = (pooled / counts[:, None]).astype(jnp.bfloat16)
    grad_low = query_grad.astype(jnp.bfloat16)
    grad_full = lax.all_gather(grad_low, "fsdp", axis=1, tiled=True)
    mean_part = lax.dot_general(
        grad_full, proj_weight, contract_last, preferred_element_type=jnp.float32
    )
    mean_grad = lax.all_gather(mean_part, "fsdp", axis=1, tiled=True)
    pool_grad = mean_grad / counts[:, None]
    normed_grad = lax.dot_general(
        member.astype(jnp.float32),
        pool_grad,
        contract_first,
        precision=lax.Precision.HIGHEST,
        preferred_element_type=jnp.float32,
    )
    gain_part = jnp.sum(normed_grad * states * inv_rms, axis=0)
    scaled = gain * normed_grad
    inner = jnp.mean(scaled * states, axis=1, keepdims=True)
    hidden_grad = (inv_rms * scaled - states * inv_rms**3 * inner).astype(jnp.bfloat16)
    proj_grad = lax.psum_scatter(
        lax.dot_general(mean_pooled, grad_low, contract_first, preferred_element_type=jnp.float32),
        "dp",
        scatter_dimension=0,
        tiled=True,
    )
    loss_total = lax.psum(loss_local, "dp")
    gain_grad = lax.psum(gain_part, ("dp", "fsdp"))
    mean_loss = loss_total / pair_count
    return (mean_loss, query_grad, region_grad, hidden_grad, gain_grad, proj_grad)


def local_small(query_cache, region_cache, positive, hidden_states, segment_ids, norm_gain, proj_weight):
    rows, width = query_cache.shape
    data_count = lax.axis_size("dp")
    feature_count = lax.axis_size("fsdp")
    pair_count = rows * data_count
    tokens = segment_ids.shape[1]
    model_width = hidden_states.shape[1]
    logit_scale = float(E) ** (-0.5)
    contract_last = (((1,), (1,)), ((), ()))
    contract_first = (((0,), (0,)), ((), ()))
    me_dp = lax.axis_index("dp")
    me_f = lax.axis_index("fsdp")

    extra = jnp.concatenate(
        [positive // 64, positive % 64, segment_ids[0]]
    ).astype(jnp.float32)
    extra_rows = -(-extra.shape[0] // width)
    extra = jnp.pad(extra, (0, extra_rows * width - extra.shape[0]))
    packed = jnp.concatenate(
        [query_cache, region_cache, extra.reshape(extra_rows, width).astype(jnp.bfloat16)], axis=0
    )
    gathered = lax.all_gather(packed, ("dp", "fsdp"), axis=0, tiled=False)
    gathered = gathered.reshape(data_count, feature_count, 2 * rows + extra_rows, width)
    query_all = gathered[:, :, :rows].transpose(0, 2, 1, 3).reshape(pair_count, feature_count * width)
    region_all = gathered[:, :, rows : 2 * rows].transpose(0, 2, 1, 3).reshape(
        pair_count, feature_count * width
    )
    side = gathered[:, :, 2 * rows :].reshape(data_count, feature_count, extra_rows * width)
    side = side.astype(jnp.float32)
    positive_all = (side[:, 0, :rows] * 64 + side[:, 0, rows : 2 * rows]).astype(jnp.int32)
    positive_all = positive_all.reshape(pair_count)
    group_ids = side[:, :, 2 * rows : 2 * rows + tokens].reshape(data_count, feature_count * tokens)
    group_ids = lax.dynamic_index_in_dim(group_ids, me_dp, axis=0, keepdims=False).astype(jnp.int32)

    scores = (
        lax.dot_general(query_all, region_all, contract_last, preferred_element_type=jnp.float32)
        * logit_scale
    )
    row_max = jnp.max(scores, axis=1, keepdims=True)
    log_total = row_max[:, 0] + jnp.log(jnp.sum(jnp.exp(scores - row_max), axis=1))
    columns = lax.broadcasted_iota(jnp.int32, (1, pair_count), 1)
    matched = columns == positive_all[:, None]
    target_score = jnp.sum(jnp.where(matched, scores, jnp.zeros_like(scores)), axis=1)
    mean_loss = jnp.sum(log_total - target_score) / pair_count
    grad_probs = (jnp.exp(scores - log_total[:, None]) - matched.astype(jnp.float32)).astype(
        jnp.bfloat16
    )
    query_grad_all = logit_scale * jnp.dot(grad_probs, region_all, preferred_element_type=jnp.float32)
    query_grad = lax.dynamic_slice(query_grad_all, (me_dp * rows, me_f * width), (rows, width))
    grad_low = lax.dynamic_slice(query_grad_all, (me_dp * rows, 0), (rows, feature_count * width))
    grad_low = grad_low.astype(jnp.bfloat16)
    grad_low_cols = lax.dynamic_slice(query_grad_all, (0, me_f * width), (pair_count, width))
    grad_low_cols = grad_low_cols.astype(jnp.bfloat16)
    probs_cols = lax.dynamic_slice(grad_probs, (0, me_dp * rows), (pair_count, rows))
    query_cols = lax.dynamic_slice(query_all, (0, me_f * width), (pair_count, width))
    region_grad = logit_scale * lax.dot_general(
        probs_cols, query_cols, contract_first, preferred_element_type=jnp.float32
    )

    gain = norm_gain.astype(jnp.float32)
    states = hidden_states.astype(jnp.float32)
    inv_rms = lax.rsqrt(jnp.mean(states * states, axis=1, keepdims=True) + EPS)
    normed = (states * inv_rms * gain).astype(jnp.bfloat16)
    labels = lax.broadcasted_iota(jnp.int32, (rows, 1), 0)
    member = segment_ids[0][None, :] == labels
    pooled_part = jnp.dot(member.astype(jnp.bfloat16), normed, preferred_element_type=jnp.float32)
    counts = jnp.sum((group_ids[None, :] == labels).astype(jnp.float32), axis=1)
    pooled = lax.psum(pooled_part, "fsdp")
    mean_pooled = (pooled / counts[:, None]).astype(jnp.bfloat16)

    slice_width = model_width // data_count
    pieces = mean_pooled.reshape(rows, data_count, slice_width).transpose(1, 0, 2)
    pieces = lax.all_to_all(pieces, "dp", 0, 0, tiled=True)
    pooled_cols = pieces.reshape(pair_count, slice_width)
    proj_grad = lax.dot_general(
        pooled_cols, grad_low_cols, contract_first, preferred_element_type=jnp.float32
    )

    mean_part = lax.dot_general(
        grad_low, proj_weight, contract_last, preferred_element_type=jnp.float32
    )
    mean_grad = lax.all_gather(mean_part, "fsdp", axis=1, tiled=True)
    pool_grad = mean_grad / counts[:, None]
    normed_grad = lax.dot_general(
        member.astype(jnp.float32),
        pool_grad,
        contract_first,
        precision=lax.Precision.HIGHEST,
        preferred_element_type=jnp.float32,
    )
    gain_part = jnp.sum(normed_grad * states * inv_rms, axis=0)
    scaled = gain * normed_grad
    inner = jnp.mean(scaled * states, axis=1, keepdims=True)
    hidden_grad = (inv_rms * scaled - states * inv_rms**3 * inner).astype(jnp.bfloat16)
    gain_grad = lax.psum(gain_part, ("dp", "fsdp"))
    return (mean_loss, query_grad, region_grad, hidden_grad, gain_grad, proj_grad)


SMALL_PAIRS = 1024


def local(query_cache, region_cache, positive, hidden_states, segment_ids, norm_gain, proj_weight):
    pair_count = query_cache.shape[0] * lax.axis_size("dp")
    args = (query_cache, region_cache, positive, hidden_states, segment_ids, norm_gain, proj_weight)
    if pair_count <= SMALL_PAIRS:
        return local_small(*args)
    return local_sharded(*args)


def solution(mesh):
    in_specs = (
        P("dp", "fsdp"),
        P("dp", "fsdp"),
        P("dp"),
        P(("dp", "fsdp"), None),
        P("dp", "fsdp"),
        P(),
        P("fsdp", None),
    )
    out_specs = (
        P(),
        P("dp", "fsdp"),
        P("dp", "fsdp"),
        P(("dp", "fsdp"), None),
        P(),
        P("dp", "fsdp"),
    )
    return jax.shard_map(local, mesh=mesh, in_specs=in_specs, out_specs=out_specs, check_vma=False)
```

```python
import jax
import jax.numpy as jnp
from jax import lax
from jax.sharding import PartitionSpec as P

E = 1024


EPS = 1e-05


def local_sharded(query_cache, region_cache, positive, hidden_states, segment_ids, norm_gain, proj_weight):
    row_count = query_cache.shape[0]
    data_count = lax.axis_size("dp")
    pair_count = row_count * data_count
    logit_scale = float(E) ** (-0.5)
    contract_last = (((1,), (1,)), ((), ()))
    contract_first = (((0,), (0,)), ((), ()))
    region_all, query_all = (
        lax.all_gather(region_cache, "dp", axis=0, tiled=True),
        lax.all_gather(query_cache, "dp", axis=0, tiled=True),
    )
    partial_value = lax.dot_general(
        query_cache, region_all, contract_last, preferred_element_type=jnp.float32
    )
    scores = lax.psum(partial_value, "fsdp") * logit_scale
    row_max = jnp.max(scores, axis=1, keepdims=True)
    log_total = row_max[:, 0] + jnp.log(jnp.sum(jnp.exp(scores - row_max), axis=1))
    columns = lax.broadcasted_iota(jnp.int32, (1, pair_count), 1)
    matched = columns == positive[:, None]
    target_score = jnp.sum(jnp.where(matched, scores, jnp.zeros_like(scores)), axis=1)
    loss_local = jnp.sum(log_total - target_score)
    grad_probs = (jnp.exp(scores - log_total[:, None]) - matched.astype(jnp.float32)).astype(
        jnp.bfloat16
    )
    query_grad = logit_scale * jnp.dot(grad_probs, region_all, preferred_element_type=jnp.float32)
    totals_all, targets_all = (
        lax.all_gather(log_total, "dp", axis=0, tiled=True),
        lax.all_gather(positive.astype(jnp.float32), "dp", axis=0, tiled=True),
    )
    partial_t = lax.dot_general(
        region_cache, query_all, contract_last, preferred_element_type=jnp.float32
    )
    scores_t = lax.psum(partial_t, "fsdp") * logit_scale
    own_rows = (
        lax.axis_index("dp") * row_count + lax.broadcasted_iota(jnp.int32, (row_count, 1), 0)
    ).astype(jnp.float32)
    matched_t = targets_all[None, :] == own_rows
    probs_t = (jnp.exp(scores_t - totals_all[None, :]) - matched_t.astype(jnp.float32)).astype(
        jnp.bfloat16
    )
    region_grad = logit_scale * jnp.dot(probs_t, query_all, preferred_element_type=jnp.float32)
    gain = norm_gain.astype(jnp.float32)
    states = hidden_states.astype(jnp.float32)
    inv_rms = lax.rsqrt(jnp.mean(states * states, axis=1, keepdims=True) + EPS)
    normed = (states * inv_rms * gain).astype(jnp.bfloat16)
    labels = lax.broadcasted_iota(jnp.int32, (row_count, 1), 0)
    member = segment_ids[0][None, :] == labels
    pooled_part = jnp.dot(member.astype(jnp.bfloat16), normed, preferred_element_type=jnp.float32)
    counts_part = jnp.sum(member.astype(jnp.float32), axis=1)
    pooled, counts = lax.psum((pooled_part, counts_part), "fsdp")
    mean_pooled = (pooled / counts[:, None]).astype(jnp.bfloat16)
    grad_low = query_grad.astype(jnp.bfloat16)
    grad_full = lax.all_gather(grad_low, "fsdp", axis=1, tiled=True)
    mean_part = lax.dot_general(
        grad_full, proj_weight, contract_last, preferred_element_type=jnp.float32
    )
    mean_grad = lax.all_gather(mean_part, "fsdp", axis=1, tiled=True)
    pool_grad = mean_grad / counts[:, None]
    normed_grad = lax.dot_general(
        member.astype(jnp.float32),
        pool_grad,
        contract_first,
        precision=lax.Precision.HIGHEST,
        preferred_element_type=jnp.float32,
    )
    gain_part = jnp.sum(normed_grad * states * inv_rms, axis=0)
    scaled = gain * normed_grad
    inner = jnp.mean(scaled * states, axis=1, keepdims=True)
    hidden_grad = (inv_rms * scaled - states * inv_rms**3 * inner).astype(jnp.bfloat16)
    proj_grad = lax.psum_scatter(
        lax.dot_general(mean_pooled, grad_low, contract_first, preferred_element_type=jnp.float32),
        "dp",
        scatter_dimension=0,
        tiled=True,
    )
    loss_total = lax.psum(loss_local, "dp")
    gain_grad = lax.psum(gain_part, ("dp", "fsdp"))
    mean_loss = loss_total / pair_count
    return (mean_loss, query_grad, region_grad, hidden_grad, gain_grad, proj_grad)


def gather_blocks(x, axis):
    n = lax.axis_size(axis)
    copies = [x] + [
        lax.ppermute(x, axis, [(i, (i + s) % n) for i in range(n)]) for s in range(1, n)
    ]
    stack = jnp.stack(copies)
    order = (lax.axis_index(axis) - jnp.arange(n)) % n
    return jnp.take(stack, order, axis=0)


def sum_blocks(x, axis):
    return jnp.sum(gather_blocks(x, axis), axis=0)


def local_small(query_cache, region_cache, positive, hidden_states, segment_ids, norm_gain, proj_weight):
    rows, width = query_cache.shape
    data_count = lax.axis_size("dp")
    feature_count = lax.axis_size("fsdp")
    pair_count = rows * data_count
    tokens = segment_ids.shape[1]
    model_width = hidden_states.shape[1]
    logit_scale = float(E) ** (-0.5)
    contract_last = (((1,), (1,)), ((), ()))
    contract_first = (((0,), (0,)), ((), ()))
    me_dp = lax.axis_index("dp")
    me_f = lax.axis_index("fsdp")

    extra = jnp.concatenate(
        [positive // 64, positive % 64, segment_ids[0]]
    ).astype(jnp.float32)
    extra_rows = -(-extra.shape[0] // width)
    extra = jnp.pad(extra, (0, extra_rows * width - extra.shape[0]))
    packed = jnp.concatenate(
        [query_cache, region_cache, extra.reshape(extra_rows, width).astype(jnp.bfloat16)], axis=0
    )
    gathered = gather_blocks(gather_blocks(packed, "fsdp"), "dp")
    gathered = gathered.reshape(data_count, feature_count, 2 * rows + extra_rows, width)
    query_all = gathered[:, :, :rows].transpose(0, 2, 1, 3).reshape(pair_count, feature_count * width)
    region_all = gathered[:, :, rows : 2 * rows].transpose(0, 2, 1, 3).reshape(
        pair_count, feature_count * width
    )
    side = gathered[:, :, 2 * rows :].reshape(data_count, feature_count, extra_rows * width)
    side = side.astype(jnp.float32)
    positive_all = (side[:, 0, :rows] * 64 + side[:, 0, rows : 2 * rows]).astype(jnp.int32)
    positive_all = positive_all.reshape(pair_count)
    group_ids = side[:, :, 2 * rows : 2 * rows + tokens].reshape(data_count, feature_count * tokens)
    group_ids = lax.dynamic_index_in_dim(group_ids, me_dp, axis=0, keepdims=False).astype(jnp.int32)

    scores = (
        lax.dot_general(query_all, region_all, contract_last, preferred_element_type=jnp.float32)
        * logit_scale
    )
    row_max = jnp.max(scores, axis=1, keepdims=True)
    log_total = row_max[:, 0] + jnp.log(jnp.sum(jnp.exp(scores - row_max), axis=1))
    columns = lax.broadcasted_iota(jnp.int32, (1, pair_count), 1)
    matched = columns == positive_all[:, None]
    target_score = jnp.sum(jnp.where(matched, scores, jnp.zeros_like(scores)), axis=1)
    mean_loss = jnp.sum(log_total - target_score) / pair_count
    grad_probs = (jnp.exp(scores - log_total[:, None]) - matched.astype(jnp.float32)).astype(
        jnp.bfloat16
    )
    query_grad_all = logit_scale * jnp.dot(grad_probs, region_all, preferred_element_type=jnp.float32)
    query_grad = lax.dynamic_slice(query_grad_all, (me_dp * rows, me_f * width), (rows, width))
    grad_low = lax.dynamic_slice(query_grad_all, (me_dp * rows, 0), (rows, feature_count * width))
    grad_low = grad_low.astype(jnp.bfloat16)
    grad_low_cols = lax.dynamic_slice(query_grad_all, (0, me_f * width), (pair_count, width))
    grad_low_cols = grad_low_cols.astype(jnp.bfloat16)
    probs_cols = lax.dynamic_slice(grad_probs, (0, me_dp * rows), (pair_count, rows))
    query_cols = lax.dynamic_slice(query_all, (0, me_f * width), (pair_count, width))
    region_grad = logit_scale * lax.dot_general(
        probs_cols, query_cols, contract_first, preferred_element_type=jnp.float32
    )

    gain = norm_gain.astype(jnp.float32)
    states = hidden_states.astype(jnp.float32)
    inv_rms = lax.rsqrt(jnp.mean(states * states, axis=1, keepdims=True) + EPS)
    normed = (states * inv_rms * gain).astype(jnp.bfloat16)
    labels = lax.broadcasted_iota(jnp.int32, (rows, 1), 0)
    member = segment_ids[0][None, :] == labels
    pooled_part = jnp.dot(member.astype(jnp.bfloat16), normed, preferred_element_type=jnp.float32)
    counts = jnp.sum((group_ids[None, :] == labels).astype(jnp.float32), axis=1)
    pooled = sum_blocks(pooled_part, "fsdp")
    mean_pooled = (pooled / counts[:, None]).astype(jnp.bfloat16)

    slice_width = model_width // data_count
    pieces = mean_pooled.reshape(rows, data_count, slice_width).transpose(1, 0, 2)
    pieces = lax.all_to_all(pieces, "dp", 0, 0, tiled=True)
    pooled_cols = pieces.reshape(pair_count, slice_width)
    proj_grad = lax.dot_general(
        pooled_cols, grad_low_cols, contract_first, preferred_element_type=jnp.float32
    )

    mean_part = lax.dot_general(
        grad_low, proj_weight, contract_last, preferred_element_type=jnp.float32
    )
    mean_grad = lax.all_gather(mean_part, "fsdp", axis=1, tiled=True)
    pool_grad = mean_grad / counts[:, None]
    normed_grad = lax.dot_general(
        member.astype(jnp.float32),
        pool_grad,
        contract_first,
        precision=lax.Precision.HIGHEST,
        preferred_element_type=jnp.float32,
    )
    gain_part = jnp.sum(normed_grad * states * inv_rms, axis=0)
    scaled = gain * normed_grad
    inner = jnp.mean(scaled * states, axis=1, keepdims=True)
    hidden_grad = (inv_rms * scaled - states * inv_rms**3 * inner).astype(jnp.bfloat16)
    gain_grad = sum_blocks(sum_blocks(gain_part, "dp"), "fsdp")
    return (mean_loss, query_grad, region_grad, hidden_grad, gain_grad, proj_grad)


SMALL_PAIRS = 1024


def local(query_cache, region_cache, positive, hidden_states, segment_ids, norm_gain, proj_weight):
    pair_count = query_cache.shape[0] * lax.axis_size("dp")
    args = (query_cache, region_cache, positive, hidden_states, segment_ids, norm_gain, proj_weight)
    if pair_count <= SMALL_PAIRS:
        return local_small(*args)
    return local_sharded(*args)


def solution(mesh):
    in_specs = (
        P("dp", "fsdp"),
        P("dp", "fsdp"),
        P("dp"),
        P(("dp", "fsdp"), None),
        P("dp", "fsdp"),
        P(),
        P("fsdp", None),
    )
    out_specs = (
        P(),
        P("dp", "fsdp"),
        P("dp", "fsdp"),
        P(("dp", "fsdp"), None),
        P(),
        P("dp", "fsdp"),
    )
    return jax.shard_map(local, mesh=mesh, in_specs=in_specs, out_specs=out_specs, check_vma=False)
```

```python
import jax
import jax.numpy as jnp
from jax import lax
from jax.sharding import PartitionSpec as P

E = 1024


EPS = 1e-05


def local_sharded(query_cache, region_cache, positive, hidden_states, segment_ids, norm_gain, proj_weight):
    row_count = query_cache.shape[0]
    data_count = lax.axis_size("dp")
    pair_count = row_count * data_count
    logit_scale = float(E) ** (-0.5)
    contract_last = (((1,), (1,)), ((), ()))
    contract_first = (((0,), (0,)), ((), ()))
    region_all, query_all = (
        lax.all_gather(region_cache, "dp", axis=0, tiled=True),
        lax.all_gather(query_cache, "dp", axis=0, tiled=True),
    )
    partial_value = lax.dot_general(
        query_cache, region_all, contract_last, preferred_element_type=jnp.float32
    )
    scores = lax.psum(partial_value, "fsdp") * logit_scale
    row_max = jnp.max(scores, axis=1, keepdims=True)
    log_total = row_max[:, 0] + jnp.log(jnp.sum(jnp.exp(scores - row_max), axis=1))
    columns = lax.broadcasted_iota(jnp.int32, (1, pair_count), 1)
    matched = columns == positive[:, None]
    target_score = jnp.sum(jnp.where(matched, scores, jnp.zeros_like(scores)), axis=1)
    loss_local = jnp.sum(log_total - target_score)
    grad_probs = (jnp.exp(scores - log_total[:, None]) - matched.astype(jnp.float32)).astype(
        jnp.bfloat16
    )
    query_grad = logit_scale * jnp.dot(grad_probs, region_all, preferred_element_type=jnp.float32)
    totals_all, targets_all = (
        lax.all_gather(log_total, "dp", axis=0, tiled=True),
        lax.all_gather(positive.astype(jnp.float32), "dp", axis=0, tiled=True),
    )
    partial_t = lax.dot_general(
        region_cache, query_all, contract_last, preferred_element_type=jnp.float32
    )
    scores_t = lax.psum(partial_t, "fsdp") * logit_scale
    own_rows = (
        lax.axis_index("dp") * row_count + lax.broadcasted_iota(jnp.int32, (row_count, 1), 0)
    ).astype(jnp.float32)
    matched_t = targets_all[None, :] == own_rows
    probs_t = (jnp.exp(scores_t - totals_all[None, :]) - matched_t.astype(jnp.float32)).astype(
        jnp.bfloat16
    )
    region_grad = logit_scale * jnp.dot(probs_t, query_all, preferred_element_type=jnp.float32)
    gain = norm_gain.astype(jnp.float32)
    states = hidden_states.astype(jnp.float32)
    inv_rms = lax.rsqrt(jnp.mean(states * states, axis=1, keepdims=True) + EPS)
    normed = (states * inv_rms * gain).astype(jnp.bfloat16)
    labels = lax.broadcasted_iota(jnp.int32, (row_count, 1), 0)
    member = segment_ids[0][None, :] == labels
    pooled_part = jnp.dot(member.astype(jnp.bfloat16), normed, preferred_element_type=jnp.float32)
    counts_part = jnp.sum(member.astype(jnp.float32), axis=1)
    pooled, counts = lax.psum((pooled_part, counts_part), "fsdp")
    mean_pooled = (pooled / counts[:, None]).astype(jnp.bfloat16)
    grad_low = query_grad.astype(jnp.bfloat16)
    grad_full = lax.all_gather(grad_low, "fsdp", axis=1, tiled=True)
    mean_part = lax.dot_general(
        grad_full, proj_weight, contract_last, preferred_element_type=jnp.float32
    )
    mean_grad = lax.all_gather(mean_part, "fsdp", axis=1, tiled=True)
    pool_grad = mean_grad / counts[:, None]
    normed_grad = lax.dot_general(
        member.astype(jnp.float32),
        pool_grad,
        contract_first,
        precision=lax.Precision.HIGHEST,
        preferred_element_type=jnp.float32,
    )
    gain_part = jnp.sum(normed_grad * states * inv_rms, axis=0)
    scaled = gain * normed_grad
    inner = jnp.mean(scaled * states, axis=1, keepdims=True)
    hidden_grad = (inv_rms * scaled - states * inv_rms**3 * inner).astype(jnp.bfloat16)
    proj_grad = lax.psum_scatter(
        lax.dot_general(mean_pooled, grad_low, contract_first, preferred_element_type=jnp.float32),
        "dp",
        scatter_dimension=0,
        tiled=True,
    )
    loss_total = lax.psum(loss_local, "dp")
    gain_grad = lax.psum(gain_part, ("dp", "fsdp"))
    mean_loss = loss_total / pair_count
    return (mean_loss, query_grad, region_grad, hidden_grad, gain_grad, proj_grad)


def gather_blocks(x, axis):
    n = lax.axis_size(axis)
    copies = [x] + [
        lax.ppermute(x, axis, [(i, (i + s) % n) for i in range(n)]) for s in range(1, n)
    ]
    stack = jnp.stack(copies)
    order = (lax.axis_index(axis) - jnp.arange(n)) % n
    return jnp.take(stack, order, axis=0)


def sum_blocks(x, axis):
    return jnp.sum(gather_blocks(x, axis), axis=0)


def scatter_sum(chunks, axis):
    n = lax.axis_size(axis)
    me = lax.axis_index(axis)
    copies = [lax.dynamic_index_in_dim(chunks, me, axis=0, keepdims=False)]
    for s in range(1, n):
        piece = lax.dynamic_index_in_dim(chunks, (me + s) % n, axis=0, keepdims=False)
        copies.append(lax.ppermute(piece, axis, [(i, (i + s) % n) for i in range(n)]))
    order = (me - jnp.arange(n)) % n
    return jnp.sum(jnp.take(jnp.stack(copies), order, axis=0), axis=0)


def local_small(query_cache, region_cache, positive, hidden_states, segment_ids, norm_gain, proj_weight):
    rows, width = query_cache.shape
    data_count = lax.axis_size("dp")
    feature_count = lax.axis_size("fsdp")
    pair_count = rows * data_count
    tokens = segment_ids.shape[1]
    model_width = hidden_states.shape[1]
    logit_scale = float(E) ** (-0.5)
    contract_last = (((1,), (1,)), ((), ()))
    contract_first = (((0,), (0,)), ((), ()))
    me_dp = lax.axis_index("dp")
    me_f = lax.axis_index("fsdp")

    extra = jnp.concatenate(
        [positive // 64, positive % 64, segment_ids[0]]
    ).astype(jnp.float32)
    extra_rows = -(-extra.shape[0] // width)
    extra = jnp.pad(extra, (0, extra_rows * width - extra.shape[0]))
    packed = jnp.concatenate(
        [query_cache, region_cache, extra.reshape(extra_rows, width).astype(jnp.bfloat16)], axis=0
    )
    group_blocks = gather_blocks(packed, "fsdp")
    group_side = group_blocks[:, 2 * rows :].reshape(feature_count, extra_rows * width)
    group_ids = group_side[:, 2 * rows : 2 * rows + tokens].reshape(feature_count * tokens)
    group_ids = group_ids.astype(jnp.int32)

    gain = norm_gain.astype(jnp.float32)
    states = hidden_states.astype(jnp.float32)
    inv_rms = lax.rsqrt(jnp.mean(states * states, axis=1, keepdims=True) + EPS)
    normed = (states * inv_rms * gain).astype(jnp.bfloat16)
    labels = lax.broadcasted_iota(jnp.int32, (rows, 1), 0)
    member = segment_ids[0][None, :] == labels
    pooled_part = jnp.dot(member.astype(jnp.bfloat16), normed, preferred_element_type=jnp.float32)
    counts = jnp.sum((group_ids[None, :] == labels).astype(jnp.float32), axis=1)
    chunk = model_width // feature_count
    pooled_chunk = scatter_sum(
        pooled_part.reshape(rows, feature_count, chunk).transpose(1, 0, 2), "fsdp"
    )
    mean_chunk = (pooled_chunk / counts[:, None]).astype(jnp.bfloat16)
    mean_pooled = gather_blocks(mean_chunk, "fsdp").transpose(1, 0, 2).reshape(rows, model_width)

    gathered = gather_blocks(group_blocks, "dp")
    mean_pooled, gathered = lax.optimization_barrier((mean_pooled, gathered))
    slice_width = model_width // data_count
    pieces = mean_pooled.reshape(rows, data_count, slice_width).transpose(1, 0, 2)
    pieces = lax.all_to_all(pieces, "dp", 0, 0, tiled=True)
    pooled_cols = pieces.reshape(pair_count, slice_width)

    query_all = gathered[:, :, :rows].transpose(0, 2, 1, 3).reshape(pair_count, feature_count * width)
    region_all = gathered[:, :, rows : 2 * rows].transpose(0, 2, 1, 3).reshape(
        pair_count, feature_count * width
    )
    side = gathered[:, :, 2 * rows :].reshape(data_count, feature_count, extra_rows * width)
    side = side.astype(jnp.float32)
    positive_all = (side[:, 0, :rows] * 64 + side[:, 0, rows : 2 * rows]).astype(jnp.int32)
    positive_all = positive_all.reshape(pair_count)

    scores = (
        lax.dot_general(query_all, region_all, contract_last, preferred_element_type=jnp.float32)
        * logit_scale
    )
    row_max = jnp.max(scores, axis=1, keepdims=True)
    log_total = row_max[:, 0] + jnp.log(jnp.sum(jnp.exp(scores - row_max), axis=1))
    columns = lax.broadcasted_iota(jnp.int32, (1, pair_count), 1)
    matched = columns == positive_all[:, None]
    target_score = jnp.sum(jnp.where(matched, scores, jnp.zeros_like(scores)), axis=1)
    mean_loss = jnp.sum(log_total - target_score) / pair_count
    grad_probs = (jnp.exp(scores - log_total[:, None]) - matched.astype(jnp.float32)).astype(
        jnp.bfloat16
    )
    query_grad_all = logit_scale * jnp.dot(grad_probs, region_all, preferred_element_type=jnp.float32)
    query_grad = lax.dynamic_slice(query_grad_all, (me_dp * rows, me_f * width), (rows, width))
    grad_low = lax.dynamic_slice(query_grad_all, (me_dp * rows, 0), (rows, feature_count * width))
    grad_low = grad_low.astype(jnp.bfloat16)
    grad_low_cols = lax.dynamic_slice(query_grad_all, (0, me_f * width), (pair_count, width))
    grad_low_cols = grad_low_cols.astype(jnp.bfloat16)
    probs_cols = lax.dynamic_slice(grad_probs, (0, me_dp * rows), (pair_count, rows))
    query_cols = lax.dynamic_slice(query_all, (0, me_f * width), (pair_count, width))
    region_grad = logit_scale * lax.dot_general(
        probs_cols, query_cols, contract_first, preferred_element_type=jnp.float32
    )

    mean_part = lax.dot_general(
        grad_low, proj_weight, contract_last, preferred_element_type=jnp.float32
    )
    mean_part, pooled_cols = lax.optimization_barrier((mean_part, pooled_cols))
    proj_grad = lax.dot_general(
        pooled_cols, grad_low_cols, contract_first, preferred_element_type=jnp.float32
    )
    mean_grad = lax.all_gather(mean_part, "fsdp", axis=1, tiled=True)
    pool_grad = mean_grad / counts[:, None]
    normed_grad = lax.dot_general(
        member.astype(jnp.float32),
        pool_grad,
        contract_first,
        precision=lax.Precision.HIGHEST,
        preferred_element_type=jnp.float32,
    )
    gain_part = jnp.sum(normed_grad * states * inv_rms, axis=0)
    scaled = gain * normed_grad
    inner = jnp.mean(scaled * states, axis=1, keepdims=True)
    hidden_grad = (inv_rms * scaled - states * inv_rms**3 * inner).astype(jnp.bfloat16)
    gain_grad = sum_blocks(sum_blocks(gain_part, "dp"), "fsdp")
    return (mean_loss, query_grad, region_grad, hidden_grad, gain_grad, proj_grad)


SMALL_PAIRS = 1024


def local(query_cache, region_cache, positive, hidden_states, segment_ids, norm_gain, proj_weight):
    pair_count = query_cache.shape[0] * lax.axis_size("dp")
    args = (query_cache, region_cache, positive, hidden_states, segment_ids, norm_gain, proj_weight)
    if pair_count <= SMALL_PAIRS:
        return local_small(*args)
    return local_sharded(*args)


def solution(mesh):
    in_specs = (
        P("dp", "fsdp"),
        P("dp", "fsdp"),
        P("dp"),
        P(("dp", "fsdp"), None),
        P("dp", "fsdp"),
        P(),
        P("fsdp", None),
    )
    out_specs = (
        P(),
        P("dp", "fsdp"),
        P("dp", "fsdp"),
        P(("dp", "fsdp"), None),
        P(),
        P("dp", "fsdp"),
    )
    return jax.shard_map(local, mesh=mesh, in_specs=in_specs, out_specs=out_specs, check_vma=False)
```

```python
import jax
import jax.numpy as jnp
from jax import lax
from jax.sharding import PartitionSpec as P

E = 1024


EPS = 1e-05


def local_sharded(query_cache, region_cache, positive, hidden_states, segment_ids, norm_gain, proj_weight):
    row_count = query_cache.shape[0]
    data_count = lax.axis_size("dp")
    pair_count = row_count * data_count
    logit_scale = float(E) ** (-0.5)
    contract_last = (((1,), (1,)), ((), ()))
    contract_first = (((0,), (0,)), ((), ()))
    region_all, query_all = (
        lax.all_gather(region_cache, "dp", axis=0, tiled=True),
        lax.all_gather(query_cache, "dp", axis=0, tiled=True),
    )
    partial_value = lax.dot_general(
        query_cache, region_all, contract_last, preferred_element_type=jnp.float32
    )
    scores = lax.psum(partial_value, "fsdp") * logit_scale
    row_max = jnp.max(scores, axis=1, keepdims=True)
    log_total = row_max[:, 0] + jnp.log(jnp.sum(jnp.exp(scores - row_max), axis=1))
    columns = lax.broadcasted_iota(jnp.int32, (1, pair_count), 1)
    matched = columns == positive[:, None]
    target_score = jnp.sum(jnp.where(matched, scores, jnp.zeros_like(scores)), axis=1)
    loss_local = jnp.sum(log_total - target_score)
    grad_probs = (jnp.exp(scores - log_total[:, None]) - matched.astype(jnp.float32)).astype(
        jnp.bfloat16
    )
    query_grad = logit_scale * jnp.dot(grad_probs, region_all, preferred_element_type=jnp.float32)
    totals_all, targets_all = (
        lax.all_gather(log_total, "dp", axis=0, tiled=True),
        lax.all_gather(positive.astype(jnp.float32), "dp", axis=0, tiled=True),
    )
    partial_t = lax.dot_general(
        region_cache, query_all, contract_last, preferred_element_type=jnp.float32
    )
    scores_t = lax.psum(partial_t, "fsdp") * logit_scale
    own_rows = (
        lax.axis_index("dp") * row_count + lax.broadcasted_iota(jnp.int32, (row_count, 1), 0)
    ).astype(jnp.float32)
    matched_t = targets_all[None, :] == own_rows
    probs_t = (jnp.exp(scores_t - totals_all[None, :]) - matched_t.astype(jnp.float32)).astype(
        jnp.bfloat16
    )
    region_grad = logit_scale * jnp.dot(probs_t, query_all, preferred_element_type=jnp.float32)
    gain = norm_gain.astype(jnp.float32)
    states = hidden_states.astype(jnp.float32)
    inv_rms = lax.rsqrt(jnp.mean(states * states, axis=1, keepdims=True) + EPS)
    normed = (states * inv_rms * gain).astype(jnp.bfloat16)
    labels = lax.broadcasted_iota(jnp.int32, (row_count, 1), 0)
    member = segment_ids[0][None, :] == labels
    pooled_part = jnp.dot(member.astype(jnp.bfloat16), normed, preferred_element_type=jnp.float32)
    counts_part = jnp.sum(member.astype(jnp.float32), axis=1)
    pooled, counts = lax.psum((pooled_part, counts_part), "fsdp")
    mean_pooled = (pooled / counts[:, None]).astype(jnp.bfloat16)
    grad_low = query_grad.astype(jnp.bfloat16)
    grad_full = lax.all_gather(grad_low, "fsdp", axis=1, tiled=True)
    mean_part = lax.dot_general(
        grad_full, proj_weight, contract_last, preferred_element_type=jnp.float32
    )
    mean_grad = lax.all_gather(mean_part, "fsdp", axis=1, tiled=True)
    pool_grad = mean_grad / counts[:, None]
    normed_grad = lax.dot_general(
        member.astype(jnp.float32),
        pool_grad,
        contract_first,
        precision=lax.Precision.HIGHEST,
        preferred_element_type=jnp.float32,
    )
    gain_part = jnp.sum(normed_grad * states * inv_rms, axis=0)
    scaled = gain * normed_grad
    inner = jnp.mean(scaled * states, axis=1, keepdims=True)
    hidden_grad = (inv_rms * scaled - states * inv_rms**3 * inner).astype(jnp.bfloat16)
    proj_grad = lax.psum_scatter(
        lax.dot_general(mean_pooled, grad_low, contract_first, preferred_element_type=jnp.float32),
        "dp",
        scatter_dimension=0,
        tiled=True,
    )
    loss_total = lax.psum(loss_local, "dp")
    gain_grad = lax.psum(gain_part, ("dp", "fsdp"))
    mean_loss = loss_total / pair_count
    return (mean_loss, query_grad, region_grad, hidden_grad, gain_grad, proj_grad)


def gather_blocks(x, axis):
    n = lax.axis_size(axis)
    copies = [x] + [
        lax.ppermute(x, axis, [(i, (i + s) % n) for i in range(n)]) for s in range(1, n)
    ]
    stack = jnp.stack(copies)
    order = (lax.axis_index(axis) - jnp.arange(n)) % n
    return jnp.take(stack, order, axis=0)


def sum_blocks(x, axis):
    return jnp.sum(gather_blocks(x, axis), axis=0)


def scatter_sum(chunks, axis):
    n = lax.axis_size(axis)
    me = lax.axis_index(axis)
    copies = [lax.dynamic_index_in_dim(chunks, me, axis=0, keepdims=False)]
    for s in range(1, n):
        piece = lax.dynamic_index_in_dim(chunks, (me + s) % n, axis=0, keepdims=False)
        copies.append(lax.ppermute(piece, axis, [(i, (i + s) % n) for i in range(n)]))
    order = (me - jnp.arange(n)) % n
    return jnp.sum(jnp.take(jnp.stack(copies), order, axis=0), axis=0)


def local_small(query_cache, region_cache, positive, hidden_states, segment_ids, norm_gain, proj_weight):
    rows, width = query_cache.shape
    data_count = lax.axis_size("dp")
    feature_count = lax.axis_size("fsdp")
    pair_count = rows * data_count
    tokens = segment_ids.shape[1]
    model_width = hidden_states.shape[1]
    logit_scale = float(E) ** (-0.5)
    contract_last = (((1,), (1,)), ((), ()))
    contract_first = (((0,), (0,)), ((), ()))
    me_dp = lax.axis_index("dp")
    me_f = lax.axis_index("fsdp")

    extra = jnp.concatenate(
        [positive // 64, positive % 64, segment_ids[0]]
    ).astype(jnp.float32)
    extra_rows = -(-extra.shape[0] // width)
    extra = jnp.pad(extra, (0, extra_rows * width - extra.shape[0]))
    packed = jnp.concatenate(
        [query_cache, region_cache, extra.reshape(extra_rows, width).astype(jnp.bfloat16)], axis=0
    )
    group_blocks = gather_blocks(packed, "fsdp")
    group_side = group_blocks[:, 2 * rows :].reshape(feature_count, extra_rows * width)
    group_ids = group_side[:, 2 * rows : 2 * rows + tokens].reshape(feature_count * tokens)
    group_ids = group_ids.astype(jnp.int32)

    gain = norm_gain.astype(jnp.float32)
    states = hidden_states.astype(jnp.float32)
    inv_rms = lax.rsqrt(jnp.mean(states * states, axis=1, keepdims=True) + EPS)
    normed = (states * inv_rms * gain).astype(jnp.bfloat16)
    labels = lax.broadcasted_iota(jnp.int32, (rows, 1), 0)
    member = segment_ids[0][None, :] == labels
    pooled_part = jnp.dot(member.astype(jnp.bfloat16), normed, preferred_element_type=jnp.float32)
    counts = jnp.sum((group_ids[None, :] == labels).astype(jnp.float32), axis=1)
    scaled_part = lax.dot_general(
        member.astype(jnp.float32),
        states * inv_rms,
        (((1,), (0,)), ((), ())),
        precision=lax.Precision.HIGHEST,
        preferred_element_type=jnp.float32,
    )
    chunk = model_width // feature_count
    both = jnp.stack([pooled_part, scaled_part]).reshape(2, rows, feature_count, chunk)
    pooled_chunk, scaled_chunk = scatter_sum(both.transpose(2, 0, 1, 3), "fsdp")
    mean_chunk = (pooled_chunk / counts[:, None]).astype(jnp.bfloat16)
    mean_pooled = gather_blocks(mean_chunk, "fsdp").transpose(1, 0, 2).reshape(rows, model_width)

    gathered = gather_blocks(group_blocks, "dp")
    mean_pooled, gathered = lax.optimization_barrier((mean_pooled, gathered))
    slice_width = model_width // data_count
    pieces = mean_pooled.reshape(rows, data_count, slice_width).transpose(1, 0, 2)
    pieces = lax.all_to_all(pieces, "dp", 0, 0, tiled=True)
    pooled_cols = pieces.reshape(pair_count, slice_width)

    query_all = gathered[:, :, :rows].transpose(0, 2, 1, 3).reshape(pair_count, feature_count * width)
    region_all = gathered[:, :, rows : 2 * rows].transpose(0, 2, 1, 3).reshape(
        pair_count, feature_count * width
    )
    side = gathered[:, :, 2 * rows :].reshape(data_count, feature_count, extra_rows * width)
    side = side.astype(jnp.float32)
    positive_all = (side[:, 0, :rows] * 64 + side[:, 0, rows : 2 * rows]).astype(jnp.int32)
    positive_all = positive_all.reshape(pair_count)

    scores = (
        lax.dot_general(query_all, region_all, contract_last, preferred_element_type=jnp.float32)
        * logit_scale
    )
    row_max = jnp.max(scores, axis=1, keepdims=True)
    log_total = row_max[:, 0] + jnp.log(jnp.sum(jnp.exp(scores - row_max), axis=1))
    columns = lax.broadcasted_iota(jnp.int32, (1, pair_count), 1)
    matched = columns == positive_all[:, None]
    target_score = jnp.sum(jnp.where(matched, scores, jnp.zeros_like(scores)), axis=1)
    mean_loss = jnp.sum(log_total - target_score) / pair_count
    grad_probs = (jnp.exp(scores - log_total[:, None]) - matched.astype(jnp.float32)).astype(
        jnp.bfloat16
    )
    query_grad_all = logit_scale * jnp.dot(grad_probs, region_all, preferred_element_type=jnp.float32)
    query_grad = lax.dynamic_slice(query_grad_all, (me_dp * rows, me_f * width), (rows, width))
    grad_low = lax.dynamic_slice(query_grad_all, (me_dp * rows, 0), (rows, feature_count * width))
    grad_low = grad_low.astype(jnp.bfloat16)
    grad_low_cols = lax.dynamic_slice(query_grad_all, (0, me_f * width), (pair_count, width))
    grad_low_cols = grad_low_cols.astype(jnp.bfloat16)
    probs_cols = lax.dynamic_slice(grad_probs, (0, me_dp * rows), (pair_count, rows))
    query_cols = lax.dynamic_slice(query_all, (0, me_f * width), (pair_count, width))
    region_grad = logit_scale * lax.dot_general(
        probs_cols, query_cols, contract_first, preferred_element_type=jnp.float32
    )

    mean_part = lax.dot_general(
        grad_low, proj_weight, contract_last, preferred_element_type=jnp.float32
    )
    mean_part, pooled_cols = lax.optimization_barrier((mean_part, pooled_cols))
    proj_grad = lax.dot_general(
        pooled_cols, grad_low_cols, contract_first, preferred_element_type=jnp.float32
    )
    gain_slice = jnp.sum((mean_part / counts[:, None]) * scaled_chunk, axis=0)
    both = jnp.concatenate([mean_part, gain_slice[None, :]], axis=0)
    both = lax.all_gather(both, "fsdp", axis=1, tiled=True)
    mean_grad = both[:rows]
    pool_grad = mean_grad / counts[:, None]
    normed_grad = lax.dot_general(
        member.astype(jnp.float32),
        pool_grad,
        contract_first,
        precision=lax.Precision.HIGHEST,
        preferred_element_type=jnp.float32,
    )
    scaled = gain * normed_grad
    inner = jnp.mean(scaled * states, axis=1, keepdims=True)
    hidden_grad = (inv_rms * scaled - states * inv_rms**3 * inner).astype(jnp.bfloat16)
    gain_grad = sum_blocks(both[rows], "dp")
    return (mean_loss, query_grad, region_grad, hidden_grad, gain_grad, proj_grad)


SMALL_PAIRS = 1024


def local(query_cache, region_cache, positive, hidden_states, segment_ids, norm_gain, proj_weight):
    pair_count = query_cache.shape[0] * lax.axis_size("dp")
    args = (query_cache, region_cache, positive, hidden_states, segment_ids, norm_gain, proj_weight)
    if pair_count <= SMALL_PAIRS:
        return local_small(*args)
    return local_sharded(*args)


def solution(mesh):
    in_specs = (
        P("dp", "fsdp"),
        P("dp", "fsdp"),
        P("dp"),
        P(("dp", "fsdp"), None),
        P("dp", "fsdp"),
        P(),
        P("fsdp", None),
    )
    out_specs = (
        P(),
        P("dp", "fsdp"),
        P("dp", "fsdp"),
        P(("dp", "fsdp"), None),
        P(),
        P("dp", "fsdp"),
    )
    return jax.shard_map(local, mesh=mesh, in_specs=in_specs, out_specs=out_specs, check_vma=False)
```

```python
import jax
import jax.numpy as jnp
from jax import lax
from jax.sharding import PartitionSpec as P

E = 1024


EPS = 1e-05


def local_sharded(query_cache, region_cache, positive, hidden_states, segment_ids, norm_gain, proj_weight):
    row_count = query_cache.shape[0]
    data_count = lax.axis_size("dp")
    pair_count = row_count * data_count
    logit_scale = float(E) ** (-0.5)
    contract_last = (((1,), (1,)), ((), ()))
    contract_first = (((0,), (0,)), ((), ()))
    region_all, query_all = (
        lax.all_gather(region_cache, "dp", axis=0, tiled=True),
        lax.all_gather(query_cache, "dp", axis=0, tiled=True),
    )
    partial_value = lax.dot_general(
        query_cache, region_all, contract_last, preferred_element_type=jnp.float32
    )
    scores = lax.psum(partial_value, "fsdp") * logit_scale
    row_max = jnp.max(scores, axis=1, keepdims=True)
    log_total = row_max[:, 0] + jnp.log(jnp.sum(jnp.exp(scores - row_max), axis=1))
    columns = lax.broadcasted_iota(jnp.int32, (1, pair_count), 1)
    matched = columns == positive[:, None]
    target_score = jnp.sum(jnp.where(matched, scores, jnp.zeros_like(scores)), axis=1)
    loss_local = jnp.sum(log_total - target_score)
    grad_probs = (jnp.exp(scores - log_total[:, None]) - matched.astype(jnp.float32)).astype(
        jnp.bfloat16
    )
    query_grad = logit_scale * jnp.dot(grad_probs, region_all, preferred_element_type=jnp.float32)
    totals_all, targets_all = (
        lax.all_gather(log_total, "dp", axis=0, tiled=True),
        lax.all_gather(positive.astype(jnp.float32), "dp", axis=0, tiled=True),
    )
    partial_t = lax.dot_general(
        region_cache, query_all, contract_last, preferred_element_type=jnp.float32
    )
    scores_t = lax.psum(partial_t, "fsdp") * logit_scale
    own_rows = (
        lax.axis_index("dp") * row_count + lax.broadcasted_iota(jnp.int32, (row_count, 1), 0)
    ).astype(jnp.float32)
    matched_t = targets_all[None, :] == own_rows
    probs_t = (jnp.exp(scores_t - totals_all[None, :]) - matched_t.astype(jnp.float32)).astype(
        jnp.bfloat16
    )
    region_grad = logit_scale * jnp.dot(probs_t, query_all, preferred_element_type=jnp.float32)
    gain = norm_gain.astype(jnp.float32)
    states = hidden_states.astype(jnp.float32)
    inv_rms = lax.rsqrt(jnp.mean(states * states, axis=1, keepdims=True) + EPS)
    normed = (states * inv_rms * gain).astype(jnp.bfloat16)
    labels = lax.broadcasted_iota(jnp.int32, (row_count, 1), 0)
    member = segment_ids[0][None, :] == labels
    pooled_part = jnp.dot(member.astype(jnp.bfloat16), normed, preferred_element_type=jnp.float32)
    counts_part = jnp.sum(member.astype(jnp.float32), axis=1)
    pooled, counts = lax.psum((pooled_part, counts_part), "fsdp")
    mean_pooled = (pooled / counts[:, None]).astype(jnp.bfloat16)
    grad_low = query_grad.astype(jnp.bfloat16)
    grad_full = lax.all_gather(grad_low, "fsdp", axis=1, tiled=True)
    mean_part = lax.dot_general(
        grad_full, proj_weight, contract_last, preferred_element_type=jnp.float32
    )
    mean_grad = lax.all_gather(mean_part, "fsdp", axis=1, tiled=True)
    pool_grad = mean_grad / counts[:, None]
    normed_grad = lax.dot_general(
        member.astype(jnp.float32),
        pool_grad,
        contract_first,
        precision=lax.Precision.HIGHEST,
        preferred_element_type=jnp.float32,
    )
    gain_part = jnp.sum(normed_grad * states * inv_rms, axis=0)
    scaled = gain * normed_grad
    inner = jnp.mean(scaled * states, axis=1, keepdims=True)
    hidden_grad = (inv_rms * scaled - states * inv_rms**3 * inner).astype(jnp.bfloat16)
    proj_grad = lax.psum_scatter(
        lax.dot_general(mean_pooled, grad_low, contract_first, preferred_element_type=jnp.float32),
        "dp",
        scatter_dimension=0,
        tiled=True,
    )
    loss_total = lax.psum(loss_local, "dp")
    gain_grad = lax.psum(gain_part, ("dp", "fsdp"))
    mean_loss = loss_total / pair_count
    return (mean_loss, query_grad, region_grad, hidden_grad, gain_grad, proj_grad)


def gather_blocks(x, axis):
    n = lax.axis_size(axis)
    copies = [x] + [
        lax.ppermute(x, axis, [(i, (i + s) % n) for i in range(n)]) for s in range(1, n)
    ]
    stack = jnp.stack(copies)
    order = (lax.axis_index(axis) - jnp.arange(n)) % n
    return jnp.take(stack, order, axis=0)


def gather_grouped(x, axis, inner):
    n = lax.axis_size(axis)
    outer = n // inner
    me = lax.axis_index(axis)
    copies = [x] + [
        lax.ppermute(x, axis, [(i, i - i % inner + (i % inner + s) % inner) for i in range(n)])
        for s in range(1, inner)
    ]
    near = jnp.take(jnp.stack(copies), (me % inner - jnp.arange(inner)) % inner, axis=0)
    copies = [near] + [
        lax.ppermute(near, axis, [(i, (i + inner * s) % n) for i in range(n)]) for s in range(1, outer)
    ]
    far = jnp.take(jnp.stack(copies), (me // inner - jnp.arange(outer)) % outer, axis=0)
    return far.reshape((n,) + x.shape)


def sum_blocks(x, axis):
    return jnp.sum(gather_blocks(x, axis), axis=0)


def scatter_sum(chunks, axis):
    n = lax.axis_size(axis)
    me = lax.axis_index(axis)
    copies = [lax.dynamic_index_in_dim(chunks, me, axis=0, keepdims=False)]
    for s in range(1, n):
        piece = lax.dynamic_index_in_dim(chunks, (me + s) % n, axis=0, keepdims=False)
        copies.append(lax.ppermute(piece, axis, [(i, (i + s) % n) for i in range(n)]))
    order = (me - jnp.arange(n)) % n
    return jnp.sum(jnp.take(jnp.stack(copies), order, axis=0), axis=0)


def local_small(query_cache, region_cache, positive, hidden_states, segment_ids, norm_gain, proj_weight):
    rows, width = query_cache.shape
    data_count = lax.axis_size("dp")
    feature_count = lax.axis_size("fsdp")
    pair_count = rows * data_count
    tokens = segment_ids.shape[1]
    model_width = hidden_states.shape[1]
    logit_scale = float(E) ** (-0.5)
    contract_last = (((1,), (1,)), ((), ()))
    contract_first = (((0,), (0,)), ((), ()))
    me_dp = lax.axis_index("dp")
    me_f = lax.axis_index("fsdp")

    extra = jnp.concatenate(
        [positive // 64, positive % 64, segment_ids[0]]
    ).astype(jnp.float32)
    extra_rows = -(-extra.shape[0] // width)
    extra = jnp.pad(extra, (0, extra_rows * width - extra.shape[0]))
    packed = jnp.concatenate(
        [query_cache, region_cache, extra.reshape(extra_rows, width).astype(jnp.bfloat16)], axis=0
    )
    group_blocks = gather_blocks(packed, "fsdp")
    group_side = group_blocks[:, 2 * rows :].reshape(feature_count, extra_rows * width)
    group_ids = group_side[:, 2 * rows : 2 * rows + tokens].reshape(feature_count * tokens)
    group_ids = group_ids.astype(jnp.int32)

    gain = norm_gain.astype(jnp.float32)
    states = hidden_states.astype(jnp.float32)
    inv_rms = lax.rsqrt(jnp.mean(states * states, axis=1, keepdims=True) + EPS)
    normed = (states * inv_rms * gain).astype(jnp.bfloat16)
    labels = lax.broadcasted_iota(jnp.int32, (rows, 1), 0)
    member = segment_ids[0][None, :] == labels
    pooled_part = jnp.dot(member.astype(jnp.bfloat16), normed, preferred_element_type=jnp.float32)
    counts = jnp.sum((group_ids[None, :] == labels).astype(jnp.float32), axis=1)
    chunk = model_width // feature_count
    pooled_chunk = scatter_sum(
        pooled_part.reshape(rows, feature_count, chunk).transpose(1, 0, 2), "fsdp"
    )
    mean_chunk = (pooled_chunk / counts[:, None]).astype(jnp.bfloat16)
    mean_pooled = gather_blocks(mean_chunk, "fsdp").transpose(1, 0, 2).reshape(rows, model_width)

    gathered = gather_grouped(group_blocks, "dp", CORES)
    mean_pooled, gathered = lax.optimization_barrier((mean_pooled, gathered))
    slice_width = model_width // data_count
    pieces = mean_pooled.reshape(rows, data_count, slice_width).transpose(1, 0, 2)
    pieces = lax.all_to_all(pieces, "dp", 0, 0, tiled=True)
    pooled_cols = pieces.reshape(pair_count, slice_width)

    query_all = gathered[:, :, :rows].transpose(0, 2, 1, 3).reshape(pair_count, feature_count * width)
    region_all = gathered[:, :, rows : 2 * rows].transpose(0, 2, 1, 3).reshape(
        pair_count, feature_count * width
    )
    side = gathered[:, :, 2 * rows :].reshape(data_count, feature_count, extra_rows * width)
    side = side.astype(jnp.float32)
    positive_all = (side[:, 0, :rows] * 64 + side[:, 0, rows : 2 * rows]).astype(jnp.int32)
    positive_all = positive_all.reshape(pair_count)

    scores = (
        lax.dot_general(query_all, region_all, contract_last, preferred_element_type=jnp.float32)
        * logit_scale
    )
    row_max = jnp.max(scores, axis=1, keepdims=True)
    log_total = row_max[:, 0] + jnp.log(jnp.sum(jnp.exp(scores - row_max), axis=1))
    columns = lax.broadcasted_iota(jnp.int32, (1, pair_count), 1)
    matched = columns == positive_all[:, None]
    target_score = jnp.sum(jnp.where(matched, scores, jnp.zeros_like(scores)), axis=1)
    mean_loss = jnp.sum(log_total - target_score) / pair_count
    grad_probs = (jnp.exp(scores - log_total[:, None]) - matched.astype(jnp.float32)).astype(
        jnp.bfloat16
    )
    query_grad_all = logit_scale * jnp.dot(grad_probs, region_all, preferred_element_type=jnp.float32)
    query_grad = lax.dynamic_slice(query_grad_all, (me_dp * rows, me_f * width), (rows, width))
    grad_low = lax.dynamic_slice(query_grad_all, (me_dp * rows, 0), (rows, feature_count * width))
    grad_low = grad_low.astype(jnp.bfloat16)
    grad_low_cols = lax.dynamic_slice(query_grad_all, (0, me_f * width), (pair_count, width))
    grad_low_cols = grad_low_cols.astype(jnp.bfloat16)
    probs_cols = lax.dynamic_slice(grad_probs, (0, me_dp * rows), (pair_count, rows))
    query_cols = lax.dynamic_slice(query_all, (0, me_f * width), (pair_count, width))
    region_grad = logit_scale * lax.dot_general(
        probs_cols, query_cols, contract_first, preferred_element_type=jnp.float32
    )

    mean_part = lax.dot_general(
        grad_low, proj_weight, contract_last, preferred_element_type=jnp.float32
    )
    mean_part, pooled_cols = lax.optimization_barrier((mean_part, pooled_cols))
    proj_grad = lax.dot_general(
        pooled_cols, grad_low_cols, contract_first, preferred_element_type=jnp.float32
    )
    mean_grad = lax.all_gather(mean_part, "fsdp", axis=1, tiled=True)
    pool_grad = mean_grad / counts[:, None]
    normed_grad = lax.dot_general(
        member.astype(jnp.float32),
        pool_grad,
        contract_first,
        precision=lax.Precision.HIGHEST,
        preferred_element_type=jnp.float32,
    )
    gain_part = jnp.sum(normed_grad * states * inv_rms, axis=0)
    scaled = gain * normed_grad
    inner = jnp.mean(scaled * states, axis=1, keepdims=True)
    hidden_grad = (inv_rms * scaled - states * inv_rms**3 * inner).astype(jnp.bfloat16)
    gain_grad = sum_blocks(jnp.sum(gather_grouped(gain_part, "dp", CORES), axis=0), "fsdp")
    return (mean_loss, query_grad, region_grad, hidden_grad, gain_grad, proj_grad)


SMALL_PAIRS = 1024
CORES = 2


def local(query_cache, region_cache, positive, hidden_states, segment_ids, norm_gain, proj_weight):
    pair_count = query_cache.shape[0] * lax.axis_size("dp")
    args = (query_cache, region_cache, positive, hidden_states, segment_ids, norm_gain, proj_weight)
    if pair_count <= SMALL_PAIRS:
        return local_small(*args)
    return local_sharded(*args)


def solution(mesh):
    in_specs = (
        P("dp", "fsdp"),
        P("dp", "fsdp"),
        P("dp"),
        P(("dp", "fsdp"), None),
        P("dp", "fsdp"),
        P(),
        P("fsdp", None),
    )
    out_specs = (
        P(),
        P("dp", "fsdp"),
        P("dp", "fsdp"),
        P(("dp", "fsdp"), None),
        P(),
        P("dp", "fsdp"),
    )
    return jax.shard_map(local, mesh=mesh, in_specs=in_specs, out_specs=out_specs, check_vma=False)
```

```python
import jax
import jax.numpy as jnp
from jax import lax
from jax.sharding import PartitionSpec as P

E = 1024


EPS = 1e-05


def local_sharded(query_cache, region_cache, positive, hidden_states, segment_ids, norm_gain, proj_weight):
    row_count = query_cache.shape[0]
    data_count = lax.axis_size("dp")
    pair_count = row_count * data_count
    logit_scale = float(E) ** (-0.5)
    contract_last = (((1,), (1,)), ((), ()))
    contract_first = (((0,), (0,)), ((), ()))
    region_all, query_all = (
        lax.all_gather(region_cache, "dp", axis=0, tiled=True),
        lax.all_gather(query_cache, "dp", axis=0, tiled=True),
    )
    partial_value = lax.dot_general(
        query_cache, region_all, contract_last, preferred_element_type=jnp.float32
    )
    scores = lax.psum(partial_value, "fsdp") * logit_scale
    row_max = jnp.max(scores, axis=1, keepdims=True)
    log_total = row_max[:, 0] + jnp.log(jnp.sum(jnp.exp(scores - row_max), axis=1))
    columns = lax.broadcasted_iota(jnp.int32, (1, pair_count), 1)
    matched = columns == positive[:, None]
    target_score = jnp.sum(jnp.where(matched, scores, jnp.zeros_like(scores)), axis=1)
    loss_local = jnp.sum(log_total - target_score)
    grad_probs = (jnp.exp(scores - log_total[:, None]) - matched.astype(jnp.float32)).astype(
        jnp.bfloat16
    )
    query_grad = logit_scale * jnp.dot(grad_probs, region_all, preferred_element_type=jnp.float32)
    totals_all, targets_all = (
        lax.all_gather(log_total, "dp", axis=0, tiled=True),
        lax.all_gather(positive.astype(jnp.float32), "dp", axis=0, tiled=True),
    )
    partial_t = lax.dot_general(
        region_cache, query_all, contract_last, preferred_element_type=jnp.float32
    )
    scores_t = lax.psum(partial_t, "fsdp") * logit_scale
    own_rows = (
        lax.axis_index("dp") * row_count + lax.broadcasted_iota(jnp.int32, (row_count, 1), 0)
    ).astype(jnp.float32)
    matched_t = targets_all[None, :] == own_rows
    probs_t = (jnp.exp(scores_t - totals_all[None, :]) - matched_t.astype(jnp.float32)).astype(
        jnp.bfloat16
    )
    region_grad = logit_scale * jnp.dot(probs_t, query_all, preferred_element_type=jnp.float32)
    gain = norm_gain.astype(jnp.float32)
    states = hidden_states.astype(jnp.float32)
    inv_rms = lax.rsqrt(jnp.mean(states * states, axis=1, keepdims=True) + EPS)
    normed = (states * inv_rms * gain).astype(jnp.bfloat16)
    labels = lax.broadcasted_iota(jnp.int32, (row_count, 1), 0)
    member = segment_ids[0][None, :] == labels
    pooled_part = jnp.dot(member.astype(jnp.bfloat16), normed, preferred_element_type=jnp.float32)
    counts_part = jnp.sum(member.astype(jnp.float32), axis=1)
    pooled, counts = lax.psum((pooled_part, counts_part), "fsdp")
    mean_pooled = (pooled / counts[:, None]).astype(jnp.bfloat16)
    grad_low = query_grad.astype(jnp.bfloat16)
    grad_full = lax.all_gather(grad_low, "fsdp", axis=1, tiled=True)
    mean_part = lax.dot_general(
        grad_full, proj_weight, contract_last, preferred_element_type=jnp.float32
    )
    mean_grad = lax.all_gather(mean_part, "fsdp", axis=1, tiled=True)
    pool_grad = mean_grad / counts[:, None]
    normed_grad = lax.dot_general(
        member.astype(jnp.float32),
        pool_grad,
        contract_first,
        precision=lax.Precision.HIGHEST,
        preferred_element_type=jnp.float32,
    )
    gain_part = jnp.sum(normed_grad * states * inv_rms, axis=0)
    scaled = gain * normed_grad
    inner = jnp.mean(scaled * states, axis=1, keepdims=True)
    hidden_grad = (inv_rms * scaled - states * inv_rms**3 * inner).astype(jnp.bfloat16)
    proj_grad = lax.psum_scatter(
        lax.dot_general(mean_pooled, grad_low, contract_first, preferred_element_type=jnp.float32),
        "dp",
        scatter_dimension=0,
        tiled=True,
    )
    loss_total = lax.psum(loss_local, "dp")
    gain_grad = lax.psum(gain_part, ("dp", "fsdp"))
    mean_loss = loss_total / pair_count
    return (mean_loss, query_grad, region_grad, hidden_grad, gain_grad, proj_grad)


def gather_blocks(x, axis):
    n = lax.axis_size(axis)
    copies = [x] + [
        lax.ppermute(x, axis, [(i, (i + s) % n) for i in range(n)]) for s in range(1, n)
    ]
    stack = jnp.stack(copies)
    order = (lax.axis_index(axis) - jnp.arange(n)) % n
    return jnp.take(stack, order, axis=0)


def sum_blocks(x, axis):
    return jnp.sum(gather_blocks(x, axis), axis=0)


def scatter_sum(chunks, axis):
    n = lax.axis_size(axis)
    me = lax.axis_index(axis)
    copies = [lax.dynamic_index_in_dim(chunks, me, axis=0, keepdims=False)]
    for s in range(1, n):
        piece = lax.dynamic_index_in_dim(chunks, (me + s) % n, axis=0, keepdims=False)
        copies.append(lax.ppermute(piece, axis, [(i, (i + s) % n) for i in range(n)]))
    order = (me - jnp.arange(n)) % n
    return jnp.sum(jnp.take(jnp.stack(copies), order, axis=0), axis=0)


def local_small(query_cache, region_cache, positive, hidden_states, segment_ids, norm_gain, proj_weight):
    rows, width = query_cache.shape
    data_count = lax.axis_size("dp")
    feature_count = lax.axis_size("fsdp")
    pair_count = rows * data_count
    tokens = segment_ids.shape[1]
    model_width = hidden_states.shape[1]
    logit_scale = float(E) ** (-0.5)
    contract_last = (((1,), (1,)), ((), ()))
    contract_first = (((0,), (0,)), ((), ()))
    me_dp = lax.axis_index("dp")
    me_f = lax.axis_index("fsdp")

    extra = jnp.concatenate(
        [positive // 64, positive % 64, segment_ids[0]]
    ).astype(jnp.float32)
    extra_rows = -(-extra.shape[0] // width)
    extra = jnp.pad(extra, (0, extra_rows * width - extra.shape[0]))
    packed = jnp.concatenate(
        [query_cache, region_cache, extra.reshape(extra_rows, width).astype(jnp.bfloat16)], axis=0
    )
    group_blocks = gather_blocks(packed, "fsdp")
    group_side = group_blocks[:, 2 * rows :].reshape(feature_count, extra_rows * width)
    group_ids = group_side[:, 2 * rows : 2 * rows + tokens].reshape(feature_count * tokens)
    group_ids = group_ids.astype(jnp.int32)

    gain = norm_gain.astype(jnp.float32)
    states = hidden_states.astype(jnp.float32)
    inv_rms = lax.rsqrt(jnp.mean(states * states, axis=1, keepdims=True) + EPS)
    normed = (states * inv_rms * gain).astype(jnp.bfloat16)
    labels = lax.broadcasted_iota(jnp.int32, (rows, 1), 0)
    member = segment_ids[0][None, :] == labels
    pooled_part = jnp.dot(member.astype(jnp.bfloat16), normed, preferred_element_type=jnp.float32)
    counts = jnp.sum((group_ids[None, :] == labels).astype(jnp.float32), axis=1)
    chunk = model_width // feature_count
    gathered = gather_blocks(group_blocks, "dp")
    pooled_part, gathered = lax.optimization_barrier((pooled_part, gathered))
    pooled_chunk = scatter_sum(
        pooled_part.reshape(rows, feature_count, chunk).transpose(1, 0, 2), "fsdp"
    )
    mean_chunk = (pooled_chunk / counts[:, None]).astype(jnp.bfloat16)
    mean_pooled = gather_blocks(mean_chunk, "fsdp").transpose(1, 0, 2).reshape(rows, model_width)

    slice_width = model_width // data_count
    pieces = mean_pooled.reshape(rows, data_count, slice_width).transpose(1, 0, 2)
    pieces = lax.all_to_all(pieces, "dp", 0, 0, tiled=True)
    pooled_cols = pieces.reshape(pair_count, slice_width)

    query_all = gathered[:, :, :rows].transpose(0, 2, 1, 3).reshape(pair_count, feature_count * width)
    region_all = gathered[:, :, rows : 2 * rows].transpose(0, 2, 1, 3).reshape(
        pair_count, feature_count * width
    )
    side = gathered[:, :, 2 * rows :].reshape(data_count, feature_count, extra_rows * width)
    side = side.astype(jnp.float32)
    positive_all = (side[:, 0, :rows] * 64 + side[:, 0, rows : 2 * rows]).astype(jnp.int32)
    positive_all = positive_all.reshape(pair_count)

    scores = (
        lax.dot_general(query_all, region_all, contract_last, preferred_element_type=jnp.float32)
        * logit_scale
    )
    row_max = jnp.max(scores, axis=1, keepdims=True)
    log_total = row_max[:, 0] + jnp.log(jnp.sum(jnp.exp(scores - row_max), axis=1))
    columns = lax.broadcasted_iota(jnp.int32, (1, pair_count), 1)
    matched = columns == positive_all[:, None]
    target_score = jnp.sum(jnp.where(matched, scores, jnp.zeros_like(scores)), axis=1)
    mean_loss = jnp.sum(log_total - target_score) / pair_count
    grad_probs = (jnp.exp(scores - log_total[:, None]) - matched.astype(jnp.float32)).astype(
        jnp.bfloat16
    )
    query_grad_all = logit_scale * jnp.dot(grad_probs, region_all, preferred_element_type=jnp.float32)
    query_grad = lax.dynamic_slice(query_grad_all, (me_dp * rows, me_f * width), (rows, width))
    grad_low = lax.dynamic_slice(query_grad_all, (me_dp * rows, 0), (rows, feature_count * width))
    grad_low = grad_low.astype(jnp.bfloat16)
    grad_low_cols = lax.dynamic_slice(query_grad_all, (0, me_f * width), (pair_count, width))
    grad_low_cols = grad_low_cols.astype(jnp.bfloat16)
    probs_cols = lax.dynamic_slice(grad_probs, (0, me_dp * rows), (pair_count, rows))
    query_cols = lax.dynamic_slice(query_all, (0, me_f * width), (pair_count, width))
    region_grad = logit_scale * lax.dot_general(
        probs_cols, query_cols, contract_first, preferred_element_type=jnp.float32
    )

    mean_part = lax.dot_general(
        grad_low, proj_weight, contract_last, preferred_element_type=jnp.float32
    )
    mean_part, pooled_cols = lax.optimization_barrier((mean_part, pooled_cols))
    proj_grad = lax.dot_general(
        pooled_cols, grad_low_cols, contract_first, preferred_element_type=jnp.float32
    )
    mean_grad = lax.all_gather(mean_part, "fsdp", axis=1, tiled=True)
    pool_grad = mean_grad / counts[:, None]
    normed_grad = lax.dot_general(
        member.astype(jnp.float32),
        pool_grad,
        contract_first,
        precision=lax.Precision.HIGHEST,
        preferred_element_type=jnp.float32,
    )
    gain_part = jnp.sum(normed_grad * states * inv_rms, axis=0)
    scaled = gain * normed_grad
    inner = jnp.mean(scaled * states, axis=1, keepdims=True)
    hidden_grad = (inv_rms * scaled - states * inv_rms**3 * inner).astype(jnp.bfloat16)
    gain_grad = sum_blocks(sum_blocks(gain_part, "dp"), "fsdp")
    return (mean_loss, query_grad, region_grad, hidden_grad, gain_grad, proj_grad)


SMALL_PAIRS = 1024


def local(query_cache, region_cache, positive, hidden_states, segment_ids, norm_gain, proj_weight):
    pair_count = query_cache.shape[0] * lax.axis_size("dp")
    args = (query_cache, region_cache, positive, hidden_states, segment_ids, norm_gain, proj_weight)
    if pair_count <= SMALL_PAIRS:
        return local_small(*args)
    return local_sharded(*args)


def solution(mesh):
    in_specs = (
        P("dp", "fsdp"),
        P("dp", "fsdp"),
        P("dp"),
        P(("dp", "fsdp"), None),
        P("dp", "fsdp"),
        P(),
        P("fsdp", None),
    )
    out_specs = (
        P(),
        P("dp", "fsdp"),
        P("dp", "fsdp"),
        P(("dp", "fsdp"), None),
        P(),
        P("dp", "fsdp"),
    )
    return jax.shard_map(local, mesh=mesh, in_specs=in_specs, out_specs=out_specs, check_vma=False)
```

```python
import jax
import jax.numpy as jnp
from jax import lax
from jax.sharding import PartitionSpec as P

E = 1024


EPS = 1e-05


def local_sharded(query_cache, region_cache, positive, hidden_states, segment_ids, norm_gain, proj_weight):
    row_count = query_cache.shape[0]
    data_count = lax.axis_size("dp")
    pair_count = row_count * data_count
    logit_scale = float(E) ** (-0.5)
    contract_last = (((1,), (1,)), ((), ()))
    contract_first = (((0,), (0,)), ((), ()))
    region_all, query_all = (
        lax.all_gather(region_cache, "dp", axis=0, tiled=True),
        lax.all_gather(query_cache, "dp", axis=0, tiled=True),
    )
    partial_value = lax.dot_general(
        query_cache, region_all, contract_last, preferred_element_type=jnp.float32
    )
    scores = lax.psum(partial_value, "fsdp") * logit_scale
    row_max = jnp.max(scores, axis=1, keepdims=True)
    log_total = row_max[:, 0] + jnp.log(jnp.sum(jnp.exp(scores - row_max), axis=1))
    columns = lax.broadcasted_iota(jnp.int32, (1, pair_count), 1)
    matched = columns == positive[:, None]
    target_score = jnp.sum(jnp.where(matched, scores, jnp.zeros_like(scores)), axis=1)
    loss_local = jnp.sum(log_total - target_score)
    grad_probs = (jnp.exp(scores - log_total[:, None]) - matched.astype(jnp.float32)).astype(
        jnp.bfloat16
    )
    query_grad = logit_scale * jnp.dot(grad_probs, region_all, preferred_element_type=jnp.float32)
    totals_all, targets_all = (
        lax.all_gather(log_total, "dp", axis=0, tiled=True),
        lax.all_gather(positive.astype(jnp.float32), "dp", axis=0, tiled=True),
    )
    partial_t = lax.dot_general(
        region_cache, query_all, contract_last, preferred_element_type=jnp.float32
    )
    scores_t = lax.psum(partial_t, "fsdp") * logit_scale
    own_rows = (
        lax.axis_index("dp") * row_count + lax.broadcasted_iota(jnp.int32, (row_count, 1), 0)
    ).astype(jnp.float32)
    matched_t = targets_all[None, :] == own_rows
    probs_t = (jnp.exp(scores_t - totals_all[None, :]) - matched_t.astype(jnp.float32)).astype(
        jnp.bfloat16
    )
    region_grad = logit_scale * jnp.dot(probs_t, query_all, preferred_element_type=jnp.float32)
    gain = norm_gain.astype(jnp.float32)
    states = hidden_states.astype(jnp.float32)
    inv_rms = lax.rsqrt(jnp.mean(states * states, axis=1, keepdims=True) + EPS)
    normed = (states * inv_rms * gain).astype(jnp.bfloat16)
    labels = lax.broadcasted_iota(jnp.int32, (row_count, 1), 0)
    member = segment_ids[0][None, :] == labels
    pooled_part = jnp.dot(member.astype(jnp.bfloat16), normed, preferred_element_type=jnp.float32)
    counts_part = jnp.sum(member.astype(jnp.float32), axis=1)
    pooled, counts = lax.psum((pooled_part, counts_part), "fsdp")
    mean_pooled = (pooled / counts[:, None]).astype(jnp.bfloat16)
    grad_low = query_grad.astype(jnp.bfloat16)
    grad_full = lax.all_gather(grad_low, "fsdp", axis=1, tiled=True)
    mean_part = lax.dot_general(
        grad_full, proj_weight, contract_last, preferred_element_type=jnp.float32
    )
    mean_grad = lax.all_gather(mean_part, "fsdp", axis=1, tiled=True)
    pool_grad = mean_grad / counts[:, None]
    normed_grad = lax.dot_general(
        member.astype(jnp.float32),
        pool_grad,
        contract_first,
        precision=lax.Precision.HIGHEST,
        preferred_element_type=jnp.float32,
    )
    gain_part = jnp.sum(normed_grad * states * inv_rms, axis=0)
    scaled = gain * normed_grad
    inner = jnp.mean(scaled * states, axis=1, keepdims=True)
    hidden_grad = (inv_rms * scaled - states * inv_rms**3 * inner).astype(jnp.bfloat16)
    proj_grad = lax.psum_scatter(
        lax.dot_general(mean_pooled, grad_low, contract_first, preferred_element_type=jnp.float32),
        "dp",
        scatter_dimension=0,
        tiled=True,
    )
    loss_total = lax.psum(loss_local, "dp")
    gain_grad = lax.psum(gain_part, ("dp", "fsdp"))
    mean_loss = loss_total / pair_count
    return (mean_loss, query_grad, region_grad, hidden_grad, gain_grad, proj_grad)


def gather_blocks(x, axis):
    n = lax.axis_size(axis)
    copies = [x] + [
        lax.ppermute(x, axis, [(i, (i + s) % n) for i in range(n)]) for s in range(1, n)
    ]
    stack = jnp.stack(copies)
    order = (lax.axis_index(axis) - jnp.arange(n)) % n
    return jnp.take(stack, order, axis=0)


def sum_blocks(x, axis):
    return jnp.sum(gather_blocks(x, axis), axis=0)


def scatter_sum(chunks, axis):
    n = lax.axis_size(axis)
    me = lax.axis_index(axis)
    copies = [lax.dynamic_index_in_dim(chunks, me, axis=0, keepdims=False)]
    for s in range(1, n):
        piece = lax.dynamic_index_in_dim(chunks, (me + s) % n, axis=0, keepdims=False)
        copies.append(lax.ppermute(piece, axis, [(i, (i + s) % n) for i in range(n)]))
    order = (me - jnp.arange(n)) % n
    return jnp.sum(jnp.take(jnp.stack(copies), order, axis=0), axis=0)


def local_small(query_cache, region_cache, positive, hidden_states, segment_ids, norm_gain, proj_weight):
    rows, width = query_cache.shape
    data_count = lax.axis_size("dp")
    feature_count = lax.axis_size("fsdp")
    pair_count = rows * data_count
    tokens = segment_ids.shape[1]
    model_width = hidden_states.shape[1]
    logit_scale = float(E) ** (-0.5)
    contract_last = (((1,), (1,)), ((), ()))
    contract_first = (((0,), (0,)), ((), ()))
    me_dp = lax.axis_index("dp")
    me_f = lax.axis_index("fsdp")

    extra = jnp.concatenate(
        [positive // 64, positive % 64, segment_ids[0]]
    ).astype(jnp.float32)
    extra_rows = -(-extra.shape[0] // width)
    extra = jnp.pad(extra, (0, extra_rows * width - extra.shape[0]))
    packed = jnp.concatenate(
        [query_cache, region_cache, extra.reshape(extra_rows, width).astype(jnp.bfloat16)], axis=0
    )
    group_blocks = gather_blocks(packed, "fsdp")
    group_side = group_blocks[:, 2 * rows :].reshape(feature_count, extra_rows * width)
    group_ids = group_side[:, 2 * rows : 2 * rows + tokens].reshape(feature_count * tokens)
    group_ids = group_ids.astype(jnp.int32)

    gain = norm_gain.astype(jnp.float32)
    states = hidden_states.astype(jnp.float32)
    inv_rms = lax.rsqrt(jnp.mean(states * states, axis=1, keepdims=True) + EPS)
    normed = (states * inv_rms * gain).astype(jnp.bfloat16)
    labels = lax.broadcasted_iota(jnp.int32, (rows, 1), 0)
    member = segment_ids[0][None, :] == labels
    pooled_part = jnp.dot(member.astype(jnp.bfloat16), normed, preferred_element_type=jnp.float32)
    counts = jnp.sum((group_ids[None, :] == labels).astype(jnp.float32), axis=1)
    chunk = model_width // feature_count
    gathered = gather_blocks(group_blocks, "dp")
    pooled_part, gathered = lax.optimization_barrier((pooled_part, gathered))
    pooled_chunk = scatter_sum(
        pooled_part.reshape(rows, feature_count, chunk).transpose(1, 0, 2), "fsdp"
    )
    mean_chunk = (pooled_chunk / counts[:, None]).astype(jnp.bfloat16)
    mean_pooled = gather_blocks(mean_chunk, "fsdp").transpose(1, 0, 2).reshape(rows, model_width)

    slice_width = model_width // data_count
    pieces = mean_pooled.reshape(rows, data_count, slice_width).transpose(1, 0, 2)
    pieces = lax.all_to_all(pieces, "dp", 0, 0, tiled=True)
    pooled_cols = pieces.reshape(pair_count, slice_width)

    query_all = gathered[:, :, :rows].transpose(0, 2, 1, 3).reshape(pair_count, feature_count * width)
    region_all = gathered[:, :, rows : 2 * rows].transpose(0, 2, 1, 3).reshape(
        pair_count, feature_count * width
    )
    side = gathered[:, :, 2 * rows :].reshape(data_count, feature_count, extra_rows * width)
    side = side.astype(jnp.float32)
    positive_all = (side[:, 0, :rows] * 64 + side[:, 0, rows : 2 * rows]).astype(jnp.int32)
    positive_all = positive_all.reshape(pair_count)

    scores = (
        lax.dot_general(query_all, region_all, contract_last, preferred_element_type=jnp.float32)
        * logit_scale
    )
    row_max = jnp.max(scores, axis=1, keepdims=True)
    log_total = row_max[:, 0] + jnp.log(jnp.sum(jnp.exp(scores - row_max), axis=1))
    columns = lax.broadcasted_iota(jnp.int32, (1, pair_count), 1)
    matched = columns == positive_all[:, None]
    target_score = jnp.sum(jnp.where(matched, scores, jnp.zeros_like(scores)), axis=1)
    mean_loss = jnp.sum(log_total - target_score) / pair_count
    grad_probs = (jnp.exp(scores - log_total[:, None]) - matched.astype(jnp.float32)).astype(
        jnp.bfloat16
    )
    query_grad_all = logit_scale * jnp.dot(grad_probs, region_all, preferred_element_type=jnp.float32)
    query_grad = lax.dynamic_slice(query_grad_all, (me_dp * rows, me_f * width), (rows, width))
    grad_low = lax.dynamic_slice(query_grad_all, (me_dp * rows, 0), (rows, feature_count * width))
    grad_low = grad_low.astype(jnp.bfloat16)
    grad_low_cols = lax.dynamic_slice(query_grad_all, (0, me_f * width), (pair_count, width))
    grad_low_cols = grad_low_cols.astype(jnp.bfloat16)
    probs_cols = lax.dynamic_slice(grad_probs, (0, me_dp * rows), (pair_count, rows))
    query_cols = lax.dynamic_slice(query_all, (0, me_f * width), (pair_count, width))
    region_grad = logit_scale * lax.dot_general(
        probs_cols, query_cols, contract_first, preferred_element_type=jnp.float32
    )

    mean_part = lax.dot_general(
        grad_low, proj_weight, contract_last, preferred_element_type=jnp.float32
    )
    proj_grad = lax.dot_general(
        pooled_cols, grad_low_cols, contract_first, preferred_element_type=jnp.float32
    )
    mean_grad = lax.all_gather(mean_part, "fsdp", axis=1, tiled=True)
    pool_grad = mean_grad / counts[:, None]
    normed_grad = lax.dot_general(
        member.astype(jnp.float32),
        pool_grad,
        contract_first,
        precision=lax.Precision.HIGHEST,
        preferred_element_type=jnp.float32,
    )
    gain_part = jnp.sum(normed_grad * states * inv_rms, axis=0)
    scaled = gain * normed_grad
    inner = jnp.mean(scaled * states, axis=1, keepdims=True)
    hidden_grad = (inv_rms * scaled - states * inv_rms**3 * inner).astype(jnp.bfloat16)
    gain_grad = sum_blocks(sum_blocks(gain_part, "dp"), "fsdp")
    return (mean_loss, query_grad, region_grad, hidden_grad, gain_grad, proj_grad)


SMALL_PAIRS = 1024


def local(query_cache, region_cache, positive, hidden_states, segment_ids, norm_gain, proj_weight):
    pair_count = query_cache.shape[0] * lax.axis_size("dp")
    args = (query_cache, region_cache, positive, hidden_states, segment_ids, norm_gain, proj_weight)
    if pair_count <= SMALL_PAIRS:
        return local_small(*args)
    return local_sharded(*args)


def solution(mesh):
    in_specs = (
        P("dp", "fsdp"),
        P("dp", "fsdp"),
        P("dp"),
        P(("dp", "fsdp"), None),
        P("dp", "fsdp"),
        P(),
        P("fsdp", None),
    )
    out_specs = (
        P(),
        P("dp", "fsdp"),
        P("dp", "fsdp"),
        P(("dp", "fsdp"), None),
        P(),
        P("dp", "fsdp"),
    )
    return jax.shard_map(local, mesh=mesh, in_specs=in_specs, out_specs=out_specs, check_vma=False)
```

```python
import jax
import jax.numpy as jnp
from jax import lax
from jax.sharding import PartitionSpec as P

E = 1024


EPS = 1e-05


def local_sharded(query_cache, region_cache, positive, hidden_states, segment_ids, norm_gain, proj_weight):
    row_count = query_cache.shape[0]
    data_count = lax.axis_size("dp")
    pair_count = row_count * data_count
    logit_scale = float(E) ** (-0.5)
    contract_last = (((1,), (1,)), ((), ()))
    contract_first = (((0,), (0,)), ((), ()))
    region_all, query_all = (
        lax.all_gather(region_cache, "dp", axis=0, tiled=True),
        lax.all_gather(query_cache, "dp", axis=0, tiled=True),
    )
    partial_value = lax.dot_general(
        query_cache, region_all, contract_last, preferred_element_type=jnp.float32
    )
    scores = lax.psum(partial_value, "fsdp") * logit_scale
    row_max = jnp.max(scores, axis=1, keepdims=True)
    log_total = row_max[:, 0] + jnp.log(jnp.sum(jnp.exp(scores - row_max), axis=1))
    columns = lax.broadcasted_iota(jnp.int32, (1, pair_count), 1)
    matched = columns == positive[:, None]
    target_score = jnp.sum(jnp.where(matched, scores, jnp.zeros_like(scores)), axis=1)
    loss_local = jnp.sum(log_total - target_score)
    grad_probs = (jnp.exp(scores - log_total[:, None]) - matched.astype(jnp.float32)).astype(
        jnp.bfloat16
    )
    query_grad = logit_scale * jnp.dot(grad_probs, region_all, preferred_element_type=jnp.float32)
    totals_all, targets_all = (
        lax.all_gather(log_total, "dp", axis=0, tiled=True),
        lax.all_gather(positive.astype(jnp.float32), "dp", axis=0, tiled=True),
    )
    partial_t = lax.dot_general(
        region_cache, query_all, contract_last, preferred_element_type=jnp.float32
    )
    scores_t = lax.psum(partial_t, "fsdp") * logit_scale
    own_rows = (
        lax.axis_index("dp") * row_count + lax.broadcasted_iota(jnp.int32, (row_count, 1), 0)
    ).astype(jnp.float32)
    matched_t = targets_all[None, :] == own_rows
    probs_t = (jnp.exp(scores_t - totals_all[None, :]) - matched_t.astype(jnp.float32)).astype(
        jnp.bfloat16
    )
    region_grad = logit_scale * jnp.dot(probs_t, query_all, preferred_element_type=jnp.float32)
    gain = norm_gain.astype(jnp.float32)
    states = hidden_states.astype(jnp.float32)
    inv_rms = lax.rsqrt(jnp.mean(states * states, axis=1, keepdims=True) + EPS)
    normed = (states * inv_rms * gain).astype(jnp.bfloat16)
    labels = lax.broadcasted_iota(jnp.int32, (row_count, 1), 0)
    member = segment_ids[0][None, :] == labels
    pooled_part = jnp.dot(member.astype(jnp.bfloat16), normed, preferred_element_type=jnp.float32)
    counts_part = jnp.sum(member.astype(jnp.float32), axis=1)
    pooled, counts = lax.psum((pooled_part, counts_part), "fsdp")
    mean_pooled = (pooled / counts[:, None]).astype(jnp.bfloat16)
    grad_low = query_grad.astype(jnp.bfloat16)
    grad_full = lax.all_gather(grad_low, "fsdp", axis=1, tiled=True)
    mean_part = lax.dot_general(
        grad_full, proj_weight, contract_last, preferred_element_type=jnp.float32
    )
    mean_grad = lax.all_gather(mean_part, "fsdp", axis=1, tiled=True)
    pool_grad = mean_grad / counts[:, None]
    normed_grad = lax.dot_general(
        member.astype(jnp.float32),
        pool_grad,
        contract_first,
        precision=lax.Precision.HIGHEST,
        preferred_element_type=jnp.float32,
    )
    gain_part = jnp.sum(normed_grad * states * inv_rms, axis=0)
    scaled = gain * normed_grad
    inner = jnp.mean(scaled * states, axis=1, keepdims=True)
    hidden_grad = (inv_rms * scaled - states * inv_rms**3 * inner).astype(jnp.bfloat16)
    proj_grad = lax.psum_scatter(
        lax.dot_general(mean_pooled, grad_low, contract_first, preferred_element_type=jnp.float32),
        "dp",
        scatter_dimension=0,
        tiled=True,
    )
    loss_total = lax.psum(loss_local, "dp")
    gain_grad = lax.psum(gain_part, ("dp", "fsdp"))
    mean_loss = loss_total / pair_count
    return (mean_loss, query_grad, region_grad, hidden_grad, gain_grad, proj_grad)


def gather_blocks(x, axis):
    n = lax.axis_size(axis)
    copies = [x] + [
        lax.ppermute(x, axis, [(i, (i + s) % n) for i in range(n)]) for s in range(1, n)
    ]
    stack = jnp.stack(copies)
    order = (lax.axis_index(axis) - jnp.arange(n)) % n
    return jnp.take(stack, order, axis=0)


def sum_blocks(x, axis):
    return jnp.sum(gather_blocks(x, axis), axis=0)


def scatter_sum(chunks, axis):
    n = lax.axis_size(axis)
    me = lax.axis_index(axis)
    copies = [lax.dynamic_index_in_dim(chunks, me, axis=0, keepdims=False)]
    for s in range(1, n):
        piece = lax.dynamic_index_in_dim(chunks, (me + s) % n, axis=0, keepdims=False)
        copies.append(lax.ppermute(piece, axis, [(i, (i + s) % n) for i in range(n)]))
    order = (me - jnp.arange(n)) % n
    return jnp.sum(jnp.take(jnp.stack(copies), order, axis=0), axis=0)


def local_small(query_cache, region_cache, positive, hidden_states, segment_ids, norm_gain, proj_weight):
    rows, width = query_cache.shape
    data_count = lax.axis_size("dp")
    feature_count = lax.axis_size("fsdp")
    pair_count = rows * data_count
    tokens = segment_ids.shape[1]
    model_width = hidden_states.shape[1]
    logit_scale = float(E) ** (-0.5)
    contract_last = (((1,), (1,)), ((), ()))
    contract_first = (((0,), (0,)), ((), ()))
    me_dp = lax.axis_index("dp")
    me_f = lax.axis_index("fsdp")

    extra = jnp.concatenate(
        [positive // 64, positive % 64, segment_ids[0]]
    ).astype(jnp.float32)
    extra_rows = -(-extra.shape[0] // width)
    extra = jnp.pad(extra, (0, extra_rows * width - extra.shape[0]))
    packed = jnp.concatenate(
        [query_cache, region_cache, extra.reshape(extra_rows, width).astype(jnp.bfloat16)], axis=0
    )
    group_blocks = gather_blocks(packed, "fsdp")
    group_side = group_blocks[:, 2 * rows :].reshape(feature_count, extra_rows * width)
    group_ids = group_side[:, 2 * rows : 2 * rows + tokens].reshape(feature_count * tokens)
    group_ids = group_ids.astype(jnp.int32)

    gain = norm_gain.astype(jnp.float32)
    states = hidden_states.astype(jnp.float32)
    inv_rms = lax.rsqrt(jnp.mean(states * states, axis=1, keepdims=True) + EPS)
    normed = (states * inv_rms * gain).astype(jnp.bfloat16)
    labels = lax.broadcasted_iota(jnp.int32, (rows, 1), 0)
    member = segment_ids[0][None, :] == labels
    pooled_part = jnp.dot(member.astype(jnp.bfloat16), normed, preferred_element_type=jnp.float32)
    counts = jnp.sum((group_ids[None, :] == labels).astype(jnp.float32), axis=1)
    scaled_part = lax.dot_general(
        member.astype(jnp.float32),
        states * inv_rms,
        (((1,), (0,)), ((), ())),
        precision=lax.Precision.HIGHEST,
        preferred_element_type=jnp.float32,
    )
    chunk = model_width // feature_count
    gathered = gather_blocks(group_blocks, "dp")
    both = jnp.stack([pooled_part, scaled_part]).reshape(2, rows, feature_count, chunk)
    both, gathered = lax.optimization_barrier((both, gathered))
    pooled_chunk, scaled_chunk = scatter_sum(both.transpose(2, 0, 1, 3), "fsdp")
    mean_chunk = (pooled_chunk / counts[:, None]).astype(jnp.bfloat16)
    mean_pooled = gather_blocks(mean_chunk, "fsdp").transpose(1, 0, 2).reshape(rows, model_width)

    slice_width = model_width // data_count
    pieces = mean_pooled.reshape(rows, data_count, slice_width).transpose(1, 0, 2)
    pieces = lax.all_to_all(pieces, "dp", 0, 0, tiled=True)
    pooled_cols = pieces.reshape(pair_count, slice_width)

    query_all = gathered[:, :, :rows].transpose(0, 2, 1, 3).reshape(pair_count, feature_count * width)
    region_all = gathered[:, :, rows : 2 * rows].transpose(0, 2, 1, 3).reshape(
        pair_count, feature_count * width
    )
    side = gathered[:, :, 2 * rows :].reshape(data_count, feature_count, extra_rows * width)
    side = side.astype(jnp.float32)
    positive_all = (side[:, 0, :rows] * 64 + side[:, 0, rows : 2 * rows]).astype(jnp.int32)
    positive_all = positive_all.reshape(pair_count)

    scores = (
        lax.dot_general(query_all, region_all, contract_last, preferred_element_type=jnp.float32)
        * logit_scale
    )
    row_max = jnp.max(scores, axis=1, keepdims=True)
    log_total = row_max[:, 0] + jnp.log(jnp.sum(jnp.exp(scores - row_max), axis=1))
    columns = lax.broadcasted_iota(jnp.int32, (1, pair_count), 1)
    matched = columns == positive_all[:, None]
    target_score = jnp.sum(jnp.where(matched, scores, jnp.zeros_like(scores)), axis=1)
    mean_loss = jnp.sum(log_total - target_score) / pair_count
    grad_probs = (jnp.exp(scores - log_total[:, None]) - matched.astype(jnp.float32)).astype(
        jnp.bfloat16
    )
    query_grad_all = logit_scale * jnp.dot(grad_probs, region_all, preferred_element_type=jnp.float32)
    query_grad = lax.dynamic_slice(query_grad_all, (me_dp * rows, me_f * width), (rows, width))
    grad_low = lax.dynamic_slice(query_grad_all, (me_dp * rows, 0), (rows, feature_count * width))
    grad_low = grad_low.astype(jnp.bfloat16)
    grad_low_cols = lax.dynamic_slice(query_grad_all, (0, me_f * width), (pair_count, width))
    grad_low_cols = grad_low_cols.astype(jnp.bfloat16)
    probs_cols = lax.dynamic_slice(grad_probs, (0, me_dp * rows), (pair_count, rows))
    query_cols = lax.dynamic_slice(query_all, (0, me_f * width), (pair_count, width))
    region_grad = logit_scale * lax.dot_general(
        probs_cols, query_cols, contract_first, preferred_element_type=jnp.float32
    )

    mean_part = lax.dot_general(
        grad_low, proj_weight, contract_last, preferred_element_type=jnp.float32
    )
    proj_grad = lax.dot_general(
        pooled_cols, grad_low_cols, contract_first, preferred_element_type=jnp.float32
    )
    gain_slice = jnp.sum((mean_part / counts[:, None]) * scaled_chunk, axis=0)
    both = jnp.concatenate([mean_part, gain_slice[None, :]], axis=0)
    both = lax.all_gather(both, "fsdp", axis=1, tiled=True)
    mean_grad = both[:rows]
    pool_grad = mean_grad / counts[:, None]
    normed_grad = lax.dot_general(
        member.astype(jnp.float32),
        pool_grad,
        contract_first,
        precision=lax.Precision.HIGHEST,
        preferred_element_type=jnp.float32,
    )
    scaled = gain * normed_grad
    inner = jnp.mean(scaled * states, axis=1, keepdims=True)
    hidden_grad = (inv_rms * scaled - states * inv_rms**3 * inner).astype(jnp.bfloat16)
    gain_grad = sum_blocks(both[rows], "dp")
    return (mean_loss, query_grad, region_grad, hidden_grad, gain_grad, proj_grad)


SMALL_PAIRS = 1024


def local(query_cache, region_cache, positive, hidden_states, segment_ids, norm_gain, proj_weight):
    pair_count = query_cache.shape[0] * lax.axis_size("dp")
    args = (query_cache, region_cache, positive, hidden_states, segment_ids, norm_gain, proj_weight)
    if pair_count <= SMALL_PAIRS:
        return local_small(*args)
    return local_sharded(*args)


def solution(mesh):
    in_specs = (
        P("dp", "fsdp"),
        P("dp", "fsdp"),
        P("dp"),
        P(("dp", "fsdp"), None),
        P("dp", "fsdp"),
        P(),
        P("fsdp", None),
    )
    out_specs = (
        P(),
        P("dp", "fsdp"),
        P("dp", "fsdp"),
        P(("dp", "fsdp"), None),
        P(),
        P("dp", "fsdp"),
    )
    return jax.shard_map(local, mesh=mesh, in_specs=in_specs, out_specs=out_specs, check_vma=False)
```

```python
import jax
import jax.numpy as jnp
from jax import lax
from jax.sharding import PartitionSpec as P

E = 1024


EPS = 1e-05


def local_sharded(query_cache, region_cache, positive, hidden_states, segment_ids, norm_gain, proj_weight):
    row_count = query_cache.shape[0]
    data_count = lax.axis_size("dp")
    pair_count = row_count * data_count
    logit_scale = float(E) ** (-0.5)
    contract_last = (((1,), (1,)), ((), ()))
    contract_first = (((0,), (0,)), ((), ()))
    region_all, query_all = (
        lax.all_gather(region_cache, "dp", axis=0, tiled=True),
        lax.all_gather(query_cache, "dp", axis=0, tiled=True),
    )
    partial_value = lax.dot_general(
        query_cache, region_all, contract_last, preferred_element_type=jnp.float32
    )
    scores = lax.psum(partial_value, "fsdp") * logit_scale
    row_max = jnp.max(scores, axis=1, keepdims=True)
    log_total = row_max[:, 0] + jnp.log(jnp.sum(jnp.exp(scores - row_max), axis=1))
    columns = lax.broadcasted_iota(jnp.int32, (1, pair_count), 1)
    matched = columns == positive[:, None]
    target_score = jnp.sum(jnp.where(matched, scores, jnp.zeros_like(scores)), axis=1)
    loss_local = jnp.sum(log_total - target_score)
    grad_probs = (jnp.exp(scores - log_total[:, None]) - matched.astype(jnp.float32)).astype(
        jnp.bfloat16
    )
    query_grad = logit_scale * jnp.dot(grad_probs, region_all, preferred_element_type=jnp.float32)
    totals_all, targets_all = (
        lax.all_gather(log_total, "dp", axis=0, tiled=True),
        lax.all_gather(positive.astype(jnp.float32), "dp", axis=0, tiled=True),
    )
    partial_t = lax.dot_general(
        region_cache, query_all, contract_last, preferred_element_type=jnp.float32
    )
    scores_t = lax.psum(partial_t, "fsdp") * logit_scale
    own_rows = (
        lax.axis_index("dp") * row_count + lax.broadcasted_iota(jnp.int32, (row_count, 1), 0)
    ).astype(jnp.float32)
    matched_t = targets_all[None, :] == own_rows
    probs_t = (jnp.exp(scores_t - totals_all[None, :]) - matched_t.astype(jnp.float32)).astype(
        jnp.bfloat16
    )
    region_grad = logit_scale * jnp.dot(probs_t, query_all, preferred_element_type=jnp.float32)
    gain = norm_gain.astype(jnp.float32)
    states = hidden_states.astype(jnp.float32)
    inv_rms = lax.rsqrt(jnp.mean(states * states, axis=1, keepdims=True) + EPS)
    normed = (states * inv_rms * gain).astype(jnp.bfloat16)
    labels = lax.broadcasted_iota(jnp.int32, (row_count, 1), 0)
    member = segment_ids[0][None, :] == labels
    pooled_part = jnp.dot(member.astype(jnp.bfloat16), normed, preferred_element_type=jnp.float32)
    counts_part = jnp.sum(member.astype(jnp.float32), axis=1)
    pooled, counts = lax.psum((pooled_part, counts_part), "fsdp")
    mean_pooled = (pooled / counts[:, None]).astype(jnp.bfloat16)
    grad_low = query_grad.astype(jnp.bfloat16)
    grad_full = lax.all_gather(grad_low, "fsdp", axis=1, tiled=True)
    mean_part = lax.dot_general(
        grad_full, proj_weight, contract_last, preferred_element_type=jnp.float32
    )
    mean_grad = lax.all_gather(mean_part, "fsdp", axis=1, tiled=True)
    pool_grad = mean_grad / counts[:, None]
    normed_grad = lax.dot_general(
        member.astype(jnp.float32),
        pool_grad,
        contract_first,
        precision=lax.Precision.HIGHEST,
        preferred_element_type=jnp.float32,
    )
    gain_part = jnp.sum(normed_grad * states * inv_rms, axis=0)
    scaled = gain * normed_grad
    inner = jnp.mean(scaled * states, axis=1, keepdims=True)
    hidden_grad = (inv_rms * scaled - states * inv_rms**3 * inner).astype(jnp.bfloat16)
    proj_grad = lax.psum_scatter(
        lax.dot_general(mean_pooled, grad_low, contract_first, preferred_element_type=jnp.float32),
        "dp",
        scatter_dimension=0,
        tiled=True,
    )
    loss_total = lax.psum(loss_local, "dp")
    gain_grad = lax.psum(gain_part, ("dp", "fsdp"))
    mean_loss = loss_total / pair_count
    return (mean_loss, query_grad, region_grad, hidden_grad, gain_grad, proj_grad)


def gather_blocks(x, axis):
    n = lax.axis_size(axis)
    copies = [x] + [
        lax.ppermute(x, axis, [(i, (i + s) % n) for i in range(n)]) for s in range(1, n)
    ]
    stack = jnp.stack(copies)
    order = (lax.axis_index(axis) - jnp.arange(n)) % n
    return jnp.take(stack, order, axis=0)


def gather_grouped(x, axis, inner):
    n = lax.axis_size(axis)
    outer = n // inner
    me = lax.axis_index(axis)
    copies = [x] + [
        lax.ppermute(x, axis, [(i, i - i % inner + (i % inner + s) % inner) for i in range(n)])
        for s in range(1, inner)
    ]
    near = jnp.take(jnp.stack(copies), (me % inner - jnp.arange(inner)) % inner, axis=0)
    copies = [near] + [
        lax.ppermute(near, axis, [(i, (i + inner * s) % n) for i in range(n)]) for s in range(1, outer)
    ]
    far = jnp.take(jnp.stack(copies), (me // inner - jnp.arange(outer)) % outer, axis=0)
    return far.reshape((n,) + x.shape)


def sum_blocks(x, axis):
    return jnp.sum(gather_blocks(x, axis), axis=0)


def scatter_sum(chunks, axis):
    n = lax.axis_size(axis)
    me = lax.axis_index(axis)
    copies = [lax.dynamic_index_in_dim(chunks, me, axis=0, keepdims=False)]
    for s in range(1, n):
        piece = lax.dynamic_index_in_dim(chunks, (me + s) % n, axis=0, keepdims=False)
        copies.append(lax.ppermute(piece, axis, [(i, (i + s) % n) for i in range(n)]))
    order = (me - jnp.arange(n)) % n
    return jnp.sum(jnp.take(jnp.stack(copies), order, axis=0), axis=0)


def local_small(query_cache, region_cache, positive, hidden_states, segment_ids, norm_gain, proj_weight):
    rows, width = query_cache.shape
    data_count = lax.axis_size("dp")
    feature_count = lax.axis_size("fsdp")
    pair_count = rows * data_count
    tokens = segment_ids.shape[1]
    model_width = hidden_states.shape[1]
    logit_scale = float(E) ** (-0.5)
    contract_last = (((1,), (1,)), ((), ()))
    contract_first = (((0,), (0,)), ((), ()))
    me_dp = lax.axis_index("dp")
    me_f = lax.axis_index("fsdp")

    extra = jnp.concatenate(
        [positive // 64, positive % 64, segment_ids[0]]
    ).astype(jnp.float32)
    extra_rows = -(-extra.shape[0] // width)
    extra = jnp.pad(extra, (0, extra_rows * width - extra.shape[0]))
    packed = jnp.concatenate(
        [query_cache, region_cache, extra.reshape(extra_rows, width).astype(jnp.bfloat16)], axis=0
    )
    group_blocks = gather_blocks(packed, "fsdp")
    group_side = group_blocks[:, 2 * rows :].reshape(feature_count, extra_rows * width)
    group_ids = group_side[:, 2 * rows : 2 * rows + tokens].reshape(feature_count * tokens)
    group_ids = group_ids.astype(jnp.int32)

    gain = norm_gain.astype(jnp.float32)
    states = hidden_states.astype(jnp.float32)
    inv_rms = lax.rsqrt(jnp.mean(states * states, axis=1, keepdims=True) + EPS)
    normed = (states * inv_rms * gain).astype(jnp.bfloat16)
    labels = lax.broadcasted_iota(jnp.int32, (rows, 1), 0)
    member = segment_ids[0][None, :] == labels
    pooled_part = jnp.dot(member.astype(jnp.bfloat16), normed, preferred_element_type=jnp.float32)
    counts = jnp.sum((group_ids[None, :] == labels).astype(jnp.float32), axis=1)
    chunk = model_width // feature_count
    pooled_chunk = scatter_sum(
        pooled_part.reshape(rows, feature_count, chunk).transpose(1, 0, 2), "fsdp"
    )
    mean_chunk = (pooled_chunk / counts[:, None]).astype(jnp.bfloat16)
    mean_pooled = gather_blocks(mean_chunk, "fsdp").transpose(1, 0, 2).reshape(rows, model_width)

    gathered = gather_blocks(group_blocks, "dp")
    mean_pooled, gathered = lax.optimization_barrier((mean_pooled, gathered))
    slice_width = model_width // data_count
    pieces = mean_pooled.reshape(rows, data_count, slice_width).transpose(1, 0, 2)
    pieces = lax.all_to_all(pieces, "dp", 0, 0, tiled=True)
    pooled_cols = pieces.reshape(pair_count, slice_width)

    query_all = gathered[:, :, :rows].transpose(0, 2, 1, 3).reshape(pair_count, feature_count * width)
    region_all = gathered[:, :, rows : 2 * rows].transpose(0, 2, 1, 3).reshape(
        pair_count, feature_count * width
    )
    side = gathered[:, :, 2 * rows :].reshape(data_count, feature_count, extra_rows * width)
    side = side.astype(jnp.float32)
    positive_all = (side[:, 0, :rows] * 64 + side[:, 0, rows : 2 * rows]).astype(jnp.int32)
    positive_all = positive_all.reshape(pair_count)

    scores = (
        lax.dot_general(query_all, region_all, contract_last, preferred_element_type=jnp.float32)
        * logit_scale
    )
    row_max = jnp.max(scores, axis=1, keepdims=True)
    log_total = row_max[:, 0] + jnp.log(jnp.sum(jnp.exp(scores - row_max), axis=1))
    columns = lax.broadcasted_iota(jnp.int32, (1, pair_count), 1)
    matched = columns == positive_all[:, None]
    target_score = jnp.sum(jnp.where(matched, scores, jnp.zeros_like(scores)), axis=1)
    mean_loss = jnp.sum(log_total - target_score) / pair_count
    grad_probs = (jnp.exp(scores - log_total[:, None]) - matched.astype(jnp.float32)).astype(
        jnp.bfloat16
    )
    query_grad_all = logit_scale * jnp.dot(grad_probs, region_all, preferred_element_type=jnp.float32)
    query_grad = lax.dynamic_slice(query_grad_all, (me_dp * rows, me_f * width), (rows, width))
    grad_low = lax.dynamic_slice(query_grad_all, (me_dp * rows, 0), (rows, feature_count * width))
    grad_low = grad_low.astype(jnp.bfloat16)
    grad_low_cols = lax.dynamic_slice(query_grad_all, (0, me_f * width), (pair_count, width))
    grad_low_cols = grad_low_cols.astype(jnp.bfloat16)
    probs_cols = lax.dynamic_slice(grad_probs, (0, me_dp * rows), (pair_count, rows))
    query_cols = lax.dynamic_slice(query_all, (0, me_f * width), (pair_count, width))
    region_grad = logit_scale * lax.dot_general(
        probs_cols, query_cols, contract_first, preferred_element_type=jnp.float32
    )

    mean_part = lax.dot_general(
        grad_low, proj_weight, contract_last, preferred_element_type=jnp.float32
    )
    mean_part, pooled_cols = lax.optimization_barrier((mean_part, pooled_cols))
    proj_grad = lax.dot_general(
        pooled_cols, grad_low_cols, contract_first, preferred_element_type=jnp.float32
    )
    mean_grad = lax.all_gather(mean_part, "fsdp", axis=1, tiled=True)
    pool_grad = mean_grad / counts[:, None]
    normed_grad = lax.dot_general(
        member.astype(jnp.float32),
        pool_grad,
        contract_first,
        precision=lax.Precision.HIGHEST,
        preferred_element_type=jnp.float32,
    )
    gain_part = jnp.sum(normed_grad * states * inv_rms, axis=0)
    scaled = gain * normed_grad
    inner = jnp.mean(scaled * states, axis=1, keepdims=True)
    hidden_grad = (inv_rms * scaled - states * inv_rms**3 * inner).astype(jnp.bfloat16)
    gain_grad = sum_blocks(jnp.sum(gather_grouped(gain_part, "dp", CORES), axis=0), "fsdp")
    return (mean_loss, query_grad, region_grad, hidden_grad, gain_grad, proj_grad)


SMALL_PAIRS = 1024
CORES = 2


def local(query_cache, region_cache, positive, hidden_states, segment_ids, norm_gain, proj_weight):
    pair_count = query_cache.shape[0] * lax.axis_size("dp")
    args = (query_cache, region_cache, positive, hidden_states, segment_ids, norm_gain, proj_weight)
    if pair_count <= SMALL_PAIRS:
        return local_small(*args)
    return local_sharded(*args)


def solution(mesh):
    in_specs = (
        P("dp", "fsdp"),
        P("dp", "fsdp"),
        P("dp"),
        P(("dp", "fsdp"), None),
        P("dp", "fsdp"),
        P(),
        P("fsdp", None),
    )
    out_specs = (
        P(),
        P("dp", "fsdp"),
        P("dp", "fsdp"),
        P(("dp", "fsdp"), None),
        P(),
        P("dp", "fsdp"),
    )
    return jax.shard_map(local, mesh=mesh, in_specs=in_specs, out_specs=out_specs, check_vma=False)
```

```python
import jax
import jax.numpy as jnp
from jax import lax
from jax.sharding import PartitionSpec as P

E = 1024


EPS = 1e-05


def local_sharded(query_cache, region_cache, positive, hidden_states, segment_ids, norm_gain, proj_weight):
    row_count = query_cache.shape[0]
    data_count = lax.axis_size("dp")
    pair_count = row_count * data_count
    logit_scale = float(E) ** (-0.5)
    contract_last = (((1,), (1,)), ((), ()))
    contract_first = (((0,), (0,)), ((), ()))
    region_all, query_all = (
        lax.all_gather(region_cache, "dp", axis=0, tiled=True),
        lax.all_gather(query_cache, "dp", axis=0, tiled=True),
    )
    partial_value = lax.dot_general(
        query_cache, region_all, contract_last, preferred_element_type=jnp.float32
    )
    scores = lax.psum(partial_value, "fsdp") * logit_scale
    row_max = jnp.max(scores, axis=1, keepdims=True)
    log_total = row_max[:, 0] + jnp.log(jnp.sum(jnp.exp(scores - row_max), axis=1))
    columns = lax.broadcasted_iota(jnp.int32, (1, pair_count), 1)
    matched = columns == positive[:, None]
    target_score = jnp.sum(jnp.where(matched, scores, jnp.zeros_like(scores)), axis=1)
    loss_local = jnp.sum(log_total - target_score)
    grad_probs = (jnp.exp(scores - log_total[:, None]) - matched.astype(jnp.float32)).astype(
        jnp.bfloat16
    )
    query_grad = logit_scale * jnp.dot(grad_probs, region_all, preferred_element_type=jnp.float32)
    totals_all, targets_all = (
        lax.all_gather(log_total, "dp", axis=0, tiled=True),
        lax.all_gather(positive.astype(jnp.float32), "dp", axis=0, tiled=True),
    )
    partial_t = lax.dot_general(
        region_cache, query_all, contract_last, preferred_element_type=jnp.float32
    )
    scores_t = lax.psum(partial_t, "fsdp") * logit_scale
    own_rows = (
        lax.axis_index("dp") * row_count + lax.broadcasted_iota(jnp.int32, (row_count, 1), 0)
    ).astype(jnp.float32)
    matched_t = targets_all[None, :] == own_rows
    probs_t = (jnp.exp(scores_t - totals_all[None, :]) - matched_t.astype(jnp.float32)).astype(
        jnp.bfloat16
    )
    region_grad = logit_scale * jnp.dot(probs_t, query_all, preferred_element_type=jnp.float32)
    gain = norm_gain.astype(jnp.float32)
    states = hidden_states.astype(jnp.float32)
    inv_rms = lax.rsqrt(jnp.mean(states * states, axis=1, keepdims=True) + EPS)
    normed = (states * inv_rms * gain).astype(jnp.bfloat16)
    labels = lax.broadcasted_iota(jnp.int32, (row_count, 1), 0)
    member = segment_ids[0][None, :] == labels
    pooled_part = jnp.dot(member.astype(jnp.bfloat16), normed, preferred_element_type=jnp.float32)
    counts_part = jnp.sum(member.astype(jnp.float32), axis=1)
    pooled, counts = lax.psum((pooled_part, counts_part), "fsdp")
    mean_pooled = (pooled / counts[:, None]).astype(jnp.bfloat16)
    grad_low = query_grad.astype(jnp.bfloat16)
    grad_full = lax.all_gather(grad_low, "fsdp", axis=1, tiled=True)
    mean_part = lax.dot_general(
        grad_full, proj_weight, contract_last, preferred_element_type=jnp.float32
    )
    mean_grad = lax.all_gather(mean_part, "fsdp", axis=1, tiled=True)
    pool_grad = mean_grad / counts[:, None]
    normed_grad = lax.dot_general(
        member.astype(jnp.float32),
        pool_grad,
        contract_first,
        precision=lax.Precision.HIGHEST,
        preferred_element_type=jnp.float32,
    )
    gain_part = jnp.sum(normed_grad * states * inv_rms, axis=0)
    scaled = gain * normed_grad
    inner = jnp.mean(scaled * states, axis=1, keepdims=True)
    hidden_grad = (inv_rms * scaled - states * inv_rms**3 * inner).astype(jnp.bfloat16)
    proj_grad = lax.psum_scatter(
        lax.dot_general(mean_pooled, grad_low, contract_first, preferred_element_type=jnp.float32),
        "dp",
        scatter_dimension=0,
        tiled=True,
    )
    loss_total = lax.psum(loss_local, "dp")
    gain_grad = lax.psum(gain_part, ("dp", "fsdp"))
    mean_loss = loss_total / pair_count
    return (mean_loss, query_grad, region_grad, hidden_grad, gain_grad, proj_grad)


def gather_blocks(x, axis):
    n = lax.axis_size(axis)
    copies = [x] + [
        lax.ppermute(x, axis, [(i, (i + s) % n) for i in range(n)]) for s in range(1, n)
    ]
    stack = jnp.stack(copies)
    order = (lax.axis_index(axis) - jnp.arange(n)) % n
    return jnp.take(stack, order, axis=0)


def sum_blocks(x, axis):
    return jnp.sum(gather_blocks(x, axis), axis=0)


def scatter_sum(chunks, axis):
    n = lax.axis_size(axis)
    me = lax.axis_index(axis)
    copies = [lax.dynamic_index_in_dim(chunks, me, axis=0, keepdims=False)]
    for s in range(1, n):
        piece = lax.dynamic_index_in_dim(chunks, (me + s) % n, axis=0, keepdims=False)
        copies.append(lax.ppermute(piece, axis, [(i, (i + s) % n) for i in range(n)]))
    order = (me - jnp.arange(n)) % n
    return jnp.sum(jnp.take(jnp.stack(copies), order, axis=0), axis=0)


def spread_with_sum(total, pieces, axis):
    n = lax.axis_size(axis)
    me = lax.axis_index(axis)
    size = total.shape[0]
    sums = [total]
    got = [lax.dynamic_index_in_dim(pieces, me, axis=0, keepdims=False)]
    for s in range(1, n):
        piece = lax.dynamic_index_in_dim(pieces, (me + s) % n, axis=0, keepdims=False)
        payload = jnp.concatenate([total, piece.reshape(-1)])
        arrived = lax.ppermute(payload, axis, [(i, (i + s) % n) for i in range(n)])
        sums.append(arrived[:size])
        got.append(arrived[size:].reshape(piece.shape))
    order = (me - jnp.arange(n)) % n
    return (
        jnp.sum(jnp.take(jnp.stack(sums), order, axis=0), axis=0),
        jnp.take(jnp.stack(got), order, axis=0),
    )


def local_small(query_cache, region_cache, positive, hidden_states, segment_ids, norm_gain, proj_weight):
    rows, width = query_cache.shape
    data_count = lax.axis_size("dp")
    feature_count = lax.axis_size("fsdp")
    pair_count = rows * data_count
    tokens = segment_ids.shape[1]
    model_width = hidden_states.shape[1]
    logit_scale = float(E) ** (-0.5)
    contract_last = (((1,), (1,)), ((), ()))
    contract_first = (((0,), (0,)), ((), ()))
    me_dp = lax.axis_index("dp")
    me_f = lax.axis_index("fsdp")

    extra = jnp.concatenate(
        [positive // 64, positive % 64, segment_ids[0]]
    ).astype(jnp.float32)
    extra_rows = -(-extra.shape[0] // width)
    extra = jnp.pad(extra, (0, extra_rows * width - extra.shape[0]))
    packed = jnp.concatenate(
        [query_cache, region_cache, extra.reshape(extra_rows, width).astype(jnp.bfloat16)], axis=0
    )
    group_blocks = gather_blocks(packed, "fsdp")
    group_side = group_blocks[:, 2 * rows :].reshape(feature_count, extra_rows * width)
    group_ids = group_side[:, 2 * rows : 2 * rows + tokens].reshape(feature_count * tokens)
    group_ids = group_ids.astype(jnp.int32)

    gain = norm_gain.astype(jnp.float32)
    states = hidden_states.astype(jnp.float32)
    inv_rms = lax.rsqrt(jnp.mean(states * states, axis=1, keepdims=True) + EPS)
    normed = (states * inv_rms * gain).astype(jnp.bfloat16)
    labels = lax.broadcasted_iota(jnp.int32, (rows, 1), 0)
    member = segment_ids[0][None, :] == labels
    pooled_part = jnp.dot(member.astype(jnp.bfloat16), normed, preferred_element_type=jnp.float32)
    counts = jnp.sum((group_ids[None, :] == labels).astype(jnp.float32), axis=1)
    chunk = model_width // feature_count
    pooled_chunk = scatter_sum(
        pooled_part.reshape(rows, feature_count, chunk).transpose(1, 0, 2), "fsdp"
    )
    mean_chunk = (pooled_chunk / counts[:, None]).astype(jnp.bfloat16)
    mean_pooled = gather_blocks(mean_chunk, "fsdp").transpose(1, 0, 2).reshape(rows, model_width)

    gathered = gather_blocks(group_blocks, "dp")
    mean_pooled, gathered = lax.optimization_barrier((mean_pooled, gathered))
    slice_width = model_width // data_count
    pieces = mean_pooled.reshape(rows, data_count, slice_width).transpose(1, 0, 2)

    query_all = gathered[:, :, :rows].transpose(0, 2, 1, 3).reshape(pair_count, feature_count * width)
    region_all = gathered[:, :, rows : 2 * rows].transpose(0, 2, 1, 3).reshape(
        pair_count, feature_count * width
    )
    side = gathered[:, :, 2 * rows :].reshape(data_count, feature_count, extra_rows * width)
    side = side.astype(jnp.float32)
    positive_all = (side[:, 0, :rows] * 64 + side[:, 0, rows : 2 * rows]).astype(jnp.int32)
    positive_all = positive_all.reshape(pair_count)

    scores = (
        lax.dot_general(query_all, region_all, contract_last, preferred_element_type=jnp.float32)
        * logit_scale
    )
    row_max = jnp.max(scores, axis=1, keepdims=True)
    log_total = row_max[:, 0] + jnp.log(jnp.sum(jnp.exp(scores - row_max), axis=1))
    columns = lax.broadcasted_iota(jnp.int32, (1, pair_count), 1)
    matched = columns == positive_all[:, None]
    target_score = jnp.sum(jnp.where(matched, scores, jnp.zeros_like(scores)), axis=1)
    mean_loss = jnp.sum(log_total - target_score) / pair_count
    grad_probs = (jnp.exp(scores - log_total[:, None]) - matched.astype(jnp.float32)).astype(
        jnp.bfloat16
    )
    query_grad_all = logit_scale * jnp.dot(grad_probs, region_all, preferred_element_type=jnp.float32)
    query_grad = lax.dynamic_slice(query_grad_all, (me_dp * rows, me_f * width), (rows, width))
    grad_low = lax.dynamic_slice(query_grad_all, (me_dp * rows, 0), (rows, feature_count * width))
    grad_low = grad_low.astype(jnp.bfloat16)
    grad_low_cols = lax.dynamic_slice(query_grad_all, (0, me_f * width), (pair_count, width))
    grad_low_cols = grad_low_cols.astype(jnp.bfloat16)
    probs_cols = lax.dynamic_slice(grad_probs, (0, me_dp * rows), (pair_count, rows))
    query_cols = lax.dynamic_slice(query_all, (0, me_f * width), (pair_count, width))
    region_grad = logit_scale * lax.dot_general(
        probs_cols, query_cols, contract_first, preferred_element_type=jnp.float32
    )

    mean_part = lax.dot_general(
        grad_low, proj_weight, contract_last, preferred_element_type=jnp.float32
    )
    mean_grad = lax.all_gather(mean_part, "fsdp", axis=1, tiled=True)
    pool_grad = mean_grad / counts[:, None]
    normed_grad = lax.dot_general(
        member.astype(jnp.float32),
        pool_grad,
        contract_first,
        precision=lax.Precision.HIGHEST,
        preferred_element_type=jnp.float32,
    )
    gain_part = jnp.sum(normed_grad * states * inv_rms, axis=0)
    scaled = gain * normed_grad
    inner = jnp.mean(scaled * states, axis=1, keepdims=True)
    hidden_grad = (inv_rms * scaled - states * inv_rms**3 * inner).astype(jnp.bfloat16)
    gain_dp, pieces = spread_with_sum(gain_part, pieces.astype(jnp.float32), "dp")
    gain_grad = sum_blocks(gain_dp, "fsdp")
    pooled_cols = pieces.reshape(pair_count, slice_width).astype(jnp.bfloat16)
    proj_grad = lax.dot_general(
        pooled_cols, grad_low_cols, contract_first, preferred_element_type=jnp.float32
    )
    return (mean_loss, query_grad, region_grad, hidden_grad, gain_grad, proj_grad)


SMALL_PAIRS = 1024


def local(query_cache, region_cache, positive, hidden_states, segment_ids, norm_gain, proj_weight):
    pair_count = query_cache.shape[0] * lax.axis_size("dp")
    args = (query_cache, region_cache, positive, hidden_states, segment_ids, norm_gain, proj_weight)
    if pair_count <= SMALL_PAIRS:
        return local_small(*args)
    return local_sharded(*args)


def solution(mesh):
    in_specs = (
        P("dp", "fsdp"),
        P("dp", "fsdp"),
        P("dp"),
        P(("dp", "fsdp"), None),
        P("dp", "fsdp"),
        P(),
        P("fsdp", None),
    )
    out_specs = (
        P(),
        P("dp", "fsdp"),
        P("dp", "fsdp"),
        P(("dp", "fsdp"), None),
        P(),
        P("dp", "fsdp"),
    )
    return jax.shard_map(local, mesh=mesh, in_specs=in_specs, out_specs=out_specs, check_vma=False)
```

```python
import jax
import jax.numpy as jnp
from jax import lax
from jax.sharding import PartitionSpec as P

E = 1024


EPS = 1e-05


def local_sharded(query_cache, region_cache, positive, hidden_states, segment_ids, norm_gain, proj_weight):
    row_count = query_cache.shape[0]
    data_count = lax.axis_size("dp")
    pair_count = row_count * data_count
    logit_scale = float(E) ** (-0.5)
    contract_last = (((1,), (1,)), ((), ()))
    contract_first = (((0,), (0,)), ((), ()))
    region_all, query_all = (
        lax.all_gather(region_cache, "dp", axis=0, tiled=True),
        lax.all_gather(query_cache, "dp", axis=0, tiled=True),
    )
    partial_value = lax.dot_general(
        query_cache, region_all, contract_last, preferred_element_type=jnp.float32
    )
    scores = lax.psum(partial_value, "fsdp") * logit_scale
    row_max = jnp.max(scores, axis=1, keepdims=True)
    log_total = row_max[:, 0] + jnp.log(jnp.sum(jnp.exp(scores - row_max), axis=1))
    columns = lax.broadcasted_iota(jnp.int32, (1, pair_count), 1)
    matched = columns == positive[:, None]
    target_score = jnp.sum(jnp.where(matched, scores, jnp.zeros_like(scores)), axis=1)
    loss_local = jnp.sum(log_total - target_score)
    grad_probs = (jnp.exp(scores - log_total[:, None]) - matched.astype(jnp.float32)).astype(
        jnp.bfloat16
    )
    query_grad = logit_scale * jnp.dot(grad_probs, region_all, preferred_element_type=jnp.float32)
    totals_all, targets_all = (
        lax.all_gather(log_total, "dp", axis=0, tiled=True),
        lax.all_gather(positive.astype(jnp.float32), "dp", axis=0, tiled=True),
    )
    partial_t = lax.dot_general(
        region_cache, query_all, contract_last, preferred_element_type=jnp.float32
    )
    scores_t = lax.psum(partial_t, "fsdp") * logit_scale
    own_rows = (
        lax.axis_index("dp") * row_count + lax.broadcasted_iota(jnp.int32, (row_count, 1), 0)
    ).astype(jnp.float32)
    matched_t = targets_all[None, :] == own_rows
    probs_t = (jnp.exp(scores_t - totals_all[None, :]) - matched_t.astype(jnp.float32)).astype(
        jnp.bfloat16
    )
    region_grad = logit_scale * jnp.dot(probs_t, query_all, preferred_element_type=jnp.float32)
    gain = norm_gain.astype(jnp.float32)
    states = hidden_states.astype(jnp.float32)
    inv_rms = lax.rsqrt(jnp.mean(states * states, axis=1, keepdims=True) + EPS)
    normed = (states * inv_rms * gain).astype(jnp.bfloat16)
    labels = lax.broadcasted_iota(jnp.int32, (row_count, 1), 0)
    member = segment_ids[0][None, :] == labels
    pooled_part = jnp.dot(member.astype(jnp.bfloat16), normed, preferred_element_type=jnp.float32)
    counts_part = jnp.sum(member.astype(jnp.float32), axis=1)
    pooled, counts = lax.psum((pooled_part, counts_part), "fsdp")
    mean_pooled = (pooled / counts[:, None]).astype(jnp.bfloat16)
    grad_low = query_grad.astype(jnp.bfloat16)
    grad_full = lax.all_gather(grad_low, "fsdp", axis=1, tiled=True)
    mean_part = lax.dot_general(
        grad_full, proj_weight, contract_last, preferred_element_type=jnp.float32
    )
    mean_grad = lax.all_gather(mean_part, "fsdp", axis=1, tiled=True)
    pool_grad = mean_grad / counts[:, None]
    normed_grad = lax.dot_general(
        member.astype(jnp.float32),
        pool_grad,
        contract_first,
        precision=lax.Precision.HIGHEST,
        preferred_element_type=jnp.float32,
    )
    gain_part = jnp.sum(normed_grad * states * inv_rms, axis=0)
    scaled = gain * normed_grad
    inner = jnp.mean(scaled * states, axis=1, keepdims=True)
    hidden_grad = (inv_rms * scaled - states * inv_rms**3 * inner).astype(jnp.bfloat16)
    proj_grad = lax.psum_scatter(
        lax.dot_general(mean_pooled, grad_low, contract_first, preferred_element_type=jnp.float32),
        "dp",
        scatter_dimension=0,
        tiled=True,
    )
    loss_total = lax.psum(loss_local, "dp")
    gain_grad = lax.psum(gain_part, ("dp", "fsdp"))
    mean_loss = loss_total / pair_count
    return (mean_loss, query_grad, region_grad, hidden_grad, gain_grad, proj_grad)


def arrange(copies, me):
    n = len(copies)
    source = ((me - jnp.arange(n)) % n).reshape((n,) + (1,) * copies[0].ndim)
    out = jnp.broadcast_to(copies[0][None], (n,) + copies[0].shape)
    for s in range(1, n):
        out = jnp.where(source == s, copies[s][None], out)
    return out


def gather_blocks(x, axis):
    n = lax.axis_size(axis)
    copies = [x] + [
        lax.ppermute(x, axis, [(i, (i + s) % n) for i in range(n)]) for s in range(1, n)
    ]
    return arrange(copies, lax.axis_index(axis))


def sum_blocks(x, axis):
    return jnp.sum(gather_blocks(x, axis), axis=0)


def scatter_sum(chunks, axis):
    n = lax.axis_size(axis)
    me = lax.axis_index(axis)
    copies = [lax.dynamic_index_in_dim(chunks, me, axis=0, keepdims=False)]
    for s in range(1, n):
        piece = lax.dynamic_index_in_dim(chunks, (me + s) % n, axis=0, keepdims=False)
        copies.append(lax.ppermute(piece, axis, [(i, (i + s) % n) for i in range(n)]))
    return jnp.sum(arrange(copies, me), axis=0)


def spread_with_sum(total, pieces, axis):
    n = lax.axis_size(axis)
    me = lax.axis_index(axis)
    size = total.shape[0]
    sums = [total]
    got = [lax.dynamic_index_in_dim(pieces, me, axis=0, keepdims=False)]
    for s in range(1, n):
        piece = lax.dynamic_index_in_dim(pieces, (me + s) % n, axis=0, keepdims=False)
        payload = jnp.concatenate([total, piece.reshape(-1)])
        arrived = lax.ppermute(payload, axis, [(i, (i + s) % n) for i in range(n)])
        sums.append(arrived[:size])
        got.append(arrived[size:].reshape(piece.shape))
    return jnp.sum(arrange(sums, me), axis=0), arrange(got, me)


def local_small(query_cache, region_cache, positive, hidden_states, segment_ids, norm_gain, proj_weight):
    rows, width = query_cache.shape
    data_count = lax.axis_size("dp")
    feature_count = lax.axis_size("fsdp")
    pair_count = rows * data_count
    tokens = segment_ids.shape[1]
    model_width = hidden_states.shape[1]
    logit_scale = float(E) ** (-0.5)
    contract_last = (((1,), (1,)), ((), ()))
    contract_first = (((0,), (0,)), ((), ()))
    me_dp = lax.axis_index("dp")
    me_f = lax.axis_index("fsdp")

    extra = jnp.concatenate(
        [positive // 64, positive % 64, segment_ids[0]]
    ).astype(jnp.float32)
    extra_rows = -(-extra.shape[0] // width)
    extra = jnp.pad(extra, (0, extra_rows * width - extra.shape[0]))
    packed = jnp.concatenate(
        [query_cache, region_cache, extra.reshape(extra_rows, width).astype(jnp.bfloat16)], axis=0
    )
    group_blocks = gather_blocks(packed, "fsdp")
    group_side = group_blocks[:, 2 * rows :].reshape(feature_count, extra_rows * width)
    group_ids = group_side[:, 2 * rows : 2 * rows + tokens].reshape(feature_count * tokens)
    group_ids = group_ids.astype(jnp.int32)

    gain = norm_gain.astype(jnp.float32)
    states = hidden_states.astype(jnp.float32)
    inv_rms = lax.rsqrt(jnp.mean(states * states, axis=1, keepdims=True) + EPS)
    normed = (states * inv_rms * gain).astype(jnp.bfloat16)
    labels = lax.broadcasted_iota(jnp.int32, (rows, 1), 0)
    member = segment_ids[0][None, :] == labels
    pooled_part = jnp.dot(member.astype(jnp.bfloat16), normed, preferred_element_type=jnp.float32)
    counts = jnp.sum((group_ids[None, :] == labels).astype(jnp.float32), axis=1)
    chunk = model_width // feature_count
    pooled_chunk = scatter_sum(
        pooled_part.reshape(rows, feature_count, chunk).transpose(1, 0, 2), "fsdp"
    )
    mean_chunk = (pooled_chunk / counts[:, None]).astype(jnp.bfloat16)
    mean_pooled = gather_blocks(mean_chunk, "fsdp").transpose(1, 0, 2).reshape(rows, model_width)

    gathered = gather_blocks(group_blocks, "dp")
    mean_pooled, gathered = lax.optimization_barrier((mean_pooled, gathered))
    slice_width = model_width // data_count
    pieces = mean_pooled.reshape(rows, data_count, slice_width).transpose(1, 0, 2)

    query_all = gathered[:, :, :rows].transpose(0, 2, 1, 3).reshape(pair_count, feature_count * width)
    region_all = gathered[:, :, rows : 2 * rows].transpose(0, 2, 1, 3).reshape(
        pair_count, feature_count * width
    )
    side = gathered[:, :, 2 * rows :].reshape(data_count, feature_count, extra_rows * width)
    side = side.astype(jnp.float32)
    positive_all = (side[:, 0, :rows] * 64 + side[:, 0, rows : 2 * rows]).astype(jnp.int32)
    positive_all = positive_all.reshape(pair_count)

    scores = (
        lax.dot_general(query_all, region_all, contract_last, preferred_element_type=jnp.float32)
        * logit_scale
    )
    row_max = jnp.max(scores, axis=1, keepdims=True)
    log_total = row_max[:, 0] + jnp.log(jnp.sum(jnp.exp(scores - row_max), axis=1))
    columns = lax.broadcasted_iota(jnp.int32, (1, pair_count), 1)
    matched = columns == positive_all[:, None]
    target_score = jnp.sum(jnp.where(matched, scores, jnp.zeros_like(scores)), axis=1)
    mean_loss = jnp.sum(log_total - target_score) / pair_count
    grad_probs = (jnp.exp(scores - log_total[:, None]) - matched.astype(jnp.float32)).astype(
        jnp.bfloat16
    )
    query_grad_all = logit_scale * jnp.dot(grad_probs, region_all, preferred_element_type=jnp.float32)
    query_grad = lax.dynamic_slice(query_grad_all, (me_dp * rows, me_f * width), (rows, width))
    grad_low = lax.dynamic_slice(query_grad_all, (me_dp * rows, 0), (rows, feature_count * width))
    grad_low = grad_low.astype(jnp.bfloat16)
    grad_low_cols = lax.dynamic_slice(query_grad_all, (0, me_f * width), (pair_count, width))
    grad_low_cols = grad_low_cols.astype(jnp.bfloat16)
    probs_cols = lax.dynamic_slice(grad_probs, (0, me_dp * rows), (pair_count, rows))
    query_cols = lax.dynamic_slice(query_all, (0, me_f * width), (pair_count, width))
    region_grad = logit_scale * lax.dot_general(
        probs_cols, query_cols, contract_first, preferred_element_type=jnp.float32
    )

    mean_part = lax.dot_general(
        grad_low, proj_weight, contract_last, preferred_element_type=jnp.float32
    )
    mean_grad = lax.all_gather(mean_part, "fsdp", axis=1, tiled=True)
    pool_grad = mean_grad / counts[:, None]
    normed_grad = lax.dot_general(
        member.astype(jnp.float32),
        pool_grad,
        contract_first,
        precision=lax.Precision.HIGHEST,
        preferred_element_type=jnp.float32,
    )
    gain_part = jnp.sum(normed_grad * states * inv_rms, axis=0)
    scaled = gain * normed_grad
    inner = jnp.mean(scaled * states, axis=1, keepdims=True)
    hidden_grad = (inv_rms * scaled - states * inv_rms**3 * inner).astype(jnp.bfloat16)
    gain_dp, pieces = spread_with_sum(gain_part, pieces.astype(jnp.float32), "dp")
    gain_grad = sum_blocks(gain_dp, "fsdp")
    pooled_cols = pieces.reshape(pair_count, slice_width).astype(jnp.bfloat16)
    proj_grad = lax.dot_general(
        pooled_cols, grad_low_cols, contract_first, preferred_element_type=jnp.float32
    )
    return (mean_loss, query_grad, region_grad, hidden_grad, gain_grad, proj_grad)


SMALL_PAIRS = 1024


def local(query_cache, region_cache, positive, hidden_states, segment_ids, norm_gain, proj_weight):
    pair_count = query_cache.shape[0] * lax.axis_size("dp")
    args = (query_cache, region_cache, positive, hidden_states, segment_ids, norm_gain, proj_weight)
    if pair_count <= SMALL_PAIRS:
        return local_small(*args)
    return local_sharded(*args)


def solution(mesh):
    in_specs = (
        P("dp", "fsdp"),
        P("dp", "fsdp"),
        P("dp"),
        P(("dp", "fsdp"), None),
        P("dp", "fsdp"),
        P(),
        P("fsdp", None),
    )
    out_specs = (
        P(),
        P("dp", "fsdp"),
        P("dp", "fsdp"),
        P(("dp", "fsdp"), None),
        P(),
        P("dp", "fsdp"),
    )
    return jax.shard_map(local, mesh=mesh, in_specs=in_specs, out_specs=out_specs, check_vma=False)
```

```python
import jax
import jax.numpy as jnp
from jax import lax
from jax.sharding import PartitionSpec as P

E = 1024


EPS = 1e-05


def local_sharded(query_cache, region_cache, positive, hidden_states, segment_ids, norm_gain, proj_weight):
    row_count = query_cache.shape[0]
    data_count = lax.axis_size("dp")
    pair_count = row_count * data_count
    logit_scale = float(E) ** (-0.5)
    contract_last = (((1,), (1,)), ((), ()))
    contract_first = (((0,), (0,)), ((), ()))
    region_all, query_all = (
        lax.all_gather(region_cache, "dp", axis=0, tiled=True),
        lax.all_gather(query_cache, "dp", axis=0, tiled=True),
    )
    partial_value = lax.dot_general(
        query_cache, region_all, contract_last, preferred_element_type=jnp.float32
    )
    scores = lax.psum(partial_value, "fsdp") * logit_scale
    row_max = jnp.max(scores, axis=1, keepdims=True)
    log_total = row_max[:, 0] + jnp.log(jnp.sum(jnp.exp(scores - row_max), axis=1))
    columns = lax.broadcasted_iota(jnp.int32, (1, pair_count), 1)
    matched = columns == positive[:, None]
    target_score = jnp.sum(jnp.where(matched, scores, jnp.zeros_like(scores)), axis=1)
    loss_local = jnp.sum(log_total - target_score)
    grad_probs = (jnp.exp(scores - log_total[:, None]) - matched.astype(jnp.float32)).astype(
        jnp.bfloat16
    )
    query_grad = logit_scale * jnp.dot(grad_probs, region_all, preferred_element_type=jnp.float32)
    totals_all, targets_all = (
        lax.all_gather(log_total, "dp", axis=0, tiled=True),
        lax.all_gather(positive.astype(jnp.float32), "dp", axis=0, tiled=True),
    )
    partial_t = lax.dot_general(
        region_cache, query_all, contract_last, preferred_element_type=jnp.float32
    )
    scores_t = lax.psum(partial_t, "fsdp") * logit_scale
    own_rows = (
        lax.axis_index("dp") * row_count + lax.broadcasted_iota(jnp.int32, (row_count, 1), 0)
    ).astype(jnp.float32)
    matched_t = targets_all[None, :] == own_rows
    probs_t = (jnp.exp(scores_t - totals_all[None, :]) - matched_t.astype(jnp.float32)).astype(
        jnp.bfloat16
    )
    region_grad = logit_scale * jnp.dot(probs_t, query_all, preferred_element_type=jnp.float32)
    gain = norm_gain.astype(jnp.float32)
    states = hidden_states.astype(jnp.float32)
    inv_rms = lax.rsqrt(jnp.mean(states * states, axis=1, keepdims=True) + EPS)
    normed = (states * inv_rms * gain).astype(jnp.bfloat16)
    labels = lax.broadcasted_iota(jnp.int32, (row_count, 1), 0)
    member = segment_ids[0][None, :] == labels
    pooled_part = jnp.dot(member.astype(jnp.bfloat16), normed, preferred_element_type=jnp.float32)
    counts_part = jnp.sum(member.astype(jnp.float32), axis=1)
    pooled, counts = lax.psum((pooled_part, counts_part), "fsdp")
    mean_pooled = (pooled / counts[:, None]).astype(jnp.bfloat16)
    grad_low = query_grad.astype(jnp.bfloat16)
    grad_full = lax.all_gather(grad_low, "fsdp", axis=1, tiled=True)
    mean_part = lax.dot_general(
        grad_full, proj_weight, contract_last, preferred_element_type=jnp.float32
    )
    mean_grad = lax.all_gather(mean_part, "fsdp", axis=1, tiled=True)
    pool_grad = mean_grad / counts[:, None]
    normed_grad = lax.dot_general(
        member.astype(jnp.float32),
        pool_grad,
        contract_first,
        precision=lax.Precision.HIGHEST,
        preferred_element_type=jnp.float32,
    )
    gain_part = jnp.sum(normed_grad * states * inv_rms, axis=0)
    scaled = gain * normed_grad
    inner = jnp.mean(scaled * states, axis=1, keepdims=True)
    hidden_grad = (inv_rms * scaled - states * inv_rms**3 * inner).astype(jnp.bfloat16)
    proj_grad = lax.psum_scatter(
        lax.dot_general(mean_pooled, grad_low, contract_first, preferred_element_type=jnp.float32),
        "dp",
        scatter_dimension=0,
        tiled=True,
    )
    loss_total = lax.psum(loss_local, "dp")
    gain_grad = lax.psum(gain_part, ("dp", "fsdp"))
    mean_loss = loss_total / pair_count
    return (mean_loss, query_grad, region_grad, hidden_grad, gain_grad, proj_grad)


def arrange(copies, me):
    n = len(copies)
    source = ((me - jnp.arange(n)) % n).reshape((n,) + (1,) * copies[0].ndim)
    out = jnp.broadcast_to(copies[0][None], (n,) + copies[0].shape)
    for s in range(1, n):
        out = jnp.where(source == s, copies[s][None], out)
    return out


def gather_blocks(x, axis):
    n = lax.axis_size(axis)
    copies = [x] + [
        lax.ppermute(x, axis, [(i, (i + s) % n) for i in range(n)]) for s in range(1, n)
    ]
    return arrange(copies, lax.axis_index(axis))


def sum_blocks(x, axis):
    return jnp.sum(gather_blocks(x, axis), axis=0)


def scatter_sum(chunks, axis):
    n = lax.axis_size(axis)
    me = lax.axis_index(axis)
    copies = [lax.dynamic_index_in_dim(chunks, me, axis=0, keepdims=False)]
    for s in range(1, n):
        piece = lax.dynamic_index_in_dim(chunks, (me + s) % n, axis=0, keepdims=False)
        copies.append(lax.ppermute(piece, axis, [(i, (i + s) % n) for i in range(n)]))
    return jnp.sum(arrange(copies, me), axis=0)


def spread_with_sum(total, pieces, axis):
    n = lax.axis_size(axis)
    me = lax.axis_index(axis)
    size = total.shape[0]
    sums = [total]
    got = [lax.dynamic_index_in_dim(pieces, me, axis=0, keepdims=False)]
    for s in range(1, n):
        piece = lax.dynamic_index_in_dim(pieces, (me + s) % n, axis=0, keepdims=False)
        payload = jnp.concatenate([total, piece.reshape(-1)])
        arrived = lax.ppermute(payload, axis, [(i, (i + s) % n) for i in range(n)])
        sums.append(arrived[:size])
        got.append(arrived[size:].reshape(piece.shape))
    return jnp.sum(arrange(sums, me), axis=0), arrange(got, me)


def local_small(query_cache, region_cache, positive, hidden_states, segment_ids, norm_gain, proj_weight):
    rows, width = query_cache.shape
    data_count = lax.axis_size("dp")
    feature_count = lax.axis_size("fsdp")
    pair_count = rows * data_count
    tokens = segment_ids.shape[1]
    model_width = hidden_states.shape[1]
    logit_scale = float(E) ** (-0.5)
    contract_last = (((1,), (1,)), ((), ()))
    contract_first = (((0,), (0,)), ((), ()))
    me_dp = lax.axis_index("dp")
    me_f = lax.axis_index("fsdp")

    extra = jnp.concatenate(
        [positive // 64, positive % 64, segment_ids[0]]
    ).astype(jnp.float32)
    extra_rows = -(-extra.shape[0] // width)
    extra = jnp.pad(extra, (0, extra_rows * width - extra.shape[0]))
    packed = jnp.concatenate(
        [query_cache, region_cache, extra.reshape(extra_rows, width).astype(jnp.bfloat16)], axis=0
    )
    group_blocks = gather_blocks(packed, "fsdp")
    group_side = group_blocks[:, 2 * rows :].reshape(feature_count, extra_rows * width)
    group_ids = group_side[:, 2 * rows : 2 * rows + tokens].reshape(feature_count * tokens)
    group_ids = group_ids.astype(jnp.int32)

    gain = norm_gain.astype(jnp.float32)
    states = hidden_states.astype(jnp.float32)
    inv_rms = lax.rsqrt(jnp.mean(states * states, axis=1, keepdims=True) + EPS)
    normed = (states * inv_rms * gain).astype(jnp.bfloat16)
    labels = lax.broadcasted_iota(jnp.int32, (rows, 1), 0)
    member = segment_ids[0][None, :] == labels
    pooled_part = jnp.dot(member.astype(jnp.bfloat16), normed, preferred_element_type=jnp.float32)
    counts = jnp.sum((group_ids[None, :] == labels).astype(jnp.float32), axis=1)
    chunk = model_width // feature_count
    pooled_chunk = scatter_sum(
        pooled_part.reshape(rows, feature_count, chunk).transpose(1, 0, 2), "fsdp"
    )
    mean_chunk = (pooled_chunk / counts[:, None]).astype(jnp.bfloat16)
    mean_pooled = gather_blocks(mean_chunk, "fsdp").transpose(1, 0, 2).reshape(rows, model_width)

    gathered = gather_blocks(group_blocks, "dp")
    mean_pooled, gathered = lax.optimization_barrier((mean_pooled, gathered))
    slice_width = model_width // data_count
    pieces = mean_pooled.reshape(rows, data_count, slice_width).transpose(1, 0, 2)

    query_all = gathered[:, :, :rows].transpose(0, 2, 1, 3).reshape(pair_count, feature_count * width)
    region_all = gathered[:, :, rows : 2 * rows].transpose(0, 2, 1, 3).reshape(
        pair_count, feature_count * width
    )
    side = gathered[:, :, 2 * rows :].reshape(data_count, feature_count, extra_rows * width)
    side = side.astype(jnp.float32)
    positive_all = (side[:, 0, :rows] * 64 + side[:, 0, rows : 2 * rows]).astype(jnp.int32)
    positive_all = positive_all.reshape(pair_count)

    scores = (
        lax.dot_general(query_all, region_all, contract_last, preferred_element_type=jnp.float32)
        * logit_scale
    )
    row_max = jnp.max(scores, axis=1, keepdims=True)
    log_total = row_max[:, 0] + jnp.log(jnp.sum(jnp.exp(scores - row_max), axis=1))
    columns = lax.broadcasted_iota(jnp.int32, (1, pair_count), 1)
    matched = columns == positive_all[:, None]
    target_score = jnp.sum(jnp.where(matched, scores, jnp.zeros_like(scores)), axis=1)
    mean_loss = jnp.sum(log_total - target_score) / pair_count
    grad_probs = (jnp.exp(scores - log_total[:, None]) - matched.astype(jnp.float32)).astype(
        jnp.bfloat16
    )
    query_grad_all = logit_scale * jnp.dot(grad_probs, region_all, preferred_element_type=jnp.float32)
    query_grad = lax.dynamic_slice(query_grad_all, (me_dp * rows, me_f * width), (rows, width))
    grad_low = lax.dynamic_slice(query_grad_all, (me_dp * rows, 0), (rows, feature_count * width))
    grad_low = grad_low.astype(jnp.bfloat16)
    grad_low_cols = lax.dynamic_slice(query_grad_all, (0, me_f * width), (pair_count, width))
    grad_low_cols = grad_low_cols.astype(jnp.bfloat16)
    probs_cols = lax.dynamic_slice(grad_probs, (0, me_dp * rows), (pair_count, rows))
    query_cols = lax.dynamic_slice(query_all, (0, me_f * width), (pair_count, width))
    region_grad = logit_scale * lax.dot_general(
        probs_cols, query_cols, contract_first, preferred_element_type=jnp.float32
    )

    mean_part = lax.dot_general(
        grad_low, proj_weight, contract_last, preferred_element_type=jnp.float32
    )
    mean_grad = lax.all_gather(mean_part, "fsdp", axis=1, tiled=True)
    pool_grad = mean_grad / counts[:, None]
    normed_grad = lax.dot_general(
        member.astype(jnp.float32),
        pool_grad,
        contract_first,
        precision=lax.Precision.HIGHEST,
        preferred_element_type=jnp.float32,
    )
    gain_part = jnp.sum(normed_grad * states * inv_rms, axis=0)
    scaled = gain * normed_grad
    inner = jnp.mean(scaled * states, axis=1, keepdims=True)
    hidden_grad = (inv_rms * scaled - states * inv_rms**3 * inner).astype(jnp.bfloat16)
    gain_dp, pieces = spread_with_sum(gain_part, pieces.astype(jnp.float32), "dp")
    gain_grad = sum_blocks(gain_dp, "fsdp")
    proj_grad = lax.dot_general(
        pieces.astype(jnp.bfloat16),
        grad_low_cols.reshape(data_count, rows, width),
        (((0, 1), (0, 1)), ((), ())),
        preferred_element_type=jnp.float32,
    )
    return (mean_loss, query_grad, region_grad, hidden_grad, gain_grad, proj_grad)


SMALL_PAIRS = 1024


def local(query_cache, region_cache, positive, hidden_states, segment_ids, norm_gain, proj_weight):
    pair_count = query_cache.shape[0] * lax.axis_size("dp")
    args = (query_cache, region_cache, positive, hidden_states, segment_ids, norm_gain, proj_weight)
    if pair_count <= SMALL_PAIRS:
        return local_small(*args)
    return local_sharded(*args)


def solution(mesh):
    in_specs = (
        P("dp", "fsdp"),
        P("dp", "fsdp"),
        P("dp"),
        P(("dp", "fsdp"), None),
        P("dp", "fsdp"),
        P(),
        P("fsdp", None),
    )
    out_specs = (
        P(),
        P("dp", "fsdp"),
        P("dp", "fsdp"),
        P(("dp", "fsdp"), None),
        P(),
        P("dp", "fsdp"),
    )
    return jax.shard_map(local, mesh=mesh, in_specs=in_specs, out_specs=out_specs, check_vma=False)
```

```python
import jax
import jax.numpy as jnp
from jax import lax
from jax.sharding import PartitionSpec as P

E = 1024


EPS = 1e-05


def local_sharded(query_cache, region_cache, positive, hidden_states, segment_ids, norm_gain, proj_weight):
    row_count = query_cache.shape[0]
    data_count = lax.axis_size("dp")
    pair_count = row_count * data_count
    logit_scale = float(E) ** (-0.5)
    contract_last = (((1,), (1,)), ((), ()))
    contract_first = (((0,), (0,)), ((), ()))
    region_all, query_all = (
        lax.all_gather(region_cache, "dp", axis=0, tiled=True),
        lax.all_gather(query_cache, "dp", axis=0, tiled=True),
    )
    partial_value = lax.dot_general(
        query_cache, region_all, contract_last, preferred_element_type=jnp.float32
    )
    scores = lax.psum(partial_value, "fsdp") * logit_scale
    row_max = jnp.max(scores, axis=1, keepdims=True)
    log_total = row_max[:, 0] + jnp.log(jnp.sum(jnp.exp(scores - row_max), axis=1))
    columns = lax.broadcasted_iota(jnp.int32, (1, pair_count), 1)
    matched = columns == positive[:, None]
    target_score = jnp.sum(jnp.where(matched, scores, jnp.zeros_like(scores)), axis=1)
    loss_local = jnp.sum(log_total - target_score)
    grad_probs = (jnp.exp(scores - log_total[:, None]) - matched.astype(jnp.float32)).astype(
        jnp.bfloat16
    )
    query_grad = logit_scale * jnp.dot(grad_probs, region_all, preferred_element_type=jnp.float32)
    totals_all, targets_all = (
        lax.all_gather(log_total, "dp", axis=0, tiled=True),
        lax.all_gather(positive.astype(jnp.float32), "dp", axis=0, tiled=True),
    )
    partial_t = lax.dot_general(
        region_cache, query_all, contract_last, preferred_element_type=jnp.float32
    )
    scores_t = lax.psum(partial_t, "fsdp") * logit_scale
    own_rows = (
        lax.axis_index("dp") * row_count + lax.broadcasted_iota(jnp.int32, (row_count, 1), 0)
    ).astype(jnp.float32)
    matched_t = targets_all[None, :] == own_rows
    probs_t = (jnp.exp(scores_t - totals_all[None, :]) - matched_t.astype(jnp.float32)).astype(
        jnp.bfloat16
    )
    region_grad = logit_scale * jnp.dot(probs_t, query_all, preferred_element_type=jnp.float32)
    gain = norm_gain.astype(jnp.float32)
    states = hidden_states.astype(jnp.float32)
    inv_rms = lax.rsqrt(jnp.mean(states * states, axis=1, keepdims=True) + EPS)
    normed = (states * inv_rms * gain).astype(jnp.bfloat16)
    labels = lax.broadcasted_iota(jnp.int32, (row_count, 1), 0)
    member = segment_ids[0][None, :] == labels
    pooled_part = jnp.dot(member.astype(jnp.bfloat16), normed, preferred_element_type=jnp.float32)
    counts_part = jnp.sum(member.astype(jnp.float32), axis=1)
    pooled, counts = lax.psum((pooled_part, counts_part), "fsdp")
    mean_pooled = (pooled / counts[:, None]).astype(jnp.bfloat16)
    grad_low = query_grad.astype(jnp.bfloat16)
    grad_full = lax.all_gather(grad_low, "fsdp", axis=1, tiled=True)
    mean_part = lax.dot_general(
        grad_full, proj_weight, contract_last, preferred_element_type=jnp.float32
    )
    mean_grad = lax.all_gather(mean_part, "fsdp", axis=1, tiled=True)
    pool_grad = mean_grad / counts[:, None]
    normed_grad = lax.dot_general(
        member.astype(jnp.float32),
        pool_grad,
        contract_first,
        precision=lax.Precision.HIGHEST,
        preferred_element_type=jnp.float32,
    )
    gain_part = jnp.sum(normed_grad * states * inv_rms, axis=0)
    scaled = gain * normed_grad
    inner = jnp.mean(scaled * states, axis=1, keepdims=True)
    hidden_grad = (inv_rms * scaled - states * inv_rms**3 * inner).astype(jnp.bfloat16)
    proj_grad = lax.psum_scatter(
        lax.dot_general(mean_pooled, grad_low, contract_first, preferred_element_type=jnp.float32),
        "dp",
        scatter_dimension=0,
        tiled=True,
    )
    loss_total = lax.psum(loss_local, "dp")
    gain_grad = lax.psum(gain_part, ("dp", "fsdp"))
    mean_loss = loss_total / pair_count
    return (mean_loss, query_grad, region_grad, hidden_grad, gain_grad, proj_grad)


def arrange(copies, me):
    n = len(copies)
    source = ((me - jnp.arange(n)) % n).reshape((n,) + (1,) * copies[0].ndim)
    out = jnp.broadcast_to(copies[0][None], (n,) + copies[0].shape)
    for s in range(1, n):
        out = jnp.where(source == s, copies[s][None], out)
    return out


def gather_blocks(x, axis):
    n = lax.axis_size(axis)
    copies = [x] + [
        lax.ppermute(x, axis, [(i, (i + s) % n) for i in range(n)]) for s in range(1, n)
    ]
    return arrange(copies, lax.axis_index(axis))


def sum_blocks(x, axis):
    return jnp.sum(gather_blocks(x, axis), axis=0)


def scatter_sum(chunks, axis):
    n = lax.axis_size(axis)
    me = lax.axis_index(axis)
    copies = [lax.dynamic_index_in_dim(chunks, me, axis=0, keepdims=False)]
    for s in range(1, n):
        piece = lax.dynamic_index_in_dim(chunks, (me + s) % n, axis=0, keepdims=False)
        copies.append(lax.ppermute(piece, axis, [(i, (i + s) % n) for i in range(n)]))
    return jnp.sum(arrange(copies, me), axis=0)


def spread_with_sum(total, pieces, axis):
    n = lax.axis_size(axis)
    me = lax.axis_index(axis)
    size = total.shape[0]
    sums = [total]
    got = [lax.dynamic_index_in_dim(pieces, me, axis=0, keepdims=False)]
    for s in range(1, n):
        piece = lax.dynamic_index_in_dim(pieces, (me + s) % n, axis=0, keepdims=False)
        payload = jnp.concatenate([total, piece.reshape(-1)])
        arrived = lax.ppermute(payload, axis, [(i, (i + s) % n) for i in range(n)])
        sums.append(arrived[:size])
        got.append(arrived[size:].reshape(piece.shape))
    return jnp.sum(arrange(sums, me), axis=0), lax.optimization_barrier(arrange(got, me))


def local_small(query_cache, region_cache, positive, hidden_states, segment_ids, norm_gain, proj_weight):
    rows, width = query_cache.shape
    data_count = lax.axis_size("dp")
    feature_count = lax.axis_size("fsdp")
    pair_count = rows * data_count
    tokens = segment_ids.shape[1]
    model_width = hidden_states.shape[1]
    logit_scale = float(E) ** (-0.5)
    contract_last = (((1,), (1,)), ((), ()))
    contract_first = (((0,), (0,)), ((), ()))
    me_dp = lax.axis_index("dp")
    me_f = lax.axis_index("fsdp")

    extra = jnp.concatenate(
        [positive // 64, positive % 64, segment_ids[0]]
    ).astype(jnp.float32)
    extra_rows = -(-extra.shape[0] // width)
    extra = jnp.pad(extra, (0, extra_rows * width - extra.shape[0]))
    packed = jnp.concatenate(
        [query_cache, region_cache, extra.reshape(extra_rows, width).astype(jnp.bfloat16)], axis=0
    )
    group_blocks = gather_blocks(packed, "fsdp")
    group_side = group_blocks[:, 2 * rows :].reshape(feature_count, extra_rows * width)
    group_ids = group_side[:, 2 * rows : 2 * rows + tokens].reshape(feature_count * tokens)
    group_ids = group_ids.astype(jnp.int32)

    gain = norm_gain.astype(jnp.float32)
    states = hidden_states.astype(jnp.float32)
    inv_rms = lax.rsqrt(jnp.mean(states * states, axis=1, keepdims=True) + EPS)
    normed = (states * inv_rms * gain).astype(jnp.bfloat16)
    labels = lax.broadcasted_iota(jnp.int32, (rows, 1), 0)
    member = segment_ids[0][None, :] == labels
    pooled_part = jnp.dot(member.astype(jnp.bfloat16), normed, preferred_element_type=jnp.float32)
    counts = jnp.sum((group_ids[None, :] == labels).astype(jnp.float32), axis=1)
    chunk = model_width // feature_count
    pooled_chunk = scatter_sum(
        pooled_part.reshape(rows, feature_count, chunk).transpose(1, 0, 2), "fsdp"
    )
    mean_chunk = (pooled_chunk / counts[:, None]).astype(jnp.bfloat16)
    mean_pooled = gather_blocks(mean_chunk, "fsdp").transpose(1, 0, 2).reshape(rows, model_width)

    gathered = gather_blocks(group_blocks, "dp")
    mean_pooled, gathered = lax.optimization_barrier((mean_pooled, gathered))
    slice_width = model_width // data_count
    pieces = mean_pooled.reshape(rows, data_count, slice_width).transpose(1, 0, 2)

    query_all = gathered[:, :, :rows].transpose(0, 2, 1, 3).reshape(pair_count, feature_count * width)
    region_all = gathered[:, :, rows : 2 * rows].transpose(0, 2, 1, 3).reshape(
        pair_count, feature_count * width
    )
    side = gathered[:, :, 2 * rows :].reshape(data_count, feature_count, extra_rows * width)
    side = side.astype(jnp.float32)
    positive_all = (side[:, 0, :rows] * 64 + side[:, 0, rows : 2 * rows]).astype(jnp.int32)
    positive_all = positive_all.reshape(pair_count)

    scores = (
        lax.dot_general(query_all, region_all, contract_last, preferred_element_type=jnp.float32)
        * logit_scale
    )
    row_max = jnp.max(scores, axis=1, keepdims=True)
    log_total = row_max[:, 0] + jnp.log(jnp.sum(jnp.exp(scores - row_max), axis=1))
    columns = lax.broadcasted_iota(jnp.int32, (1, pair_count), 1)
    matched = columns == positive_all[:, None]
    target_score = jnp.sum(jnp.where(matched, scores, jnp.zeros_like(scores)), axis=1)
    mean_loss = jnp.sum(log_total - target_score) / pair_count
    grad_probs = (jnp.exp(scores - log_total[:, None]) - matched.astype(jnp.float32)).astype(
        jnp.bfloat16
    )
    query_grad_all = logit_scale * jnp.dot(grad_probs, region_all, preferred_element_type=jnp.float32)
    query_grad = lax.dynamic_slice(query_grad_all, (me_dp * rows, me_f * width), (rows, width))
    grad_low = lax.dynamic_slice(query_grad_all, (me_dp * rows, 0), (rows, feature_count * width))
    grad_low = grad_low.astype(jnp.bfloat16)
    grad_low_cols = lax.dynamic_slice(query_grad_all, (0, me_f * width), (pair_count, width))
    grad_low_cols = grad_low_cols.astype(jnp.bfloat16)
    probs_cols = lax.dynamic_slice(grad_probs, (0, me_dp * rows), (pair_count, rows))
    query_cols = lax.dynamic_slice(query_all, (0, me_f * width), (pair_count, width))
    region_grad = logit_scale * lax.dot_general(
        probs_cols, query_cols, contract_first, preferred_element_type=jnp.float32
    )

    mean_part = lax.dot_general(
        grad_low, proj_weight, contract_last, preferred_element_type=jnp.float32
    )
    mean_grad = lax.all_gather(mean_part, "fsdp", axis=1, tiled=True)
    pool_grad = mean_grad / counts[:, None]
    normed_grad = lax.dot_general(
        member.astype(jnp.float32),
        pool_grad,
        contract_first,
        precision=lax.Precision.HIGHEST,
        preferred_element_type=jnp.float32,
    )
    gain_part = jnp.sum(normed_grad * states * inv_rms, axis=0)
    scaled = gain * normed_grad
    inner = jnp.mean(scaled * states, axis=1, keepdims=True)
    hidden_grad = (inv_rms * scaled - states * inv_rms**3 * inner).astype(jnp.bfloat16)
    gain_dp, pieces = spread_with_sum(gain_part, pieces.astype(jnp.float32), "dp")
    gain_grad = sum_blocks(gain_dp, "fsdp")
    pooled_cols = pieces.reshape(pair_count, slice_width).astype(jnp.bfloat16)
    proj_grad = lax.dot_general(
        pooled_cols, grad_low_cols, contract_first, preferred_element_type=jnp.float32
    )
    return (mean_loss, query_grad, region_grad, hidden_grad, gain_grad, proj_grad)


SMALL_PAIRS = 1024


def local(query_cache, region_cache, positive, hidden_states, segment_ids, norm_gain, proj_weight):
    pair_count = query_cache.shape[0] * lax.axis_size("dp")
    args = (query_cache, region_cache, positive, hidden_states, segment_ids, norm_gain, proj_weight)
    if pair_count <= SMALL_PAIRS:
        return local_small(*args)
    return local_sharded(*args)


def solution(mesh):
    in_specs = (
        P("dp", "fsdp"),
        P("dp", "fsdp"),
        P("dp"),
        P(("dp", "fsdp"), None),
        P("dp", "fsdp"),
        P(),
        P("fsdp", None),
    )
    out_specs = (
        P(),
        P("dp", "fsdp"),
        P("dp", "fsdp"),
        P(("dp", "fsdp"), None),
        P(),
        P("dp", "fsdp"),
    )
    return jax.shard_map(local, mesh=mesh, in_specs=in_specs, out_specs=out_specs, check_vma=False)
```

```python
import jax
import jax.numpy as jnp
from jax import lax
from jax.sharding import PartitionSpec as P

E = 1024


EPS = 1e-05


def local_sharded(query_cache, region_cache, positive, hidden_states, segment_ids, norm_gain, proj_weight):
    row_count = query_cache.shape[0]
    data_count = lax.axis_size("dp")
    pair_count = row_count * data_count
    logit_scale = float(E) ** (-0.5)
    contract_last = (((1,), (1,)), ((), ()))
    contract_first = (((0,), (0,)), ((), ()))
    region_all, query_all = (
        lax.all_gather(region_cache, "dp", axis=0, tiled=True),
        lax.all_gather(query_cache, "dp", axis=0, tiled=True),
    )
    partial_value = lax.dot_general(
        query_cache, region_all, contract_last, preferred_element_type=jnp.float32
    )
    scores = lax.psum(partial_value, "fsdp") * logit_scale
    row_max = jnp.max(scores, axis=1, keepdims=True)
    log_total = row_max[:, 0] + jnp.log(jnp.sum(jnp.exp(scores - row_max), axis=1))
    columns = lax.broadcasted_iota(jnp.int32, (1, pair_count), 1)
    matched = columns == positive[:, None]
    target_score = jnp.sum(jnp.where(matched, scores, jnp.zeros_like(scores)), axis=1)
    loss_local = jnp.sum(log_total - target_score)
    grad_probs = (jnp.exp(scores - log_total[:, None]) - matched.astype(jnp.float32)).astype(
        jnp.bfloat16
    )
    query_grad = logit_scale * jnp.dot(grad_probs, region_all, preferred_element_type=jnp.float32)
    totals_all, targets_all = (
        lax.all_gather(log_total, "dp", axis=0, tiled=True),
        lax.all_gather(positive.astype(jnp.float32), "dp", axis=0, tiled=True),
    )
    partial_t = lax.dot_general(
        region_cache, query_all, contract_last, preferred_element_type=jnp.float32
    )
    scores_t = lax.psum(partial_t, "fsdp") * logit_scale
    own_rows = (
        lax.axis_index("dp") * row_count + lax.broadcasted_iota(jnp.int32, (row_count, 1), 0)
    ).astype(jnp.float32)
    matched_t = targets_all[None, :] == own_rows
    probs_t = (jnp.exp(scores_t - totals_all[None, :]) - matched_t.astype(jnp.float32)).astype(
        jnp.bfloat16
    )
    region_grad = logit_scale * jnp.dot(probs_t, query_all, preferred_element_type=jnp.float32)
    gain = norm_gain.astype(jnp.float32)
    states = hidden_states.astype(jnp.float32)
    inv_rms = lax.rsqrt(jnp.mean(states * states, axis=1, keepdims=True) + EPS)
    normed = (states * inv_rms * gain).astype(jnp.bfloat16)
    labels = lax.broadcasted_iota(jnp.int32, (row_count, 1), 0)
    member = segment_ids[0][None, :] == labels
    pooled_part = jnp.dot(member.astype(jnp.bfloat16), normed, preferred_element_type=jnp.float32)
    counts_part = jnp.sum(member.astype(jnp.float32), axis=1)
    pooled, counts = lax.psum((pooled_part, counts_part), "fsdp")
    mean_pooled = (pooled / counts[:, None]).astype(jnp.bfloat16)
    grad_low = query_grad.astype(jnp.bfloat16)
    grad_full = lax.all_gather(grad_low, "fsdp", axis=1, tiled=True)
    mean_part = lax.dot_general(
        grad_full, proj_weight, contract_last, preferred_element_type=jnp.float32
    )
    mean_grad = lax.all_gather(mean_part, "fsdp", axis=1, tiled=True)
    pool_grad = mean_grad / counts[:, None]
    normed_grad = lax.dot_general(
        member.astype(jnp.float32),
        pool_grad,
        contract_first,
        precision=lax.Precision.HIGHEST,
        preferred_element_type=jnp.float32,
    )
    gain_part = jnp.sum(normed_grad * states * inv_rms, axis=0)
    scaled = gain * normed_grad
    inner = jnp.mean(scaled * states, axis=1, keepdims=True)
    hidden_grad = (inv_rms * scaled - states * inv_rms**3 * inner).astype(jnp.bfloat16)
    proj_grad = lax.psum_scatter(
        lax.dot_general(mean_pooled, grad_low, contract_first, preferred_element_type=jnp.float32),
        "dp",
        scatter_dimension=0,
        tiled=True,
    )
    loss_total = lax.psum(loss_local, "dp")
    gain_grad = lax.psum(gain_part, ("dp", "fsdp"))
    mean_loss = loss_total / pair_count
    return (mean_loss, query_grad, region_grad, hidden_grad, gain_grad, proj_grad)


def arrange(copies, me):
    n = len(copies)
    source = ((me - jnp.arange(n)) % n).reshape((n,) + (1,) * copies[0].ndim)
    out = jnp.broadcast_to(copies[0][None], (n,) + copies[0].shape)
    for s in range(1, n):
        out = jnp.where(source == s, copies[s][None], out)
    return out


def gather_blocks(x, axis):
    n = lax.axis_size(axis)
    copies = [x] + [
        lax.ppermute(x, axis, [(i, (i + s) % n) for i in range(n)]) for s in range(1, n)
    ]
    return arrange(copies, lax.axis_index(axis))


def sum_blocks(x, axis):
    return jnp.sum(gather_blocks(x, axis), axis=0)


def scatter_sum(whole, axis):
    n = lax.axis_size(axis)
    me = lax.axis_index(axis)
    chunk = whole.shape[1] // n
    copies = [lax.dynamic_slice_in_dim(whole, me * chunk, chunk, axis=1)]
    for s in range(1, n):
        piece = lax.dynamic_slice_in_dim(whole, (me + s) % n * chunk, chunk, axis=1)
        copies.append(lax.ppermute(piece, axis, [(i, (i + s) % n) for i in range(n)]))
    return jnp.sum(arrange(copies, me), axis=0)


def spread_with_sum(total, pieces, axis):
    n = lax.axis_size(axis)
    me = lax.axis_index(axis)
    size = total.shape[0]
    sums = [total]
    got = [lax.dynamic_index_in_dim(pieces, me, axis=0, keepdims=False)]
    for s in range(1, n):
        piece = lax.dynamic_index_in_dim(pieces, (me + s) % n, axis=0, keepdims=False)
        payload = jnp.concatenate([total, piece.reshape(-1)])
        arrived = lax.ppermute(payload, axis, [(i, (i + s) % n) for i in range(n)])
        sums.append(arrived[:size])
        got.append(arrived[size:].reshape(piece.shape))
    return jnp.sum(arrange(sums, me), axis=0), lax.optimization_barrier(arrange(got, me))


def local_small(query_cache, region_cache, positive, hidden_states, segment_ids, norm_gain, proj_weight):
    rows, width = query_cache.shape
    data_count = lax.axis_size("dp")
    feature_count = lax.axis_size("fsdp")
    pair_count = rows * data_count
    tokens = segment_ids.shape[1]
    model_width = hidden_states.shape[1]
    logit_scale = float(E) ** (-0.5)
    contract_last = (((1,), (1,)), ((), ()))
    contract_first = (((0,), (0,)), ((), ()))
    me_dp = lax.axis_index("dp")
    me_f = lax.axis_index("fsdp")

    extra = jnp.concatenate(
        [positive // 64, positive % 64, segment_ids[0]]
    ).astype(jnp.float32)
    extra_rows = -(-extra.shape[0] // width)
    extra = jnp.pad(extra, (0, extra_rows * width - extra.shape[0]))
    packed = jnp.concatenate(
        [query_cache, region_cache, extra.reshape(extra_rows, width).astype(jnp.bfloat16)], axis=0
    )
    group_blocks = gather_blocks(packed, "fsdp")
    group_side = group_blocks[:, 2 * rows :].reshape(feature_count, extra_rows * width)
    group_ids = group_side[:, 2 * rows : 2 * rows + tokens].reshape(feature_count * tokens)
    group_ids = group_ids.astype(jnp.int32)

    gain = norm_gain.astype(jnp.float32)
    states = hidden_states.astype(jnp.float32)
    inv_rms = lax.rsqrt(jnp.mean(states * states, axis=1, keepdims=True) + EPS)
    normed = (states * inv_rms * gain).astype(jnp.bfloat16)
    labels = lax.broadcasted_iota(jnp.int32, (rows, 1), 0)
    member = segment_ids[0][None, :] == labels
    pooled_part = jnp.dot(member.astype(jnp.bfloat16), normed, preferred_element_type=jnp.float32)
    counts = jnp.sum((group_ids[None, :] == labels).astype(jnp.float32), axis=1)
    chunk = model_width // feature_count
    pooled_chunk = scatter_sum(pooled_part, "fsdp")
    mean_chunk = (pooled_chunk / counts[:, None]).astype(jnp.bfloat16)
    mean_blocks = lax.optimization_barrier(gather_blocks(mean_chunk, "fsdp"))
    mean_pooled = mean_blocks.transpose(1, 0, 2).reshape(rows, model_width)

    gathered = gather_blocks(group_blocks, "dp")
    mean_pooled, gathered = lax.optimization_barrier((mean_pooled, gathered))
    slice_width = model_width // data_count
    pieces = mean_pooled.reshape(rows, data_count, slice_width).transpose(1, 0, 2)

    query_all = gathered[:, :, :rows].transpose(0, 2, 1, 3).reshape(pair_count, feature_count * width)
    region_all = gathered[:, :, rows : 2 * rows].transpose(0, 2, 1, 3).reshape(
        pair_count, feature_count * width
    )
    side = gathered[:, :, 2 * rows :].reshape(data_count, feature_count, extra_rows * width)
    side = side.astype(jnp.float32)
    positive_all = (side[:, 0, :rows] * 64 + side[:, 0, rows : 2 * rows]).astype(jnp.int32)
    positive_all = positive_all.reshape(pair_count)

    scores = (
        lax.dot_general(query_all, region_all, contract_last, preferred_element_type=jnp.float32)
        * logit_scale
    )
    row_max = jnp.max(scores, axis=1, keepdims=True)
    log_total = row_max[:, 0] + jnp.log(jnp.sum(jnp.exp(scores - row_max), axis=1))
    columns = lax.broadcasted_iota(jnp.int32, (1, pair_count), 1)
    matched = columns == positive_all[:, None]
    target_score = jnp.sum(jnp.where(matched, scores, jnp.zeros_like(scores)), axis=1)
    mean_loss = jnp.sum(log_total - target_score) / pair_count
    grad_probs = (jnp.exp(scores - log_total[:, None]) - matched.astype(jnp.float32)).astype(
        jnp.bfloat16
    )
    query_grad_all = logit_scale * jnp.dot(grad_probs, region_all, preferred_element_type=jnp.float32)
    query_grad = lax.dynamic_slice(query_grad_all, (me_dp * rows, me_f * width), (rows, width))
    grad_low = lax.dynamic_slice(query_grad_all, (me_dp * rows, 0), (rows, feature_count * width))
    grad_low = grad_low.astype(jnp.bfloat16)
    grad_low_cols = lax.dynamic_slice(query_grad_all, (0, me_f * width), (pair_count, width))
    grad_low_cols = grad_low_cols.astype(jnp.bfloat16)
    probs_cols = lax.dynamic_slice(grad_probs, (0, me_dp * rows), (pair_count, rows))
    query_cols = lax.dynamic_slice(query_all, (0, me_f * width), (pair_count, width))
    region_grad = logit_scale * lax.dot_general(
        probs_cols, query_cols, contract_first, preferred_element_type=jnp.float32
    )

    mean_part = lax.dot_general(
        grad_low, proj_weight, contract_last, preferred_element_type=jnp.float32
    )
    mean_grad = lax.all_gather(mean_part, "fsdp", axis=1, tiled=True)
    pool_grad = mean_grad / counts[:, None]
    normed_grad = lax.dot_general(
        member.astype(jnp.float32),
        pool_grad,
        contract_first,
        precision=lax.Precision.HIGHEST,
        preferred_element_type=jnp.float32,
    )
    gain_part = jnp.sum(normed_grad * states * inv_rms, axis=0)
    scaled = gain * normed_grad
    inner = jnp.mean(scaled * states, axis=1, keepdims=True)
    hidden_grad = (inv_rms * scaled - states * inv_rms**3 * inner).astype(jnp.bfloat16)
    gain_dp, pieces = spread_with_sum(gain_part, pieces.astype(jnp.float32), "dp")
    gain_grad = sum_blocks(gain_dp, "fsdp")
    pooled_cols = pieces.reshape(pair_count, slice_width).astype(jnp.bfloat16)
    proj_grad = lax.dot_general(
        pooled_cols, grad_low_cols, contract_first, preferred_element_type=jnp.float32
    )
    return (mean_loss, query_grad, region_grad, hidden_grad, gain_grad, proj_grad)


SMALL_PAIRS = 1024


def local(query_cache, region_cache, positive, hidden_states, segment_ids, norm_gain, proj_weight):
    pair_count = query_cache.shape[0] * lax.axis_size("dp")
    args = (query_cache, region_cache, positive, hidden_states, segment_ids, norm_gain, proj_weight)
    if pair_count <= SMALL_PAIRS:
        return local_small(*args)
    return local_sharded(*args)


def solution(mesh):
    in_specs = (
        P("dp", "fsdp"),
        P("dp", "fsdp"),
        P("dp"),
        P(("dp", "fsdp"), None),
        P("dp", "fsdp"),
        P(),
        P("fsdp", None),
    )
    out_specs = (
        P(),
        P("dp", "fsdp"),
        P("dp", "fsdp"),
        P(("dp", "fsdp"), None),
        P(),
        P("dp", "fsdp"),
    )
    return jax.shard_map(local, mesh=mesh, in_specs=in_specs, out_specs=out_specs, check_vma=False)
```

```python
import jax
import jax.numpy as jnp
from jax import lax
from jax.sharding import PartitionSpec as P

E = 1024


EPS = 1e-05


def local_sharded(query_cache, region_cache, positive, hidden_states, segment_ids, norm_gain, proj_weight):
    row_count = query_cache.shape[0]
    data_count = lax.axis_size("dp")
    pair_count = row_count * data_count
    logit_scale = float(E) ** (-0.5)
    contract_last = (((1,), (1,)), ((), ()))
    contract_first = (((0,), (0,)), ((), ()))
    region_all, query_all = (
        lax.all_gather(region_cache, "dp", axis=0, tiled=True),
        lax.all_gather(query_cache, "dp", axis=0, tiled=True),
    )
    partial_value = lax.dot_general(
        query_cache, region_all, contract_last, preferred_element_type=jnp.float32
    )
    scores = lax.psum(partial_value, "fsdp") * logit_scale
    row_max = jnp.max(scores, axis=1, keepdims=True)
    log_total = row_max[:, 0] + jnp.log(jnp.sum(jnp.exp(scores - row_max), axis=1))
    columns = lax.broadcasted_iota(jnp.int32, (1, pair_count), 1)
    matched = columns == positive[:, None]
    target_score = jnp.sum(jnp.where(matched, scores, jnp.zeros_like(scores)), axis=1)
    loss_local = jnp.sum(log_total - target_score)
    grad_probs = (jnp.exp(scores - log_total[:, None]) - matched.astype(jnp.float32)).astype(
        jnp.bfloat16
    )
    query_grad = logit_scale * jnp.dot(grad_probs, region_all, preferred_element_type=jnp.float32)
    totals_all, targets_all = (
        lax.all_gather(log_total, "dp", axis=0, tiled=True),
        lax.all_gather(positive.astype(jnp.float32), "dp", axis=0, tiled=True),
    )
    partial_t = lax.dot_general(
        region_cache, query_all, contract_last, preferred_element_type=jnp.float32
    )
    scores_t = lax.psum(partial_t, "fsdp") * logit_scale
    own_rows = (
        lax.axis_index("dp") * row_count + lax.broadcasted_iota(jnp.int32, (row_count, 1), 0)
    ).astype(jnp.float32)
    matched_t = targets_all[None, :] == own_rows
    probs_t = (jnp.exp(scores_t - totals_all[None, :]) - matched_t.astype(jnp.float32)).astype(
        jnp.bfloat16
    )
    region_grad = logit_scale * jnp.dot(probs_t, query_all, preferred_element_type=jnp.float32)
    gain = norm_gain.astype(jnp.float32)
    states = hidden_states.astype(jnp.float32)
    inv_rms = lax.rsqrt(jnp.mean(states * states, axis=1, keepdims=True) + EPS)
    normed = (states * inv_rms * gain).astype(jnp.bfloat16)
    labels = lax.broadcasted_iota(jnp.int32, (row_count, 1), 0)
    member = segment_ids[0][None, :] == labels
    pooled_part = jnp.dot(member.astype(jnp.bfloat16), normed, preferred_element_type=jnp.float32)
    counts_part = jnp.sum(member.astype(jnp.float32), axis=1)
    pooled, counts = lax.psum((pooled_part, counts_part), "fsdp")
    mean_pooled = (pooled / counts[:, None]).astype(jnp.bfloat16)
    grad_low = query_grad.astype(jnp.bfloat16)
    grad_full = lax.all_gather(grad_low, "fsdp", axis=1, tiled=True)
    mean_part = lax.dot_general(
        grad_full, proj_weight, contract_last, preferred_element_type=jnp.float32
    )
    mean_grad = lax.all_gather(mean_part, "fsdp", axis=1, tiled=True)
    pool_grad = mean_grad / counts[:, None]
    normed_grad = lax.dot_general(
        member.astype(jnp.float32),
        pool_grad,
        contract_first,
        precision=lax.Precision.HIGHEST,
        preferred_element_type=jnp.float32,
    )
    gain_part = jnp.sum(normed_grad * states * inv_rms, axis=0)
    scaled = gain * normed_grad
    inner = jnp.mean(scaled * states, axis=1, keepdims=True)
    hidden_grad = (inv_rms * scaled - states * inv_rms**3 * inner).astype(jnp.bfloat16)
    proj_grad = lax.psum_scatter(
        lax.dot_general(mean_pooled, grad_low, contract_first, preferred_element_type=jnp.float32),
        "dp",
        scatter_dimension=0,
        tiled=True,
    )
    loss_total = lax.psum(loss_local, "dp")
    gain_grad = lax.psum(gain_part, ("dp", "fsdp"))
    mean_loss = loss_total / pair_count
    return (mean_loss, query_grad, region_grad, hidden_grad, gain_grad, proj_grad)


def arrange(copies, me):
    n = len(copies)
    source = ((me - jnp.arange(n)) % n).reshape((n,) + (1,) * copies[0].ndim)
    out = jnp.broadcast_to(copies[0][None], (n,) + copies[0].shape)
    for s in range(1, n):
        out = jnp.where(source == s, copies[s][None], out)
    return out


def gather_blocks(x, axis):
    n = lax.axis_size(axis)
    copies = [x] + [
        lax.ppermute(x, axis, [(i, (i + s) % n) for i in range(n)]) for s in range(1, n)
    ]
    return arrange(copies, lax.axis_index(axis))


def sum_blocks(x, axis):
    return jnp.sum(gather_blocks(x, axis), axis=0)


def scatter_sum(whole, axis):
    n = lax.axis_size(axis)
    me = lax.axis_index(axis)
    chunk = whole.shape[1] // n
    copies = [lax.dynamic_slice_in_dim(whole, me * chunk, chunk, axis=1)]
    for s in range(1, n):
        piece = lax.dynamic_slice_in_dim(whole, (me + s) % n * chunk, chunk, axis=1)
        copies.append(lax.ppermute(piece, axis, [(i, (i + s) % n) for i in range(n)]))
    return jnp.sum(arrange(copies, me), axis=0)


def spread_with_sum(total, pieces, axis):
    n = lax.axis_size(axis)
    me = lax.axis_index(axis)
    size = total.shape[0]
    sums = [total]
    got = [lax.dynamic_index_in_dim(pieces, me, axis=0, keepdims=False)]
    for s in range(1, n):
        piece = lax.dynamic_index_in_dim(pieces, (me + s) % n, axis=0, keepdims=False)
        payload = jnp.concatenate([total, piece.reshape(-1)])
        arrived = lax.ppermute(payload, axis, [(i, (i + s) % n) for i in range(n)])
        sums.append(arrived[:size])
        got.append(arrived[size:].reshape(piece.shape))
    return jnp.sum(arrange(sums, me), axis=0), lax.optimization_barrier(arrange(got, me))


def local_small(query_cache, region_cache, positive, hidden_states, segment_ids, norm_gain, proj_weight):
    rows, width = query_cache.shape
    data_count = lax.axis_size("dp")
    feature_count = lax.axis_size("fsdp")
    pair_count = rows * data_count
    tokens = segment_ids.shape[1]
    model_width = hidden_states.shape[1]
    logit_scale = float(E) ** (-0.5)
    contract_last = (((1,), (1,)), ((), ()))
    contract_first = (((0,), (0,)), ((), ()))
    me_dp = lax.axis_index("dp")
    me_f = lax.axis_index("fsdp")

    extra = jnp.concatenate(
        [positive // 64, positive % 64, segment_ids[0]]
    ).astype(jnp.float32)
    extra_rows = -(-extra.shape[0] // width)
    extra = jnp.pad(extra, (0, extra_rows * width - extra.shape[0]))
    packed = jnp.concatenate(
        [query_cache, region_cache, extra.reshape(extra_rows, width).astype(jnp.bfloat16)], axis=0
    )
    group_blocks = gather_blocks(packed, "fsdp")
    group_side = group_blocks[:, 2 * rows :].reshape(feature_count, extra_rows * width)
    group_ids = group_side[:, 2 * rows : 2 * rows + tokens].reshape(feature_count * tokens)
    group_ids = group_ids.astype(jnp.int32)

    gain = norm_gain.astype(jnp.float32)
    states = hidden_states.astype(jnp.float32)
    inv_rms = lax.rsqrt(jnp.mean(states * states, axis=1, keepdims=True) + EPS)
    normed = (states * inv_rms * gain).astype(jnp.bfloat16)
    labels = lax.broadcasted_iota(jnp.int32, (rows, 1), 0)
    member = segment_ids[0][None, :] == labels
    pooled_part = jnp.dot(member.astype(jnp.bfloat16), normed, preferred_element_type=jnp.float32)
    counts = jnp.sum((group_ids[None, :] == labels).astype(jnp.float32), axis=1)
    chunk = model_width // feature_count
    pooled_chunk = scatter_sum(pooled_part, "fsdp")
    mean_chunk = (pooled_chunk / counts[:, None]).astype(jnp.bfloat16)
    mean_blocks = lax.optimization_barrier(gather_blocks(mean_chunk, "fsdp"))
    mean_pooled = mean_blocks.transpose(1, 0, 2).reshape(rows, model_width)

    gathered = gather_blocks(group_blocks, "dp")
    mean_pooled, gathered = lax.optimization_barrier((mean_pooled, gathered))
    slice_width = model_width // data_count
    pieces = mean_pooled.reshape(rows, data_count, slice_width).transpose(1, 0, 2)

    query_all = gathered[:, :, :rows].transpose(0, 2, 1, 3).reshape(pair_count, feature_count * width)
    region_all = gathered[:, :, rows : 2 * rows].transpose(0, 2, 1, 3).reshape(
        pair_count, feature_count * width
    )
    side = gathered[:, :, 2 * rows :].reshape(data_count, feature_count, extra_rows * width)
    side = side.astype(jnp.float32)
    positive_all = (side[:, 0, :rows] * 64 + side[:, 0, rows : 2 * rows]).astype(jnp.int32)
    positive_all = positive_all.reshape(pair_count)

    scores = (
        lax.dot_general(query_all, region_all, contract_last, preferred_element_type=jnp.float32)
        * logit_scale
    )
    row_max = jnp.max(scores, axis=1, keepdims=True)
    log_total = row_max[:, 0] + jnp.log(jnp.sum(jnp.exp(scores - row_max), axis=1))
    columns = lax.broadcasted_iota(jnp.int32, (1, pair_count), 1)
    matched = columns == positive_all[:, None]
    target_score = jnp.sum(jnp.where(matched, scores, jnp.zeros_like(scores)), axis=1)
    mean_loss = jnp.sum(log_total - target_score) / pair_count
    grad_probs = (jnp.exp(scores - log_total[:, None]) - matched.astype(jnp.float32)).astype(
        jnp.bfloat16
    )
    query_grad_all = logit_scale * jnp.dot(grad_probs, region_all, preferred_element_type=jnp.float32)
    query_grad = lax.dynamic_slice(query_grad_all, (me_dp * rows, me_f * width), (rows, width))
    grad_low = lax.dynamic_slice(query_grad_all, (me_dp * rows, 0), (rows, feature_count * width))
    grad_low = grad_low.astype(jnp.bfloat16)
    grad_low_cols = lax.dynamic_slice(query_grad_all, (0, me_f * width), (pair_count, width))
    grad_low_cols = grad_low_cols.astype(jnp.bfloat16)
    probs_cols = lax.dynamic_slice(grad_probs, (0, me_dp * rows), (pair_count, rows))
    query_cols = lax.dynamic_slice(query_all, (0, me_f * width), (pair_count, width))
    region_grad = logit_scale * lax.dot_general(
        probs_cols, query_cols, contract_first, preferred_element_type=jnp.float32
    )

    mean_part = lax.dot_general(
        grad_low, proj_weight, contract_last, preferred_element_type=jnp.float32
    )
    mean_grad = lax.all_gather(mean_part, "fsdp", axis=1, tiled=True)
    pool_grad = mean_grad / counts[:, None]
    normed_grad = lax.dot_general(
        member.astype(jnp.float32),
        pool_grad,
        contract_first,
        precision=lax.Precision.HIGHEST,
        preferred_element_type=jnp.float32,
    )
    gain_part = jnp.sum(normed_grad * states * inv_rms, axis=0)
    scaled = gain * normed_grad
    inner = jnp.mean(scaled * states, axis=1, keepdims=True)
    hidden_grad = (inv_rms * scaled - states * inv_rms**3 * inner).astype(jnp.bfloat16)
    gain_grad, pieces = spread_with_sum(
        sum_blocks(gain_part, "fsdp"), pieces.astype(jnp.float32), "dp"
    )
    pooled_cols = pieces.reshape(pair_count, slice_width).astype(jnp.bfloat16)
    proj_grad = lax.dot_general(
        pooled_cols, grad_low_cols, contract_first, preferred_element_type=jnp.float32
    )
    return (mean_loss, query_grad, region_grad, hidden_grad, gain_grad, proj_grad)


SMALL_PAIRS = 1024


def local(query_cache, region_cache, positive, hidden_states, segment_ids, norm_gain, proj_weight):
    pair_count = query_cache.shape[0] * lax.axis_size("dp")
    args = (query_cache, region_cache, positive, hidden_states, segment_ids, norm_gain, proj_weight)
    if pair_count <= SMALL_PAIRS:
        return local_small(*args)
    return local_sharded(*args)


def solution(mesh):
    in_specs = (
        P("dp", "fsdp"),
        P("dp", "fsdp"),
        P("dp"),
        P(("dp", "fsdp"), None),
        P("dp", "fsdp"),
        P(),
        P("fsdp", None),
    )
    out_specs = (
        P(),
        P("dp", "fsdp"),
        P("dp", "fsdp"),
        P(("dp", "fsdp"), None),
        P(),
        P("dp", "fsdp"),
    )
    return jax.shard_map(local, mesh=mesh, in_specs=in_specs, out_specs=out_specs, check_vma=False)
```

```python
import jax
import jax.numpy as jnp
from jax import lax
from jax.sharding import PartitionSpec as P

E = 1024


EPS = 1e-05


def local_sharded(query_cache, region_cache, positive, hidden_states, segment_ids, norm_gain, proj_weight):
    row_count = query_cache.shape[0]
    data_count = lax.axis_size("dp")
    pair_count = row_count * data_count
    logit_scale = float(E) ** (-0.5)
    contract_last = (((1,), (1,)), ((), ()))
    contract_first = (((0,), (0,)), ((), ()))
    region_all, query_all = (
        lax.all_gather(region_cache, "dp", axis=0, tiled=True),
        lax.all_gather(query_cache, "dp", axis=0, tiled=True),
    )
    partial_value = lax.dot_general(
        query_cache, region_all, contract_last, preferred_element_type=jnp.float32
    )
    scores = lax.psum(partial_value, "fsdp") * logit_scale
    row_max = jnp.max(scores, axis=1, keepdims=True)
    log_total = row_max[:, 0] + jnp.log(jnp.sum(jnp.exp(scores - row_max), axis=1))
    columns = lax.broadcasted_iota(jnp.int32, (1, pair_count), 1)
    matched = columns == positive[:, None]
    target_score = jnp.sum(jnp.where(matched, scores, jnp.zeros_like(scores)), axis=1)
    loss_local = jnp.sum(log_total - target_score)
    grad_probs = (jnp.exp(scores - log_total[:, None]) - matched.astype(jnp.float32)).astype(
        jnp.bfloat16
    )
    query_grad = logit_scale * jnp.dot(grad_probs, region_all, preferred_element_type=jnp.float32)
    totals_all, targets_all = (
        lax.all_gather(log_total, "dp", axis=0, tiled=True),
        lax.all_gather(positive.astype(jnp.float32), "dp", axis=0, tiled=True),
    )
    partial_t = lax.dot_general(
        region_cache, query_all, contract_last, preferred_element_type=jnp.float32
    )
    scores_t = lax.psum(partial_t, "fsdp") * logit_scale
    own_rows = (
        lax.axis_index("dp") * row_count + lax.broadcasted_iota(jnp.int32, (row_count, 1), 0)
    ).astype(jnp.float32)
    matched_t = targets_all[None, :] == own_rows
    probs_t = (jnp.exp(scores_t - totals_all[None, :]) - matched_t.astype(jnp.float32)).astype(
        jnp.bfloat16
    )
    region_grad = logit_scale * jnp.dot(probs_t, query_all, preferred_element_type=jnp.float32)
    gain = norm_gain.astype(jnp.float32)
    states = hidden_states.astype(jnp.float32)
    inv_rms = lax.rsqrt(jnp.mean(states * states, axis=1, keepdims=True) + EPS)
    normed = (states * inv_rms * gain).astype(jnp.bfloat16)
    labels = lax.broadcasted_iota(jnp.int32, (row_count, 1), 0)
    member = segment_ids[0][None, :] == labels
    pooled_part = jnp.dot(member.astype(jnp.bfloat16), normed, preferred_element_type=jnp.float32)
    counts_part = jnp.sum(member.astype(jnp.float32), axis=1)
    pooled, counts = lax.psum((pooled_part, counts_part), "fsdp")
    mean_pooled = (pooled / counts[:, None]).astype(jnp.bfloat16)
    grad_low = query_grad.astype(jnp.bfloat16)
    grad_full = lax.all_gather(grad_low, "fsdp", axis=1, tiled=True)
    mean_part = lax.dot_general(
        grad_full, proj_weight, contract_last, preferred_element_type=jnp.float32
    )
    mean_grad = lax.all_gather(mean_part, "fsdp", axis=1, tiled=True)
    pool_grad = mean_grad / counts[:, None]
    normed_grad = lax.dot_general(
        member.astype(jnp.float32),
        pool_grad,
        contract_first,
        precision=lax.Precision.HIGHEST,
        preferred_element_type=jnp.float32,
    )
    gain_part = jnp.sum(normed_grad * states * inv_rms, axis=0)
    scaled = gain * normed_grad
    inner = jnp.mean(scaled * states, axis=1, keepdims=True)
    hidden_grad = (inv_rms * scaled - states * inv_rms**3 * inner).astype(jnp.bfloat16)
    proj_grad = lax.psum_scatter(
        lax.dot_general(mean_pooled, grad_low, contract_first, preferred_element_type=jnp.float32),
        "dp",
        scatter_dimension=0,
        tiled=True,
    )
    loss_total = lax.psum(loss_local, "dp")
    gain_grad = lax.psum(gain_part, ("dp", "fsdp"))
    mean_loss = loss_total / pair_count
    return (mean_loss, query_grad, region_grad, hidden_grad, gain_grad, proj_grad)


def arrange(copies, me):
    n = len(copies)
    source = ((me - jnp.arange(n)) % n).reshape((n,) + (1,) * copies[0].ndim)
    out = jnp.broadcast_to(copies[0][None], (n,) + copies[0].shape)
    for s in range(1, n):
        out = jnp.where(source == s, copies[s][None], out)
    return out


def gather_blocks(x, axis):
    n = lax.axis_size(axis)
    copies = [x] + [
        lax.ppermute(x, axis, [(i, (i + s) % n) for i in range(n)]) for s in range(1, n)
    ]
    return arrange(copies, lax.axis_index(axis))


def sum_blocks(x, axis):
    return jnp.sum(gather_blocks(x, axis), axis=0)


def scatter_sum(whole, axis):
    n = lax.axis_size(axis)
    me = lax.axis_index(axis)
    chunk = whole.shape[1] // n
    copies = [lax.dynamic_slice_in_dim(whole, me * chunk, chunk, axis=1)]
    for s in range(1, n):
        piece = lax.dynamic_slice_in_dim(whole, (me + s) % n * chunk, chunk, axis=1)
        copies.append(lax.ppermute(piece, axis, [(i, (i + s) % n) for i in range(n)]))
    return jnp.sum(arrange(copies, me), axis=0)


def spread_with_sum(total, pieces, axis):
    n = lax.axis_size(axis)
    me = lax.axis_index(axis)
    size = total.shape[0]
    sums = [total]
    got = [lax.dynamic_index_in_dim(pieces, me, axis=0, keepdims=False)]
    for s in range(1, n):
        piece = lax.dynamic_index_in_dim(pieces, (me + s) % n, axis=0, keepdims=False)
        payload = jnp.concatenate([total, piece.reshape(-1)])
        arrived = lax.ppermute(payload, axis, [(i, (i + s) % n) for i in range(n)])
        sums.append(arrived[:size])
        got.append(arrived[size:].reshape(piece.shape))
    return jnp.sum(arrange(sums, me), axis=0), lax.optimization_barrier(arrange(got, me))


def local_small(query_cache, region_cache, positive, hidden_states, segment_ids, norm_gain, proj_weight):
    rows, width = query_cache.shape
    data_count = lax.axis_size("dp")
    feature_count = lax.axis_size("fsdp")
    pair_count = rows * data_count
    tokens = segment_ids.shape[1]
    model_width = hidden_states.shape[1]
    logit_scale = float(E) ** (-0.5)
    contract_last = (((1,), (1,)), ((), ()))
    contract_first = (((0,), (0,)), ((), ()))
    me_dp = lax.axis_index("dp")
    me_f = lax.axis_index("fsdp")

    extra = jnp.concatenate(
        [positive // 64, positive % 64, segment_ids[0]]
    ).astype(jnp.float32)
    extra_rows = -(-extra.shape[0] // width)
    extra = jnp.pad(extra, (0, extra_rows * width - extra.shape[0]))
    packed = jnp.concatenate(
        [query_cache, region_cache, extra.reshape(extra_rows, width).astype(jnp.bfloat16)], axis=0
    )
    group_blocks = gather_blocks(packed, "fsdp")
    group_side = group_blocks[:, 2 * rows :].reshape(feature_count, extra_rows * width)
    group_ids = group_side[:, 2 * rows : 2 * rows + tokens].reshape(feature_count * tokens)
    group_ids = group_ids.astype(jnp.int32)

    gain = norm_gain.astype(jnp.float32)
    states = hidden_states.astype(jnp.float32)
    inv_rms = lax.rsqrt(jnp.mean(states * states, axis=1, keepdims=True) + EPS)
    normed = (states * inv_rms * gain).astype(jnp.bfloat16)
    labels = lax.broadcasted_iota(jnp.int32, (rows, 1), 0)
    member = segment_ids[0][None, :] == labels
    pooled_part = jnp.dot(member.astype(jnp.bfloat16), normed, preferred_element_type=jnp.float32)
    counts = jnp.sum((group_ids[None, :] == labels).astype(jnp.float32), axis=1)
    chunk = model_width // feature_count
    pooled_chunk = scatter_sum(pooled_part, "fsdp")
    mean_chunk = (pooled_chunk / counts[:, None]).astype(jnp.bfloat16)
    mean_blocks = lax.optimization_barrier(gather_blocks(mean_chunk, "fsdp"))
    mean_pooled = mean_blocks.transpose(1, 0, 2).reshape(rows, model_width)

    gathered = gather_blocks(group_blocks, "dp")
    mean_pooled, gathered = lax.optimization_barrier((mean_pooled, gathered))
    slice_width = model_width // data_count
    pieces = mean_pooled.reshape(rows, data_count, slice_width).transpose(1, 0, 2)

    query_all = gathered[:, :, :rows].transpose(0, 2, 1, 3).reshape(pair_count, feature_count * width)
    region_all = gathered[:, :, rows : 2 * rows].transpose(0, 2, 1, 3).reshape(
        pair_count, feature_count * width
    )
    side = gathered[:, :, 2 * rows :].reshape(data_count, feature_count, extra_rows * width)
    side = side.astype(jnp.float32)
    positive_all = (side[:, 0, :rows] * 64 + side[:, 0, rows : 2 * rows]).astype(jnp.int32)
    positive_all = positive_all.reshape(pair_count)

    scores = (
        lax.dot_general(query_all, region_all, contract_last, preferred_element_type=jnp.float32)
        * logit_scale
    )
    row_max = jnp.max(scores, axis=1, keepdims=True)
    log_total = row_max[:, 0] + jnp.log(jnp.sum(jnp.exp(scores - row_max), axis=1))
    columns = lax.broadcasted_iota(jnp.int32, (1, pair_count), 1)
    matched = columns == positive_all[:, None]
    target_score = jnp.sum(jnp.where(matched, scores, jnp.zeros_like(scores)), axis=1)
    mean_loss = jnp.sum(log_total - target_score) / pair_count
    grad_probs = (jnp.exp(scores - log_total[:, None]) - matched.astype(jnp.float32)).astype(
        jnp.bfloat16
    )
    query_grad_all = logit_scale * jnp.dot(grad_probs, region_all, preferred_element_type=jnp.float32)
    query_grad = lax.dynamic_slice(query_grad_all, (me_dp * rows, me_f * width), (rows, width))
    grad_low = lax.dynamic_slice(query_grad_all, (me_dp * rows, 0), (rows, feature_count * width))
    grad_low = grad_low.astype(jnp.bfloat16)
    grad_low_cols = lax.dynamic_slice(query_grad_all, (0, me_f * width), (pair_count, width))
    grad_low_cols = grad_low_cols.astype(jnp.bfloat16)
    probs_cols = lax.dynamic_slice(grad_probs, (0, me_dp * rows), (pair_count, rows))
    query_cols = lax.dynamic_slice(query_all, (0, me_f * width), (pair_count, width))
    region_grad = logit_scale * lax.dot_general(
        probs_cols, query_cols, contract_first, preferred_element_type=jnp.float32
    )

    mean_part = lax.dot_general(
        grad_low, proj_weight, contract_last, preferred_element_type=jnp.float32
    )
    mean_grad = lax.optimization_barrier(gather_blocks(mean_part, "fsdp"))
    mean_grad = mean_grad.transpose(1, 0, 2).reshape(rows, model_width)
    pool_grad = mean_grad / counts[:, None]
    normed_grad = lax.dot_general(
        member.astype(jnp.float32),
        pool_grad,
        contract_first,
        precision=lax.Precision.HIGHEST,
        preferred_element_type=jnp.float32,
    )
    gain_part = jnp.sum(normed_grad * states * inv_rms, axis=0)
    scaled = gain * normed_grad
    inner = jnp.mean(scaled * states, axis=1, keepdims=True)
    hidden_grad = (inv_rms * scaled - states * inv_rms**3 * inner).astype(jnp.bfloat16)
    gain_dp, pieces = spread_with_sum(gain_part, pieces.astype(jnp.float32), "dp")
    gain_grad = sum_blocks(gain_dp, "fsdp")
    pooled_cols = pieces.reshape(pair_count, slice_width).astype(jnp.bfloat16)
    proj_grad = lax.dot_general(
        pooled_cols, grad_low_cols, contract_first, preferred_element_type=jnp.float32
    )
    return (mean_loss, query_grad, region_grad, hidden_grad, gain_grad, proj_grad)


SMALL_PAIRS = 1024


def local(query_cache, region_cache, positive, hidden_states, segment_ids, norm_gain, proj_weight):
    pair_count = query_cache.shape[0] * lax.axis_size("dp")
    args = (query_cache, region_cache, positive, hidden_states, segment_ids, norm_gain, proj_weight)
    if pair_count <= SMALL_PAIRS:
        return local_small(*args)
    return local_sharded(*args)


def solution(mesh):
    in_specs = (
        P("dp", "fsdp"),
        P("dp", "fsdp"),
        P("dp"),
        P(("dp", "fsdp"), None),
        P("dp", "fsdp"),
        P(),
        P("fsdp", None),
    )
    out_specs = (
        P(),
        P("dp", "fsdp"),
        P("dp", "fsdp"),
        P(("dp", "fsdp"), None),
        P(),
        P("dp", "fsdp"),
    )
    return jax.shard_map(local, mesh=mesh, in_specs=in_specs, out_specs=out_specs, check_vma=False)
```

```python
import jax
import jax.numpy as jnp
from jax import lax
from jax.sharding import PartitionSpec as P

E = 1024


EPS = 1e-05


def local_sharded(query_cache, region_cache, positive, hidden_states, segment_ids, norm_gain, proj_weight):
    row_count = query_cache.shape[0]
    data_count = lax.axis_size("dp")
    pair_count = row_count * data_count
    logit_scale = float(E) ** (-0.5)
    contract_last = (((1,), (1,)), ((), ()))
    contract_first = (((0,), (0,)), ((), ()))
    region_all, query_all = (
        lax.all_gather(region_cache, "dp", axis=0, tiled=True),
        lax.all_gather(query_cache, "dp", axis=0, tiled=True),
    )
    partial_value = lax.dot_general(
        query_cache, region_all, contract_last, preferred_element_type=jnp.float32
    )
    scores = lax.psum(partial_value, "fsdp") * logit_scale
    row_max = jnp.max(scores, axis=1, keepdims=True)
    log_total = row_max[:, 0] + jnp.log(jnp.sum(jnp.exp(scores - row_max), axis=1))
    columns = lax.broadcasted_iota(jnp.int32, (1, pair_count), 1)
    matched = columns == positive[:, None]
    target_score = jnp.sum(jnp.where(matched, scores, jnp.zeros_like(scores)), axis=1)
    loss_local = jnp.sum(log_total - target_score)
    grad_probs = (jnp.exp(scores - log_total[:, None]) - matched.astype(jnp.float32)).astype(
        jnp.bfloat16
    )
    query_grad = logit_scale * jnp.dot(grad_probs, region_all, preferred_element_type=jnp.float32)
    totals_all, targets_all = (
        lax.all_gather(log_total, "dp", axis=0, tiled=True),
        lax.all_gather(positive.astype(jnp.float32), "dp", axis=0, tiled=True),
    )
    partial_t = lax.dot_general(
        region_cache, query_all, contract_last, preferred_element_type=jnp.float32
    )
    scores_t = lax.psum(partial_t, "fsdp") * logit_scale
    own_rows = (
        lax.axis_index("dp") * row_count + lax.broadcasted_iota(jnp.int32, (row_count, 1), 0)
    ).astype(jnp.float32)
    matched_t = targets_all[None, :] == own_rows
    probs_t = (jnp.exp(scores_t - totals_all[None, :]) - matched_t.astype(jnp.float32)).astype(
        jnp.bfloat16
    )
    region_grad = logit_scale * jnp.dot(probs_t, query_all, preferred_element_type=jnp.float32)
    gain = norm_gain.astype(jnp.float32)
    states = hidden_states.astype(jnp.float32)
    inv_rms = lax.rsqrt(jnp.mean(states * states, axis=1, keepdims=True) + EPS)
    normed = (states * inv_rms * gain).astype(jnp.bfloat16)
    labels = lax.broadcasted_iota(jnp.int32, (row_count, 1), 0)
    member = segment_ids[0][None, :] == labels
    pooled_part = jnp.dot(member.astype(jnp.bfloat16), normed, preferred_element_type=jnp.float32)
    counts_part = jnp.sum(member.astype(jnp.float32), axis=1)
    pooled, counts = lax.psum((pooled_part, counts_part), "fsdp")
    mean_pooled = (pooled / counts[:, None]).astype(jnp.bfloat16)
    grad_low = query_grad.astype(jnp.bfloat16)
    grad_full = lax.all_gather(grad_low, "fsdp", axis=1, tiled=True)
    mean_part = lax.dot_general(
        grad_full, proj_weight, contract_last, preferred_element_type=jnp.float32
    )
    mean_grad = lax.all_gather(mean_part, "fsdp", axis=1, tiled=True)
    pool_grad = mean_grad / counts[:, None]
    normed_grad = lax.dot_general(
        member.astype(jnp.float32),
        pool_grad,
        contract_first,
        precision=lax.Precision.HIGHEST,
        preferred_element_type=jnp.float32,
    )
    gain_part = jnp.sum(normed_grad * states * inv_rms, axis=0)
    scaled = gain * normed_grad
    inner = jnp.mean(scaled * states, axis=1, keepdims=True)
    hidden_grad = (inv_rms * scaled - states * inv_rms**3 * inner).astype(jnp.bfloat16)
    proj_grad = lax.psum_scatter(
        lax.dot_general(mean_pooled, grad_low, contract_first, preferred_element_type=jnp.float32),
        "dp",
        scatter_dimension=0,
        tiled=True,
    )
    loss_total = lax.psum(loss_local, "dp")
    gain_grad = lax.psum(gain_part, ("dp", "fsdp"))
    mean_loss = loss_total / pair_count
    return (mean_loss, query_grad, region_grad, hidden_grad, gain_grad, proj_grad)


def arrange(copies, me):
    n = len(copies)
    source = ((me - jnp.arange(n)) % n).reshape((n,) + (1,) * copies[0].ndim)
    out = jnp.broadcast_to(copies[0][None], (n,) + copies[0].shape)
    for s in range(1, n):
        out = jnp.where(source == s, copies[s][None], out)
    return out


def gather_blocks(x, axis):
    n = lax.axis_size(axis)
    copies = [x] + [
        lax.ppermute(x, axis, [(i, (i + s) % n) for i in range(n)]) for s in range(1, n)
    ]
    return arrange(copies, lax.axis_index(axis))


def sum_blocks(x, axis):
    return jnp.sum(gather_blocks(x, axis), axis=0)


def scatter_sum(whole, axis):
    n = lax.axis_size(axis)
    me = lax.axis_index(axis)
    chunk = whole.shape[1] // n
    copies = [lax.dynamic_slice_in_dim(whole, me * chunk, chunk, axis=1)]
    for s in range(1, n):
        piece = lax.dynamic_slice_in_dim(whole, (me + s) % n * chunk, chunk, axis=1)
        copies.append(lax.ppermute(piece, axis, [(i, (i + s) % n) for i in range(n)]))
    return jnp.sum(arrange(copies, me), axis=0)


def spread_with_sum(total, pieces, axis):
    n = lax.axis_size(axis)
    me = lax.axis_index(axis)
    size = total.shape[0]
    sums = [total]
    got = [lax.dynamic_index_in_dim(pieces, me, axis=0, keepdims=False)]
    for s in range(1, n):
        piece = lax.dynamic_index_in_dim(pieces, (me + s) % n, axis=0, keepdims=False)
        payload = jnp.concatenate([total, piece.reshape(-1)])
        arrived = lax.ppermute(payload, axis, [(i, (i + s) % n) for i in range(n)])
        sums.append(arrived[:size])
        got.append(arrived[size:].reshape(piece.shape))
    return jnp.sum(arrange(sums, me), axis=0), lax.optimization_barrier(arrange(got, me))


def local_small(query_cache, region_cache, positive, hidden_states, segment_ids, norm_gain, proj_weight):
    rows, width = query_cache.shape
    data_count = lax.axis_size("dp")
    feature_count = lax.axis_size("fsdp")
    pair_count = rows * data_count
    tokens = segment_ids.shape[1]
    model_width = hidden_states.shape[1]
    logit_scale = float(E) ** (-0.5)
    contract_last = (((1,), (1,)), ((), ()))
    contract_first = (((0,), (0,)), ((), ()))
    me_dp = lax.axis_index("dp")
    me_f = lax.axis_index("fsdp")

    extra = jnp.concatenate(
        [positive // 64, positive % 64, segment_ids[0]]
    ).astype(jnp.float32)
    extra_rows = -(-extra.shape[0] // width)
    extra = jnp.pad(extra, (0, extra_rows * width - extra.shape[0]))
    packed = jnp.concatenate(
        [query_cache, region_cache, extra.reshape(extra_rows, width).astype(jnp.bfloat16)], axis=0
    )
    group_blocks = gather_blocks(packed, "fsdp")
    group_side = group_blocks[:, 2 * rows :].reshape(feature_count, extra_rows * width)
    group_ids = group_side[:, 2 * rows : 2 * rows + tokens].reshape(feature_count * tokens)
    group_ids = group_ids.astype(jnp.int32)

    gain = norm_gain.astype(jnp.float32)
    states = hidden_states.astype(jnp.float32)
    inv_rms = lax.rsqrt(jnp.mean(states * states, axis=1, keepdims=True) + EPS)
    normed = (states * inv_rms * gain).astype(jnp.bfloat16)
    labels = lax.broadcasted_iota(jnp.int32, (rows, 1), 0)
    member = segment_ids[0][None, :] == labels
    pooled_part = jnp.dot(member.astype(jnp.bfloat16), normed, preferred_element_type=jnp.float32)
    counts = jnp.sum((group_ids[None, :] == labels).astype(jnp.float32), axis=1)
    chunk = model_width // feature_count
    pooled_chunk = scatter_sum(pooled_part, "fsdp")
    mean_chunk = (pooled_chunk / counts[:, None]).astype(jnp.bfloat16)
    mean_blocks = lax.optimization_barrier(gather_blocks(mean_chunk, "fsdp"))
    mean_pooled = mean_blocks.transpose(1, 0, 2).reshape(rows, model_width)

    gathered = gather_blocks(group_blocks, "dp")
    mean_pooled, gathered = lax.optimization_barrier((mean_pooled, gathered))
    slice_width = model_width // data_count
    pieces = mean_pooled.reshape(rows, data_count, slice_width).transpose(1, 0, 2)

    query_all = gathered[:, :, :rows].transpose(0, 2, 1, 3).reshape(pair_count, feature_count * width)
    region_all = gathered[:, :, rows : 2 * rows].transpose(0, 2, 1, 3).reshape(
        pair_count, feature_count * width
    )
    side = gathered[:, :, 2 * rows :].reshape(data_count, feature_count, extra_rows * width)
    side = side.astype(jnp.float32)
    positive_all = (side[:, 0, :rows] * 64 + side[:, 0, rows : 2 * rows]).astype(jnp.int32)
    positive_all = positive_all.reshape(pair_count)

    scores = (
        lax.dot_general(query_all, region_all, contract_last, preferred_element_type=jnp.float32)
        * logit_scale
    )
    row_max = jnp.max(scores, axis=1, keepdims=True)
    log_total = row_max[:, 0] + jnp.log(jnp.sum(jnp.exp(scores - row_max), axis=1))
    columns = lax.broadcasted_iota(jnp.int32, (1, pair_count), 1)
    matched = columns == positive_all[:, None]
    target_score = jnp.sum(jnp.where(matched, scores, jnp.zeros_like(scores)), axis=1)
    mean_loss = jnp.sum(log_total - target_score) / pair_count
    grad_probs = (jnp.exp(scores - log_total[:, None]) - matched.astype(jnp.float32)).astype(
        jnp.bfloat16
    )
    probs_rows = lax.dynamic_slice(grad_probs, (me_dp * rows, 0), (rows, pair_count))
    query_grad_rows = logit_scale * jnp.dot(
        probs_rows, region_all, preferred_element_type=jnp.float32
    )
    query_grad = lax.dynamic_slice(query_grad_rows, (0, me_f * width), (rows, width))
    grad_low = query_grad_rows.astype(jnp.bfloat16)
    region_cols = lax.dynamic_slice(region_all, (0, me_f * width), (pair_count, width))
    grad_low_cols = logit_scale * jnp.dot(grad_probs, region_cols, preferred_element_type=jnp.float32)
    grad_low_cols = grad_low_cols.astype(jnp.bfloat16)
    probs_cols = lax.dynamic_slice(grad_probs, (0, me_dp * rows), (pair_count, rows))
    query_cols = lax.dynamic_slice(query_all, (0, me_f * width), (pair_count, width))
    region_grad = logit_scale * lax.dot_general(
        probs_cols, query_cols, contract_first, preferred_element_type=jnp.float32
    )

    mean_part = lax.dot_general(
        grad_low, proj_weight, contract_last, preferred_element_type=jnp.float32
    )
    mean_grad = lax.all_gather(mean_part, "fsdp", axis=1, tiled=True)
    pool_grad = mean_grad / counts[:, None]
    normed_grad = jnp.take(pool_grad, segment_ids[0], axis=0)
    gain_part = jnp.sum(normed_grad * states * inv_rms, axis=0)
    scaled = gain * normed_grad
    inner = jnp.mean(scaled * states, axis=1, keepdims=True)
    hidden_grad = (inv_rms * scaled - states * inv_rms**3 * inner).astype(jnp.bfloat16)
    gain_dp, pieces = spread_with_sum(gain_part, pieces.astype(jnp.float32), "dp")
    gain_grad = sum_blocks(gain_dp, "fsdp")
    pooled_cols = pieces.reshape(pair_count, slice_width).astype(jnp.bfloat16)
    proj_grad = lax.dot_general(
        pooled_cols, grad_low_cols, contract_first, preferred_element_type=jnp.float32
    )
    return (mean_loss, query_grad, region_grad, hidden_grad, gain_grad, proj_grad)


SMALL_PAIRS = 1024


def local(query_cache, region_cache, positive, hidden_states, segment_ids, norm_gain, proj_weight):
    pair_count = query_cache.shape[0] * lax.axis_size("dp")
    args = (query_cache, region_cache, positive, hidden_states, segment_ids, norm_gain, proj_weight)
    if pair_count <= SMALL_PAIRS:
        return local_small(*args)
    return local_sharded(*args)


def solution(mesh):
    in_specs = (
        P("dp", "fsdp"),
        P("dp", "fsdp"),
        P("dp"),
        P(("dp", "fsdp"), None),
        P("dp", "fsdp"),
        P(),
        P("fsdp", None),
    )
    out_specs = (
        P(),
        P("dp", "fsdp"),
        P("dp", "fsdp"),
        P(("dp", "fsdp"), None),
        P(),
        P("dp", "fsdp"),
    )
    return jax.shard_map(local, mesh=mesh, in_specs=in_specs, out_specs=out_specs, check_vma=False)
```

```python
import jax
import jax.numpy as jnp
from jax import lax
from jax.sharding import PartitionSpec as P

E = 1024


EPS = 1e-05


def local_sharded(query_cache, region_cache, positive, hidden_states, segment_ids, norm_gain, proj_weight):
    row_count = query_cache.shape[0]
    data_count = lax.axis_size("dp")
    pair_count = row_count * data_count
    logit_scale = float(E) ** (-0.5)
    contract_last = (((1,), (1,)), ((), ()))
    contract_first = (((0,), (0,)), ((), ()))
    region_all, query_all = (
        lax.all_gather(region_cache, "dp", axis=0, tiled=True),
        lax.all_gather(query_cache, "dp", axis=0, tiled=True),
    )
    partial_value = lax.dot_general(
        query_cache, region_all, contract_last, preferred_element_type=jnp.float32
    )
    scores = lax.psum(partial_value, "fsdp") * logit_scale
    row_max = jnp.max(scores, axis=1, keepdims=True)
    log_total = row_max[:, 0] + jnp.log(jnp.sum(jnp.exp(scores - row_max), axis=1))
    columns = lax.broadcasted_iota(jnp.int32, (1, pair_count), 1)
    matched = columns == positive[:, None]
    target_score = jnp.sum(jnp.where(matched, scores, jnp.zeros_like(scores)), axis=1)
    loss_local = jnp.sum(log_total - target_score)
    grad_probs = (jnp.exp(scores - log_total[:, None]) - matched.astype(jnp.float32)).astype(
        jnp.bfloat16
    )
    query_grad = logit_scale * jnp.dot(grad_probs, region_all, preferred_element_type=jnp.float32)
    totals_all, targets_all = (
        lax.all_gather(log_total, "dp", axis=0, tiled=True),
        lax.all_gather(positive.astype(jnp.float32), "dp", axis=0, tiled=True),
    )
    partial_t = lax.dot_general(
        region_cache, query_all, contract_last, preferred_element_type=jnp.float32
    )
    scores_t = lax.psum(partial_t, "fsdp") * logit_scale
    own_rows = (
        lax.axis_index("dp") * row_count + lax.broadcasted_iota(jnp.int32, (row_count, 1), 0)
    ).astype(jnp.float32)
    matched_t = targets_all[None, :] == own_rows
    probs_t = (jnp.exp(scores_t - totals_all[None, :]) - matched_t.astype(jnp.float32)).astype(
        jnp.bfloat16
    )
    region_grad = logit_scale * jnp.dot(probs_t, query_all, preferred_element_type=jnp.float32)
    gain = norm_gain.astype(jnp.float32)
    states = hidden_states.astype(jnp.float32)
    inv_rms = lax.rsqrt(jnp.mean(states * states, axis=1, keepdims=True) + EPS)
    normed = (states * inv_rms * gain).astype(jnp.bfloat16)
    labels = lax.broadcasted_iota(jnp.int32, (row_count, 1), 0)
    member = segment_ids[0][None, :] == labels
    pooled_part = jnp.dot(member.astype(jnp.bfloat16), normed, preferred_element_type=jnp.float32)
    counts_part = jnp.sum(member.astype(jnp.float32), axis=1)
    pooled, counts = lax.psum((pooled_part, counts_part), "fsdp")
    mean_pooled = (pooled / counts[:, None]).astype(jnp.bfloat16)
    grad_low = query_grad.astype(jnp.bfloat16)
    grad_full = lax.all_gather(grad_low, "fsdp", axis=1, tiled=True)
    mean_part = lax.dot_general(
        grad_full, proj_weight, contract_last, preferred_element_type=jnp.float32
    )
    mean_grad = lax.all_gather(mean_part, "fsdp", axis=1, tiled=True)
    pool_grad = mean_grad / counts[:, None]
    normed_grad = lax.dot_general(
        member.astype(jnp.float32),
        pool_grad,
        contract_first,
        precision=lax.Precision.HIGHEST,
        preferred_element_type=jnp.float32,
    )
    gain_part = jnp.sum(normed_grad * states * inv_rms, axis=0)
    scaled = gain * normed_grad
    inner = jnp.mean(scaled * states, axis=1, keepdims=True)
    hidden_grad = (inv_rms * scaled - states * inv_rms**3 * inner).astype(jnp.bfloat16)
    proj_grad = lax.psum_scatter(
        lax.dot_general(mean_pooled, grad_low, contract_first, preferred_element_type=jnp.float32),
        "dp",
        scatter_dimension=0,
        tiled=True,
    )
    loss_total = lax.psum(loss_local, "dp")
    gain_grad = lax.psum(gain_part, ("dp", "fsdp"))
    mean_loss = loss_total / pair_count
    return (mean_loss, query_grad, region_grad, hidden_grad, gain_grad, proj_grad)


def arrange(copies, me):
    n = len(copies)
    source = ((me - jnp.arange(n)) % n).reshape((n,) + (1,) * copies[0].ndim)
    out = jnp.broadcast_to(copies[0][None], (n,) + copies[0].shape)
    for s in range(1, n):
        out = jnp.where(source == s, copies[s][None], out)
    return out


def gather_blocks(x, axis):
    n = lax.axis_size(axis)
    copies = [x] + [
        lax.ppermute(x, axis, [(i, (i + s) % n) for i in range(n)]) for s in range(1, n)
    ]
    return arrange(copies, lax.axis_index(axis))


def sum_blocks(x, axis):
    return jnp.sum(gather_blocks(x, axis), axis=0)


def scatter_sum(whole, axis):
    n = lax.axis_size(axis)
    me = lax.axis_index(axis)
    chunk = whole.shape[1] // n
    copies = [lax.dynamic_slice_in_dim(whole, me * chunk, chunk, axis=1)]
    for s in range(1, n):
        piece = lax.dynamic_slice_in_dim(whole, (me + s) % n * chunk, chunk, axis=1)
        copies.append(lax.ppermute(piece, axis, [(i, (i + s) % n) for i in range(n)]))
    return jnp.sum(arrange(copies, me), axis=0)


def spread_with_sum(total, pieces, axis):
    n = lax.axis_size(axis)
    me = lax.axis_index(axis)
    size = total.shape[0]
    sums = [total]
    got = [lax.dynamic_index_in_dim(pieces, me, axis=0, keepdims=False)]
    for s in range(1, n):
        piece = lax.dynamic_index_in_dim(pieces, (me + s) % n, axis=0, keepdims=False)
        payload = jnp.concatenate([total, piece.reshape(-1)])
        arrived = lax.ppermute(payload, axis, [(i, (i + s) % n) for i in range(n)])
        sums.append(arrived[:size])
        got.append(arrived[size:].reshape(piece.shape))
    return jnp.sum(arrange(sums, me), axis=0), lax.optimization_barrier(arrange(got, me))


def local_small(query_cache, region_cache, positive, hidden_states, segment_ids, norm_gain, proj_weight):
    rows, width = query_cache.shape
    data_count = lax.axis_size("dp")
    feature_count = lax.axis_size("fsdp")
    pair_count = rows * data_count
    tokens = segment_ids.shape[1]
    model_width = hidden_states.shape[1]
    logit_scale = float(E) ** (-0.5)
    contract_last = (((1,), (1,)), ((), ()))
    contract_first = (((0,), (0,)), ((), ()))
    me_dp = lax.axis_index("dp")
    me_f = lax.axis_index("fsdp")

    extra = jnp.concatenate(
        [positive // 64, positive % 64, segment_ids[0]]
    ).astype(jnp.float32)
    extra_rows = -(-extra.shape[0] // width)
    extra = jnp.pad(extra, (0, extra_rows * width - extra.shape[0]))
    packed = jnp.concatenate(
        [query_cache, region_cache, extra.reshape(extra_rows, width).astype(jnp.bfloat16)], axis=0
    )
    group_blocks = gather_blocks(packed, "fsdp")
    group_side = group_blocks[:, 2 * rows :].reshape(feature_count, extra_rows * width)
    group_ids = group_side[:, 2 * rows : 2 * rows + tokens].reshape(feature_count * tokens)
    group_ids = group_ids.astype(jnp.int32)

    gain = norm_gain.astype(jnp.float32)
    states = hidden_states.astype(jnp.float32)
    inv_rms = lax.rsqrt(jnp.mean(states * states, axis=1, keepdims=True) + EPS)
    normed = (states * inv_rms * gain).astype(jnp.bfloat16)
    labels = lax.broadcasted_iota(jnp.int32, (rows, 1), 0)
    member = segment_ids[0][None, :] == labels
    pooled_part = jnp.dot(member.astype(jnp.bfloat16), normed, preferred_element_type=jnp.float32)
    counts = jnp.sum((group_ids[None, :] == labels).astype(jnp.float32), axis=1)
    chunk = model_width // feature_count
    pooled_chunk = scatter_sum(pooled_part, "fsdp")
    mean_chunk = (pooled_chunk / counts[:, None]).astype(jnp.bfloat16)
    mean_blocks = lax.optimization_barrier(gather_blocks(mean_chunk, "fsdp"))
    mean_pooled = mean_blocks.transpose(1, 0, 2).reshape(rows, model_width)

    gathered = gather_blocks(group_blocks, "dp")
    mean_pooled, gathered = lax.optimization_barrier((mean_pooled, gathered))
    slice_width = model_width // data_count
    pieces = mean_pooled.reshape(rows, data_count, slice_width).transpose(1, 0, 2)

    query_all = gathered[:, :, :rows].transpose(0, 2, 1, 3).reshape(pair_count, feature_count * width)
    region_all = gathered[:, :, rows : 2 * rows].transpose(0, 2, 1, 3).reshape(
        pair_count, feature_count * width
    )
    side = gathered[:, :, 2 * rows :].reshape(data_count, feature_count, extra_rows * width)
    side = side.astype(jnp.float32)
    positive_all = (side[:, 0, :rows] * 64 + side[:, 0, rows : 2 * rows]).astype(jnp.int32)
    positive_all = positive_all.reshape(pair_count)

    scores = (
        lax.dot_general(query_all, region_all, contract_last, preferred_element_type=jnp.float32)
        * logit_scale
    )
    row_max = jnp.max(scores, axis=1, keepdims=True)
    log_total = row_max[:, 0] + jnp.log(jnp.sum(jnp.exp(scores - row_max), axis=1))
    columns = lax.broadcasted_iota(jnp.int32, (1, pair_count), 1)
    matched = columns == positive_all[:, None]
    target_score = jnp.sum(jnp.where(matched, scores, jnp.zeros_like(scores)), axis=1)
    mean_loss = jnp.sum(log_total - target_score) / pair_count
    grad_probs = (jnp.exp(scores - log_total[:, None]) - matched.astype(jnp.float32)).astype(
        jnp.bfloat16
    )
    probs_rows = lax.dynamic_slice(grad_probs, (me_dp * rows, 0), (rows, pair_count))
    query_grad_rows = logit_scale * jnp.dot(
        probs_rows, region_all, preferred_element_type=jnp.float32
    )
    query_grad = lax.dynamic_slice(query_grad_rows, (0, me_f * width), (rows, width))
    grad_low = query_grad_rows.astype(jnp.bfloat16)
    region_cols = lax.dynamic_slice(region_all, (0, me_f * width), (pair_count, width))
    grad_low_cols = logit_scale * jnp.dot(grad_probs, region_cols, preferred_element_type=jnp.float32)
    grad_low_cols = grad_low_cols.astype(jnp.bfloat16)
    probs_cols = lax.dynamic_slice(grad_probs, (0, me_dp * rows), (pair_count, rows))
    query_cols = lax.dynamic_slice(query_all, (0, me_f * width), (pair_count, width))
    region_grad = logit_scale * lax.dot_general(
        probs_cols, query_cols, contract_first, preferred_element_type=jnp.float32
    )

    mean_part = lax.dot_general(
        grad_low, proj_weight, contract_last, preferred_element_type=jnp.float32
    )
    mean_grad = lax.all_gather(mean_part, "fsdp", axis=1, tiled=True)
    pool_grad = mean_grad / counts[:, None]
    normed_grad = lax.dot_general(
        member.astype(jnp.float32),
        pool_grad,
        contract_first,
        precision=lax.Precision.HIGHEST,
        preferred_element_type=jnp.float32,
    )
    gain_part = jnp.sum(normed_grad * states * inv_rms, axis=0)
    scaled = gain * normed_grad
    inner = jnp.mean(scaled * states, axis=1, keepdims=True)
    hidden_grad = (inv_rms * scaled - states * inv_rms**3 * inner).astype(jnp.bfloat16)
    gain_dp, pieces = spread_with_sum(gain_part, pieces.astype(jnp.float32), "dp")
    gain_grad = sum_blocks(gain_dp, "fsdp")
    pooled_cols = pieces.reshape(pair_count, slice_width).astype(jnp.bfloat16)
    proj_grad = lax.dot_general(
        pooled_cols, grad_low_cols, contract_first, preferred_element_type=jnp.float32
    )
    return (mean_loss, query_grad, region_grad, hidden_grad, gain_grad, proj_grad)


SMALL_PAIRS = 1024


def local(query_cache, region_cache, positive, hidden_states, segment_ids, norm_gain, proj_weight):
    pair_count = query_cache.shape[0] * lax.axis_size("dp")
    args = (query_cache, region_cache, positive, hidden_states, segment_ids, norm_gain, proj_weight)
    if pair_count <= SMALL_PAIRS:
        return local_small(*args)
    return local_sharded(*args)


def solution(mesh):
    in_specs = (
        P("dp", "fsdp"),
        P("dp", "fsdp"),
        P("dp"),
        P(("dp", "fsdp"), None),
        P("dp", "fsdp"),
        P(),
        P("fsdp", None),
    )
    out_specs = (
        P(),
        P("dp", "fsdp"),
        P("dp", "fsdp"),
        P(("dp", "fsdp"), None),
        P(),
        P("dp", "fsdp"),
    )
    return jax.shard_map(local, mesh=mesh, in_specs=in_specs, out_specs=out_specs, check_vma=False)
```

```python
import jax
import jax.numpy as jnp
from jax import lax
from jax.sharding import PartitionSpec as P

E = 1024


EPS = 1e-05


def local_sharded(query_cache, region_cache, positive, hidden_states, segment_ids, norm_gain, proj_weight):
    row_count = query_cache.shape[0]
    data_count = lax.axis_size("dp")
    pair_count = row_count * data_count
    logit_scale = float(E) ** (-0.5)
    contract_last = (((1,), (1,)), ((), ()))
    contract_first = (((0,), (0,)), ((), ()))
    region_all, query_all = (
        lax.all_gather(region_cache, "dp", axis=0, tiled=True),
        lax.all_gather(query_cache, "dp", axis=0, tiled=True),
    )
    partial_value = lax.dot_general(
        query_cache, region_all, contract_last, preferred_element_type=jnp.float32
    )
    scores = lax.psum(partial_value, "fsdp") * logit_scale
    row_max = jnp.max(scores, axis=1, keepdims=True)
    log_total = row_max[:, 0] + jnp.log(jnp.sum(jnp.exp(scores - row_max), axis=1))
    columns = lax.broadcasted_iota(jnp.int32, (1, pair_count), 1)
    matched = columns == positive[:, None]
    target_score = jnp.sum(jnp.where(matched, scores, jnp.zeros_like(scores)), axis=1)
    loss_local = jnp.sum(log_total - target_score)
    grad_probs = (jnp.exp(scores - log_total[:, None]) - matched.astype(jnp.float32)).astype(
        jnp.bfloat16
    )
    query_grad = logit_scale * jnp.dot(grad_probs, region_all, preferred_element_type=jnp.float32)
    totals_all, targets_all = (
        lax.all_gather(log_total, "dp", axis=0, tiled=True),
        lax.all_gather(positive.astype(jnp.float32), "dp", axis=0, tiled=True),
    )
    partial_t = lax.dot_general(
        region_cache, query_all, contract_last, preferred_element_type=jnp.float32
    )
    scores_t = lax.psum(partial_t, "fsdp") * logit_scale
    own_rows = (
        lax.axis_index("dp") * row_count + lax.broadcasted_iota(jnp.int32, (row_count, 1), 0)
    ).astype(jnp.float32)
    matched_t = targets_all[None, :] == own_rows
    probs_t = (jnp.exp(scores_t - totals_all[None, :]) - matched_t.astype(jnp.float32)).astype(
        jnp.bfloat16
    )
    region_grad = logit_scale * jnp.dot(probs_t, query_all, preferred_element_type=jnp.float32)
    gain = norm_gain.astype(jnp.float32)
    states = hidden_states.astype(jnp.float32)
    inv_rms = lax.rsqrt(jnp.mean(states * states, axis=1, keepdims=True) + EPS)
    normed = (states * inv_rms * gain).astype(jnp.bfloat16)
    labels = lax.broadcasted_iota(jnp.int32, (row_count, 1), 0)
    member = segment_ids[0][None, :] == labels
    pooled_part = jnp.dot(member.astype(jnp.bfloat16), normed, preferred_element_type=jnp.float32)
    counts_part = jnp.sum(member.astype(jnp.float32), axis=1)
    pooled, counts = lax.psum((pooled_part, counts_part), "fsdp")
    mean_pooled = (pooled / counts[:, None]).astype(jnp.bfloat16)
    grad_low = query_grad.astype(jnp.bfloat16)
    grad_full = lax.all_gather(grad_low, "fsdp", axis=1, tiled=True)
    mean_part = lax.dot_general(
        grad_full, proj_weight, contract_last, preferred_element_type=jnp.float32
    )
    mean_grad = lax.all_gather(mean_part, "fsdp", axis=1, tiled=True)
    pool_grad = mean_grad / counts[:, None]
    normed_grad = lax.dot_general(
        member.astype(jnp.float32),
        pool_grad,
        contract_first,
        precision=lax.Precision.HIGHEST,
        preferred_element_type=jnp.float32,
    )
    gain_part = jnp.sum(normed_grad * states * inv_rms, axis=0)
    scaled = gain * normed_grad
    inner = jnp.mean(scaled * states, axis=1, keepdims=True)
    hidden_grad = (inv_rms * scaled - states * inv_rms**3 * inner).astype(jnp.bfloat16)
    proj_grad = lax.psum_scatter(
        lax.dot_general(mean_pooled, grad_low, contract_first, preferred_element_type=jnp.float32),
        "dp",
        scatter_dimension=0,
        tiled=True,
    )
    loss_total = lax.psum(loss_local, "dp")
    gain_grad = lax.psum(gain_part, ("dp", "fsdp"))
    mean_loss = loss_total / pair_count
    return (mean_loss, query_grad, region_grad, hidden_grad, gain_grad, proj_grad)


def arrange(copies, me):
    n = len(copies)
    source = ((me - jnp.arange(n)) % n).reshape((n,) + (1,) * copies[0].ndim)
    out = jnp.broadcast_to(copies[0][None], (n,) + copies[0].shape)
    for s in range(1, n):
        out = jnp.where(source == s, copies[s][None], out)
    return out


def gather_blocks(x, axis):
    n = lax.axis_size(axis)
    copies = [x] + [
        lax.ppermute(x, axis, [(i, (i + s) % n) for i in range(n)]) for s in range(1, n)
    ]
    return arrange(copies, lax.axis_index(axis))


def sum_blocks(x, axis):
    return jnp.sum(gather_blocks(x, axis), axis=0)


def scatter_sum(whole, axis):
    n = lax.axis_size(axis)
    me = lax.axis_index(axis)
    chunk = whole.shape[1] // n
    copies = [lax.dynamic_slice_in_dim(whole, me * chunk, chunk, axis=1)]
    for s in range(1, n):
        piece = lax.dynamic_slice_in_dim(whole, (me + s) % n * chunk, chunk, axis=1)
        copies.append(lax.ppermute(piece, axis, [(i, (i + s) % n) for i in range(n)]))
    return jnp.sum(arrange(copies, me), axis=0)


def spread_with_sum(total, pieces, axis):
    n = lax.axis_size(axis)
    me = lax.axis_index(axis)
    size = total.shape[0]
    sums = [total]
    got = [lax.dynamic_index_in_dim(pieces, me, axis=0, keepdims=False)]
    for s in range(1, n):
        piece = lax.dynamic_index_in_dim(pieces, (me + s) % n, axis=0, keepdims=False)
        payload = jnp.concatenate([total, piece.reshape(-1)])
        arrived = lax.ppermute(payload, axis, [(i, (i + s) % n) for i in range(n)])
        sums.append(arrived[:size])
        got.append(arrived[size:].reshape(piece.shape))
    return jnp.sum(arrange(sums, me), axis=0), lax.optimization_barrier(arrange(got, me))


def local_small(query_cache, region_cache, positive, hidden_states, segment_ids, norm_gain, proj_weight):
    rows, width = query_cache.shape
    data_count = lax.axis_size("dp")
    feature_count = lax.axis_size("fsdp")
    pair_count = rows * data_count
    tokens = segment_ids.shape[1]
    model_width = hidden_states.shape[1]
    logit_scale = float(E) ** (-0.5)
    contract_last = (((1,), (1,)), ((), ()))
    contract_first = (((0,), (0,)), ((), ()))
    me_dp = lax.axis_index("dp")
    me_f = lax.axis_index("fsdp")

    extra = jnp.concatenate(
        [positive // 64, positive % 64, segment_ids[0]]
    ).astype(jnp.float32)
    extra_rows = -(-extra.shape[0] // width)
    extra = jnp.pad(extra, (0, extra_rows * width - extra.shape[0]))
    packed = jnp.concatenate(
        [query_cache, region_cache, extra.reshape(extra_rows, width).astype(jnp.bfloat16)], axis=0
    )
    group_blocks = gather_blocks(packed, "fsdp")
    group_side = group_blocks[:, 2 * rows :].reshape(feature_count, extra_rows * width)
    group_ids = group_side[:, 2 * rows : 2 * rows + tokens].reshape(feature_count * tokens)
    group_ids = group_ids.astype(jnp.int32)

    gain = norm_gain.astype(jnp.float32)
    states = hidden_states.astype(jnp.float32)
    inv_rms = lax.rsqrt(jnp.mean(states * states, axis=1, keepdims=True) + EPS)
    normed = (states * inv_rms * gain).astype(jnp.bfloat16)
    labels = lax.broadcasted_iota(jnp.int32, (rows, 1), 0)
    member = segment_ids[0][None, :] == labels
    pooled_part = jnp.dot(member.astype(jnp.bfloat16), normed, preferred_element_type=jnp.float32)
    counts = jnp.sum((group_ids[None, :] == labels).astype(jnp.float32), axis=1)
    chunk = model_width // feature_count
    pooled_chunk = scatter_sum(pooled_part, "fsdp")
    mean_chunk = (pooled_chunk / counts[:, None]).astype(jnp.bfloat16)
    mean_blocks = lax.optimization_barrier(gather_blocks(mean_chunk, "fsdp"))
    mean_pooled = mean_blocks.transpose(1, 0, 2).reshape(rows, model_width)

    gathered = gather_blocks(group_blocks, "dp")
    slice_width = model_width // data_count
    pieces = mean_pooled.reshape(rows, data_count, slice_width).transpose(1, 0, 2)

    query_all = gathered[:, :, :rows].transpose(0, 2, 1, 3).reshape(pair_count, feature_count * width)
    region_all = gathered[:, :, rows : 2 * rows].transpose(0, 2, 1, 3).reshape(
        pair_count, feature_count * width
    )
    side = gathered[:, :, 2 * rows :].reshape(data_count, feature_count, extra_rows * width)
    side = side.astype(jnp.float32)
    positive_all = (side[:, 0, :rows] * 64 + side[:, 0, rows : 2 * rows]).astype(jnp.int32)
    positive_all = positive_all.reshape(pair_count)

    scores = (
        lax.dot_general(query_all, region_all, contract_last, preferred_element_type=jnp.float32)
        * logit_scale
    )
    row_max = jnp.max(scores, axis=1, keepdims=True)
    log_total = row_max[:, 0] + jnp.log(jnp.sum(jnp.exp(scores - row_max), axis=1))
    columns = lax.broadcasted_iota(jnp.int32, (1, pair_count), 1)
    matched = columns == positive_all[:, None]
    target_score = jnp.sum(jnp.where(matched, scores, jnp.zeros_like(scores)), axis=1)
    mean_loss = jnp.sum(log_total - target_score) / pair_count
    grad_probs = (jnp.exp(scores - log_total[:, None]) - matched.astype(jnp.float32)).astype(
        jnp.bfloat16
    )
    query_grad_all = logit_scale * jnp.dot(grad_probs, region_all, preferred_element_type=jnp.float32)
    query_grad = lax.dynamic_slice(query_grad_all, (me_dp * rows, me_f * width), (rows, width))
    grad_low = lax.dynamic_slice(query_grad_all, (me_dp * rows, 0), (rows, feature_count * width))
    grad_low = grad_low.astype(jnp.bfloat16)
    grad_low_cols = lax.dynamic_slice(query_grad_all, (0, me_f * width), (pair_count, width))
    grad_low_cols = grad_low_cols.astype(jnp.bfloat16)
    probs_cols = lax.dynamic_slice(grad_probs, (0, me_dp * rows), (pair_count, rows))
    query_cols = lax.dynamic_slice(query_all, (0, me_f * width), (pair_count, width))
    region_grad = logit_scale * lax.dot_general(
        probs_cols, query_cols, contract_first, preferred_element_type=jnp.float32
    )

    mean_part = lax.dot_general(
        grad_low, proj_weight, contract_last, preferred_element_type=jnp.float32
    )
    mean_part, mean_pooled = lax.optimization_barrier((mean_part, mean_pooled))
    mean_grad = lax.all_gather(mean_part, "fsdp", axis=1, tiled=True)
    pool_grad = mean_grad / counts[:, None]
    normed_grad = lax.dot_general(
        member.astype(jnp.float32),
        pool_grad,
        contract_first,
        precision=lax.Precision.HIGHEST,
        preferred_element_type=jnp.float32,
    )
    gain_part = jnp.sum(normed_grad * states * inv_rms, axis=0)
    scaled = gain * normed_grad
    inner = jnp.mean(scaled * states, axis=1, keepdims=True)
    hidden_grad = (inv_rms * scaled - states * inv_rms**3 * inner).astype(jnp.bfloat16)
    gain_dp, pieces = spread_with_sum(gain_part, pieces.astype(jnp.float32), "dp")
    gain_grad = sum_blocks(gain_dp, "fsdp")
    pooled_cols = pieces.reshape(pair_count, slice_width).astype(jnp.bfloat16)
    proj_grad = lax.dot_general(
        pooled_cols, grad_low_cols, contract_first, preferred_element_type=jnp.float32
    )
    return (mean_loss, query_grad, region_grad, hidden_grad, gain_grad, proj_grad)


SMALL_PAIRS = 1024


def local(query_cache, region_cache, positive, hidden_states, segment_ids, norm_gain, proj_weight):
    pair_count = query_cache.shape[0] * lax.axis_size("dp")
    args = (query_cache, region_cache, positive, hidden_states, segment_ids, norm_gain, proj_weight)
    if pair_count <= SMALL_PAIRS:
        return local_small(*args)
    return local_sharded(*args)


def solution(mesh):
    in_specs = (
        P("dp", "fsdp"),
        P("dp", "fsdp"),
        P("dp"),
        P(("dp", "fsdp"), None),
        P("dp", "fsdp"),
        P(),
        P("fsdp", None),
    )
    out_specs = (
        P(),
        P("dp", "fsdp"),
        P("dp", "fsdp"),
        P(("dp", "fsdp"), None),
        P(),
        P("dp", "fsdp"),
    )
    return jax.shard_map(local, mesh=mesh, in_specs=in_specs, out_specs=out_specs, check_vma=False)
```

```python
import jax
import jax.numpy as jnp
from jax import lax
from jax.sharding import PartitionSpec as P

E = 1024


EPS = 1e-05


def local_sharded(query_cache, region_cache, positive, hidden_states, segment_ids, norm_gain, proj_weight):
    row_count = query_cache.shape[0]
    data_count = lax.axis_size("dp")
    pair_count = row_count * data_count
    logit_scale = float(E) ** (-0.5)
    contract_last = (((1,), (1,)), ((), ()))
    contract_first = (((0,), (0,)), ((), ()))
    region_all, query_all = (
        lax.all_gather(region_cache, "dp", axis=0, tiled=True),
        lax.all_gather(query_cache, "dp", axis=0, tiled=True),
    )
    partial_value = lax.dot_general(
        query_cache, region_all, contract_last, preferred_element_type=jnp.float32
    )
    scores = lax.psum(partial_value, "fsdp") * logit_scale
    row_max = jnp.max(scores, axis=1, keepdims=True)
    log_total = row_max[:, 0] + jnp.log(jnp.sum(jnp.exp(scores - row_max), axis=1))
    columns = lax.broadcasted_iota(jnp.int32, (1, pair_count), 1)
    matched = columns == positive[:, None]
    target_score = jnp.sum(jnp.where(matched, scores, jnp.zeros_like(scores)), axis=1)
    loss_local = jnp.sum(log_total - target_score)
    grad_probs = (jnp.exp(scores - log_total[:, None]) - matched.astype(jnp.float32)).astype(
        jnp.bfloat16
    )
    query_grad = logit_scale * jnp.dot(grad_probs, region_all, preferred_element_type=jnp.float32)
    totals_all, targets_all = (
        lax.all_gather(log_total, "dp", axis=0, tiled=True),
        lax.all_gather(positive.astype(jnp.float32), "dp", axis=0, tiled=True),
    )
    partial_t = lax.dot_general(
        region_cache, query_all, contract_last, preferred_element_type=jnp.float32
    )
    scores_t = lax.psum(partial_t, "fsdp") * logit_scale
    own_rows = (
        lax.axis_index("dp") * row_count + lax.broadcasted_iota(jnp.int32, (row_count, 1), 0)
    ).astype(jnp.float32)
    matched_t = targets_all[None, :] == own_rows
    probs_t = (jnp.exp(scores_t - totals_all[None, :]) - matched_t.astype(jnp.float32)).astype(
        jnp.bfloat16
    )
    region_grad = logit_scale * jnp.dot(probs_t, query_all, preferred_element_type=jnp.float32)
    gain = norm_gain.astype(jnp.float32)
    states = hidden_states.astype(jnp.float32)
    inv_rms = lax.rsqrt(jnp.mean(states * states, axis=1, keepdims=True) + EPS)
    normed = (states * inv_rms * gain).astype(jnp.bfloat16)
    labels = lax.broadcasted_iota(jnp.int32, (row_count, 1), 0)
    member = segment_ids[0][None, :] == labels
    pooled_part = jnp.dot(member.astype(jnp.bfloat16), normed, preferred_element_type=jnp.float32)
    counts_part = jnp.sum(member.astype(jnp.float32), axis=1)
    pooled, counts = lax.psum((pooled_part, counts_part), "fsdp")
    mean_pooled = (pooled / counts[:, None]).astype(jnp.bfloat16)
    grad_low = query_grad.astype(jnp.bfloat16)
    grad_full = lax.all_gather(grad_low, "fsdp", axis=1, tiled=True)
    mean_part = lax.dot_general(
        grad_full, proj_weight, contract_last, preferred_element_type=jnp.float32
    )
    mean_grad = lax.all_gather(mean_part, "fsdp", axis=1, tiled=True)
    pool_grad = mean_grad / counts[:, None]
    normed_grad = lax.dot_general(
        member.astype(jnp.float32),
        pool_grad,
        contract_first,
        precision=lax.Precision.HIGHEST,
        preferred_element_type=jnp.float32,
    )
    gain_part = jnp.sum(normed_grad * states * inv_rms, axis=0)
    scaled = gain * normed_grad
    inner = jnp.mean(scaled * states, axis=1, keepdims=True)
    hidden_grad = (inv_rms * scaled - states * inv_rms**3 * inner).astype(jnp.bfloat16)
    proj_grad = lax.psum_scatter(
        lax.dot_general(mean_pooled, grad_low, contract_first, preferred_element_type=jnp.float32),
        "dp",
        scatter_dimension=0,
        tiled=True,
    )
    loss_total = lax.psum(loss_local, "dp")
    gain_grad = lax.psum(gain_part, ("dp", "fsdp"))
    mean_loss = loss_total / pair_count
    return (mean_loss, query_grad, region_grad, hidden_grad, gain_grad, proj_grad)


def arrange(copies, me):
    n = len(copies)
    source = ((me - jnp.arange(n)) % n).reshape((n,) + (1,) * copies[0].ndim)
    out = jnp.broadcast_to(copies[0][None], (n,) + copies[0].shape)
    for s in range(1, n):
        out = jnp.where(source == s, copies[s][None], out)
    return out


def gather_blocks(x, axis):
    n = lax.axis_size(axis)
    copies = [x] + [
        lax.ppermute(x, axis, [(i, (i + s) % n) for i in range(n)]) for s in range(1, n)
    ]
    return arrange(copies, lax.axis_index(axis))


def sum_blocks(x, axis):
    return jnp.sum(gather_blocks(x, axis), axis=0)


def scatter_sum(whole, axis):
    n = lax.axis_size(axis)
    me = lax.axis_index(axis)
    chunk = whole.shape[1] // n
    copies = [lax.dynamic_slice_in_dim(whole, me * chunk, chunk, axis=1)]
    for s in range(1, n):
        piece = lax.dynamic_slice_in_dim(whole, (me + s) % n * chunk, chunk, axis=1)
        copies.append(lax.ppermute(piece, axis, [(i, (i + s) % n) for i in range(n)]))
    return jnp.sum(arrange(copies, me), axis=0)


def spread_with_sum(total, pieces, axis):
    n = lax.axis_size(axis)
    me = lax.axis_index(axis)
    size = total.shape[0]
    sums = [total]
    got = [lax.dynamic_index_in_dim(pieces, me, axis=0, keepdims=False)]
    for s in range(1, n):
        piece = lax.dynamic_index_in_dim(pieces, (me + s) % n, axis=0, keepdims=False)
        payload = jnp.concatenate([total, piece.reshape(-1)])
        arrived = lax.ppermute(payload, axis, [(i, (i + s) % n) for i in range(n)])
        sums.append(arrived[:size])
        got.append(arrived[size:].reshape(piece.shape))
    return jnp.sum(arrange(sums, me), axis=0), lax.optimization_barrier(arrange(got, me))


def local_small(query_cache, region_cache, positive, hidden_states, segment_ids, norm_gain, proj_weight):
    rows, width = query_cache.shape
    data_count = lax.axis_size("dp")
    feature_count = lax.axis_size("fsdp")
    pair_count = rows * data_count
    tokens = segment_ids.shape[1]
    model_width = hidden_states.shape[1]
    logit_scale = float(E) ** (-0.5)
    contract_last = (((1,), (1,)), ((), ()))
    contract_first = (((0,), (0,)), ((), ()))
    me_dp = lax.axis_index("dp")
    me_f = lax.axis_index("fsdp")

    extra = jnp.concatenate(
        [positive // 64, positive % 64, segment_ids[0]]
    ).astype(jnp.float32)
    extra_rows = -(-extra.shape[0] // width)
    extra = jnp.pad(extra, (0, extra_rows * width - extra.shape[0]))
    packed = jnp.concatenate(
        [query_cache, region_cache, extra.reshape(extra_rows, width).astype(jnp.bfloat16)], axis=0
    )
    group_blocks = lax.optimization_barrier(gather_blocks(packed, "fsdp"))
    group_side = group_blocks[:, 2 * rows :].reshape(feature_count, extra_rows * width)
    group_ids = group_side[:, 2 * rows : 2 * rows + tokens].reshape(feature_count * tokens)
    group_ids = group_ids.astype(jnp.int32)

    gain = norm_gain.astype(jnp.float32)
    states = hidden_states.astype(jnp.float32)
    inv_rms = lax.rsqrt(jnp.mean(states * states, axis=1, keepdims=True) + EPS)
    normed = (states * inv_rms * gain).astype(jnp.bfloat16)
    labels = lax.broadcasted_iota(jnp.int32, (rows, 1), 0)
    member = segment_ids[0][None, :] == labels
    pooled_part = jnp.dot(member.astype(jnp.bfloat16), normed, preferred_element_type=jnp.float32)
    counts = jnp.sum((group_ids[None, :] == labels).astype(jnp.float32), axis=1)
    chunk = model_width // feature_count
    pooled_chunk = scatter_sum(pooled_part, "fsdp")
    mean_chunk = (pooled_chunk / counts[:, None]).astype(jnp.bfloat16)
    mean_blocks = lax.optimization_barrier(gather_blocks(mean_chunk, "fsdp"))
    mean_pooled = mean_blocks.transpose(1, 0, 2).reshape(rows, model_width)

    gathered = lax.optimization_barrier(gather_blocks(group_blocks, "dp"))
    mean_pooled, gathered = lax.optimization_barrier((mean_pooled, gathered))
    slice_width = model_width // data_count
    pieces = mean_pooled.reshape(rows, data_count, slice_width).transpose(1, 0, 2)

    query_all = gathered[:, :, :rows].transpose(0, 2, 1, 3).reshape(pair_count, feature_count * width)
    region_all = gathered[:, :, rows : 2 * rows].transpose(0, 2, 1, 3).reshape(
        pair_count, feature_count * width
    )
    side = gathered[:, :, 2 * rows :].reshape(data_count, feature_count, extra_rows * width)
    side = side.astype(jnp.float32)
    positive_all = (side[:, 0, :rows] * 64 + side[:, 0, rows : 2 * rows]).astype(jnp.int32)
    positive_all = positive_all.reshape(pair_count)

    scores = (
        lax.dot_general(query_all, region_all, contract_last, preferred_element_type=jnp.float32)
        * logit_scale
    )
    row_max = jnp.max(scores, axis=1, keepdims=True)
    log_total = row_max[:, 0] + jnp.log(jnp.sum(jnp.exp(scores - row_max), axis=1))
    columns = lax.broadcasted_iota(jnp.int32, (1, pair_count), 1)
    matched = columns == positive_all[:, None]
    target_score = jnp.sum(jnp.where(matched, scores, jnp.zeros_like(scores)), axis=1)
    mean_loss = jnp.sum(log_total - target_score) / pair_count
    grad_probs = (jnp.exp(scores - log_total[:, None]) - matched.astype(jnp.float32)).astype(
        jnp.bfloat16
    )
    query_grad_all = logit_scale * jnp.dot(grad_probs, region_all, preferred_element_type=jnp.float32)
    query_grad = lax.dynamic_slice(query_grad_all, (me_dp * rows, me_f * width), (rows, width))
    grad_low = lax.dynamic_slice(query_grad_all, (me_dp * rows, 0), (rows, feature_count * width))
    grad_low = grad_low.astype(jnp.bfloat16)
    grad_low_cols = lax.dynamic_slice(query_grad_all, (0, me_f * width), (pair_count, width))
    grad_low_cols = grad_low_cols.astype(jnp.bfloat16)
    probs_cols = lax.dynamic_slice(grad_probs, (0, me_dp * rows), (pair_count, rows))
    query_cols = lax.dynamic_slice(query_all, (0, me_f * width), (pair_count, width))
    region_grad = logit_scale * lax.dot_general(
        probs_cols, query_cols, contract_first, preferred_element_type=jnp.float32
    )

    mean_part = lax.dot_general(
        grad_low, proj_weight, contract_last, preferred_element_type=jnp.float32
    )
    mean_grad = lax.all_gather(mean_part, "fsdp", axis=1, tiled=True)
    pool_grad = mean_grad / counts[:, None]
    normed_grad = lax.dot_general(
        member.astype(jnp.float32),
        pool_grad,
        contract_first,
        precision=lax.Precision.HIGHEST,
        preferred_element_type=jnp.float32,
    )
    gain_part = jnp.sum(normed_grad * states * inv_rms, axis=0)
    scaled = gain * normed_grad
    inner = jnp.mean(scaled * states, axis=1, keepdims=True)
    hidden_grad = (inv_rms * scaled - states * inv_rms**3 * inner).astype(jnp.bfloat16)
    gain_dp, pieces = spread_with_sum(gain_part, pieces.astype(jnp.float32), "dp")
    gain_grad = sum_blocks(gain_dp, "fsdp")
    pooled_cols = pieces.reshape(pair_count, slice_width).astype(jnp.bfloat16)
    proj_grad = lax.dot_general(
        pooled_cols, grad_low_cols, contract_first, preferred_element_type=jnp.float32
    )
    return (mean_loss, query_grad, region_grad, hidden_grad, gain_grad, proj_grad)


SMALL_PAIRS = 1024


def local(query_cache, region_cache, positive, hidden_states, segment_ids, norm_gain, proj_weight):
    pair_count = query_cache.shape[0] * lax.axis_size("dp")
    args = (query_cache, region_cache, positive, hidden_states, segment_ids, norm_gain, proj_weight)
    if pair_count <= SMALL_PAIRS:
        return local_small(*args)
    return local_sharded(*args)


def solution(mesh):
    in_specs = (
        P("dp", "fsdp"),
        P("dp", "fsdp"),
        P("dp"),
        P(("dp", "fsdp"), None),
        P("dp", "fsdp"),
        P(),
        P("fsdp", None),
    )
    out_specs = (
        P(),
        P("dp", "fsdp"),
        P("dp", "fsdp"),
        P(("dp", "fsdp"), None),
        P(),
        P("dp", "fsdp"),
    )
    return jax.shard_map(local, mesh=mesh, in_specs=in_specs, out_specs=out_specs, check_vma=False)
```
